32 devices in a mesh: seq: 8 (over z, y), fsdp: 4 (over x, core).
Axes of the slice: x: 2, y: 2, z: 4, core: 2. Of those that a mesh axis runs over, the one named last changes fastest.
Arguments:
- tokens: bfloat16 [2048, 2048], P('seq', 'fsdp'), may hold values from -6 to 6
- deal_order: int32 [8, 8], replicated, may hold values from 0 to 7, each once within a row
- lengths: int32 [4], replicated, may hold values from 1 to 1024, 2048 in all
- x_weight: bfloat16 [2048, 1536], P(None, 'fsdp'), may hold values from -0.0390625 to 0.0390625
- z_weight: bfloat16 [2048, 1536], P(None, 'fsdp'), may hold values from -0.125 to 0.125
- shared_weight: bfloat16 [2048, 512], P('fsdp'), may hold values from -0.0390625 to 0.0390625
- step_weight: bfloat16 [2048, 24], P(None, 'fsdp'), may hold values from -0.125 to 0.125
- conv_heads: float32 [4, 1536], P(None, 'fsdp'), may hold values from -3 to 3
- conv_shared: float32 [4, 512], replicated, may hold values from -3 to 3
- step_bias: float32 [24], P('fsdp'), as said below
- decay_log: float32 [24], P('fsdp'), may hold values from -7.1 to -2.8, as said below
- skip_gain: float32 [24], P('fsdp'), may hold values from 0.5 to 1.5
Outputs:
- mixed: bfloat16 [2048, 1536], P('seq', 'fsdp')
The draws below stay inside these ranges and needn't reach their ends.
Inputs may be any that keep to these rules, and one draw needn't show every extreme that they name: `deal_order`: each row is a permutation of 0 to 7. The lengths sum to 2048. `decay_log`: one value a head. `step_bias`: one value a head.
All inputs are finite; a program needn't handle non-finite values.
Results may differ from the reference program's by a relative error of at most 0.0095.
Values may be sent and summed in bfloat16 or wider, within the bound.
No kernel may reach another device: no remote copies, remote signals or barrier semaphores. Data moves between devices by JAX's collectives and lax.ppermute only.
A program may use at most 128 MiB of HBM per device.

```python
import math
import jax
import jax.numpy as jnp
import numpy as np
from jax import lax

D = 2048
HEADS = 24
HEAD_DIM = 64
STATE = 256
CONV = 4
TOK_DEV = 256
PROMPTS = 4
TOKENS = 2048
LONGEST = 1024
PIECE = 32
INNER = 1536
N_SEQ = 8


def head_rates(key):
    source = jax.random.fold_in(key, 11)
    head_kind = jax.random.randint(jax.random.fold_in(source, 1), (HEADS,), 0, 10)
    slow_heads = head_kind < 5
    jitter = jax.random.uniform(jax.random.fold_in(source, 2), (HEADS,), jnp.float32, -0.5, 0.5)
    slow_factor = jnp.exp(jax.random.uniform(jax.random.fold_in(source, 3), (HEADS,), jnp.float32, math.log(0.3), math.log(0.8)))
    fast_reach = jnp.exp(jax.random.uniform(jax.random.fold_in(source, 4), (HEADS,), jnp.float32, math.log(30.0), math.log(50.0)))
    rate_token = jnp.where(slow_heads, slow_factor / LONGEST, 1.0 / fast_reach)
    base_step = jnp.where(slow_heads, 200.0 / LONGEST, 1.0)
    target = base_step * jnp.exp(jitter)
    decay_log = jnp.log(rate_token / target)
    step_bias = jnp.log(jnp.expm1(target))
    return (decay_log, step_bias)


def draw_decay_log(key, part):
    return head_rates(key)[0]


def draw_step_bias(key, part):
    return head_rates(key)[1]


def steps_of(rng, shape, split, smallest, top_value):
    def one(dim, shards_of):
        heights = jax.random.uniform(jax.random.fold_in(jax.random.fold_in(rng, 6), dim), (shards_of,), jnp.float32, smallest / len(split), top_value / len(split))
        return jnp.repeat(jnp.exp(heights), shape[dim] // shards_of).reshape((-1,) + (1,) * (len(shape) - dim - 1))

    loudness = one(*split[0])
    for cut in split[1:]:
        loudness = loudness * one(*cut)
    return loudness


def length_profile(amount, total, bound, skew):
    portions = [(1 << 20) // math.isqrt(standing ** skew) + 1 for standing in range(2, amount + 1)]
    spare, counts = total - bound - (amount - 1), [1] * (amount - 1)
    while spare > 0:
        movable = [i for i in range(amount - 1) if counts[i] < bound]
        pool, remaining = sum([portions[i] for i in movable]), spare
        for i in movable:
            addition = min(bound - counts[i], max(1, remaining * portions[i] // pool), spare)
            counts[i] = counts[i] + addition
            spare = spare - addition
    return np.array([bound] + counts)


def ragged(rng, count, total, reach, slope):
    if count == 2:
        one = jax.random.randint(rng, (), max(1, total - reach), min(reach, total - 1) + 1)
        return jnp.stack([one, total - one])
    sizes = jnp.asarray(length_profile(count, total, reach, slope), jnp.int32)
    pairs = (count - 1) // 2
    giver, taker = sizes[1:1 + 2 * pairs:2], sizes[2:2 + 2 * pairs:2]
    margin = jnp.minimum(giver - 1, reach - taker)
    shifted = jax.random.randint(jax.random.fold_in(rng, 1), (pairs,), 0, 1 << 20) % (margin + 1)
    sizes = sizes.at[1:1 + 2 * pairs:2].set(giver - shifted).at[2:2 + 2 * pairs:2].set(taker + shifted)
    return sizes[jax.random.permutation(jax.random.fold_in(rng, 2), count)]


def centred(key, extent, spread, most, shards=(), kind=jnp.bfloat16):
    drawn = jax.random.normal(key, extent, jnp.float32) * spread
    if len(shards) > 0:
        drawn = steps_of(key, extent, shards, -0.22, 0.18) * drawn
    return jnp.clip(drawn, min=-most, max=most).astype(kind)


def setup_inputs(seed: int = 0) -> dict:
    streams_of = jax.random.split(jax.random.key(seed), 13)
    tokens = centred(streams_of[0], (TOKENS, D), 1.0, 6.0, ((0, 8), (1, 4)))
    deal_order = jax.vmap(lambda own: jax.random.permutation(own, N_SEQ))(jax.random.split(streams_of[1], N_SEQ)).reshape((N_SEQ, N_SEQ)).astype(jnp.int32)
    lengths = ragged(streams_of[2], PROMPTS, TOKENS, LONGEST, 2).astype(jnp.int32)
    x_weight = centred(streams_of[3], (D, INNER), (11 * D) ** -0.5, 0.0390625, ((1, 4),))
    z_weight = centred(streams_of[4], (D, INNER), D ** -0.5, 0.125, ((1, 4),))
    shared_weight = centred(streams_of[5], (D, 2 * STATE), (11 * D) ** -0.5, 0.0390625, ((0, 4),))
    step_weight = centred(streams_of[6], (D, HEADS), D ** -0.5, 0.125, ((1, 4),))
    conv_heads = centred(streams_of[7], (CONV, INNER), CONV ** -0.5, 3.0, ((1, 4),), jnp.float32)
    conv_shared = centred(streams_of[8], (CONV, 2 * STATE), CONV ** -0.5, 3.0, (), jnp.float32)
    step_bias = draw_step_bias(jax.random.fold_in(streams_of[12], 71), 0)
    decay_log = draw_decay_log(jax.random.fold_in(streams_of[12], 71), 0)
    skip_gain = jnp.clip(0.5 + 1.0 * jax.random.uniform(streams_of[11], (HEADS,), jnp.float32) ** steps_of(streams_of[11], (HEADS,), ((0, 4),), -0.2, 0.2), 0.5, 1.5)
    return {"tokens": tokens, "deal_order": deal_order, "lengths": lengths, "x_weight": x_weight, "z_weight": z_weight, "shared_weight": shared_weight, "step_weight": step_weight, "conv_heads": conv_heads, "conv_shared": conv_shared, "step_bias": step_bias, "decay_log": decay_log, "skip_gain": skip_gain}


precise = lax.Precision.HIGHEST


def segment_of(positions, lengths):
    prompt_ends = jnp.cumsum(lengths).astype(jnp.int32)
    counted = (positions[:, None] >= prompt_ends[None, :]).astype(jnp.int32)
    return jnp.sum(counted, axis=1).astype(jnp.int32)


def causal_conv(extended, segment_ids, weights, conv_width):
    out_rows = extended.shape[0] - conv_width + 1
    target = segment_ids[conv_width - 1:]
    running = jnp.zeros((out_rows, extended.shape[1]), jnp.float32)
    for tap_index in range(conv_width):
        matched = (segment_ids[tap_index:tap_index + out_rows] == target).astype(jnp.float32)
        running = running + weights[tap_index][None, :] * extended[tap_index:tap_index + out_rows] * matched[:, None]
    return running


def local_terms(x_heads, b_rows, c_rows, step_size, decay_log, segment_ids, seg_before):
    log_decay = -jnp.exp(decay_log)[None, :] * step_size
    cum_decay = jnp.cumsum(log_decay, axis=0)
    positions_in = jnp.arange(x_heads.shape[0], dtype=jnp.int32)
    same_prompt = (segment_ids[:, None] == segment_ids[None, :]) & (positions_in[:, None] >= positions_in[None, :])
    decay_gap = cum_decay.T[:, :, None] - cum_decay.T[:, None, :]
    decay_matrix = jnp.exp(jnp.where(same_prompt[None], decay_gap, -jnp.inf))
    scores = jnp.dot(c_rows, b_rows.T, precision=precise)
    x_step = x_heads * step_size[:, :, None]
    intra = jnp.einsum('hts,shp->thp', scores[None] * decay_matrix, x_step, precision=precise)
    to_end = jnp.exp(jnp.where((segment_ids == segment_ids[-1])[:, None], cum_decay[-1][None, :] - cum_decay, -jnp.inf))
    state_out = jnp.einsum('shp,sn->hpn', x_step * to_end[:, :, None], b_rows, precision=precise)
    carried = segment_ids == seg_before
    carry_in = jnp.exp(jnp.where(carried[:, None], cum_decay, -jnp.inf))
    block_decay = jnp.where(carried[-1], jnp.exp(cum_decay[-1]), 0.0)
    return intra, state_out, carry_in, block_decay


def reference(tokens, deal_order, lengths, x_weight, z_weight, shared_weight, step_weight, conv_heads, conv_shared, step_bias, decay_log, skip_gain):
    pieces = tokens.reshape(N_SEQ, N_SEQ, PIECE, D).transpose(1, 0, 2, 3)
    inverse = jnp.argsort(deal_order, axis=1).astype(jnp.int32)
    stream = jnp.take_along_axis(pieces, inverse[:, :, None, None], axis=1).reshape(TOKENS, D)
    x_raw = jnp.dot(stream, x_weight, preferred_element_type=jnp.float32).astype(jnp.bfloat16)
    z_raw = jnp.dot(stream, z_weight, preferred_element_type=jnp.float32).astype(jnp.bfloat16)
    bc_raw = jnp.dot(stream, shared_weight, preferred_element_type=jnp.float32).astype(jnp.bfloat16)
    step_size = jax.nn.softplus(jnp.dot(stream, step_weight, preferred_element_type=jnp.float32) + step_bias[None, :])
    positions = jnp.arange(TOKENS, dtype=jnp.int32)
    segment_ids = segment_of(positions, lengths)
    mixed_in = jnp.concatenate([x_raw, bc_raw], axis=1).astype(jnp.float32)
    extended = jnp.concatenate([jnp.zeros((CONV - 1, mixed_in.shape[1]), jnp.float32), mixed_in], axis=0)
    seg_ext = jnp.concatenate([jnp.full((CONV - 1,), -1, jnp.int32), segment_ids])
    activated = jax.nn.silu(causal_conv(extended, seg_ext, jnp.concatenate([conv_heads, conv_shared], axis=1), CONV))
    x_all = activated[:, :INNER].reshape(N_SEQ, TOK_DEV, HEADS, HEAD_DIM)
    b_all = activated[:, INNER:INNER + STATE].reshape(N_SEQ, TOK_DEV, STATE)
    c_all = activated[:, INNER + STATE:].reshape(N_SEQ, TOK_DEV, STATE)
    step_all = step_size.reshape(N_SEQ, TOK_DEV, HEADS)
    seg_all = segment_ids.reshape(N_SEQ, TOK_DEV)
    seg_prior = jnp.concatenate([jnp.full((1,), -1, jnp.int32), seg_all[:-1, -1]])

    def advance(state_in, block_data):
        x_heads, b_rows, c_rows, step_block, seg_block, seg_before = block_data
        intra, state_out, carry_in, block_decay = local_terms(x_heads, b_rows, c_rows, step_block, decay_log, seg_block, seg_before)
        incoming = jnp.einsum('tn,hpn->thp', c_rows, state_in, precision=precise)
        y_block = intra + carry_in[:, :, None] * incoming + skip_gain[None, :, None] * x_heads
        return block_decay[:, None, None] * state_in + state_out, y_block

    state_zero = jnp.zeros((HEADS, HEAD_DIM, STATE), jnp.float32)
    _, y_all = lax.scan(advance, state_zero, (x_all, b_all, c_all, step_all, seg_all, seg_prior))
    gated = (y_all.reshape(TOKENS, INNER) * jax.nn.silu(z_raw.astype(jnp.float32))).astype(jnp.bfloat16)
    back_pieces = gated.reshape(N_SEQ, N_SEQ, PIECE, INNER)
    dealt_back = jnp.take_along_axis(back_pieces, deal_order[:, :, None, None], axis=1)
    return dealt_back.transpose(1, 0, 2, 3).reshape(TOKENS, INNER)
```

```python
import jax
import jax.numpy as jnp
from jax import lax
from jax.sharding import PartitionSpec as P

precise = lax.Precision.HIGHEST


def shifted(array, axis, by):
    count = lax.axis_size(axis)
    pairs = [(i, i + by) for i in range(count) if 0 <= i + by < count]
    return lax.ppermute(array, axis, pairs)


def combine_packed(earlier, later):
    rows = later.shape[1] - 1
    d_e, d_l = earlier[:, rows:, :], later[:, rows:, :]
    return jnp.concatenate([d_l * earlier[:, :rows, :] + later[:, :rows, :], d_e * d_l], axis=1)


def received(packed, axis, by):
    place = lax.axis_index(axis)
    got = shifted(packed, axis, by)
    rows = packed.shape[1] - 1
    missing = (place < by).astype(packed.dtype)
    return got.at[:, rows:, :].add(missing)


def exclusive_scan(packed, axis):
    count = lax.axis_size(axis)
    if count == 1:
        return received(packed, axis, 1)
    held = received(packed, axis, 1)
    if count > 2:
        held = combine_packed(received(packed, axis, 2), held)
    cover = 2
    while cover < count - 1:
        held = combine_packed(received(held, axis, cover), held)
        cover *= 2
    return held


def segment_of(positions, lengths):
    prompt_ends = jnp.cumsum(lengths)
    counted = (positions[:, None] >= prompt_ends[None, :]).astype(jnp.int32)
    return jnp.sum(counted, axis=1)


def causal_conv(extended, segment_ids, weights, conv_width):
    out_rows = extended.shape[0] - conv_width + 1
    target = segment_ids[conv_width - 1 :]
    running = jnp.zeros((out_rows, extended.shape[1]), jnp.float32)
    for tap_index in range(conv_width):
        matched = (segment_ids[tap_index : tap_index + out_rows] == target).astype(jnp.float32)
        running = (
            running
            + weights[tap_index][None, :]
            * extended[tap_index : tap_index + out_rows]
            * matched[:, None]
        )
    return running


def local_terms(x_heads, b_rows, c_rows, step_size, decay_log, segment_ids, seg_before):
    log_decay = -jnp.exp(decay_log)[None, :] * step_size
    cum_decay = jnp.cumsum(log_decay, axis=0)
    positions_in = jnp.arange(x_heads.shape[0], dtype=jnp.int32)
    same_prompt = (segment_ids[:, None] == segment_ids[None, :]) & (
        positions_in[:, None] >= positions_in[None, :]
    )
    decay_gap = cum_decay.T[:, :, None] - cum_decay.T[:, None, :]
    decay_matrix = jnp.exp(jnp.where(same_prompt[None], decay_gap, -jnp.inf))
    scores = jnp.dot(c_rows, b_rows.T, precision=precise)
    x_step = x_heads * step_size[:, :, None]
    intra = jnp.einsum("hts,shp->thp", scores[None] * decay_matrix, x_step, precision=precise)
    to_end = jnp.exp(
        jnp.where(
            (segment_ids == segment_ids[-1])[:, None], cum_decay[-1][None, :] - cum_decay, -jnp.inf
        )
    )
    state_out = jnp.einsum("shp,sn->hpn", x_step * to_end[:, :, None], b_rows, precision=precise)
    carried = segment_ids == seg_before
    carry_in = jnp.exp(jnp.where(carried[:, None], cum_decay, -jnp.inf))
    block_decay = jnp.where(carried[-1], jnp.exp(cum_decay[-1]), 0.0)
    return (intra, state_out, carry_in, block_decay)


def per_device(
    tokens,
    deal_order,
    lengths,
    x_weight,
    z_weight,
    shared_weight,
    step_weight,
    conv_heads,
    conv_shared,
    step_bias,
    decay_log,
    skip_gain,
):
    seq_count = lax.axis_size("seq")
    own_index = lax.axis_index("seq")
    tok_dev = tokens.shape[0]
    piece_rows = tok_dev // seq_count
    slot_rows = tokens.reshape(seq_count, piece_rows, tokens.shape[1])
    arrived = lax.all_to_all(slot_rows, "seq", split_axis=0, concat_axis=0, tiled=True)
    dealt_row = lax.dynamic_slice_in_dim(deal_order, own_index, 1, 0)[0]
    inverse = jnp.argsort(dealt_row)
    stream_block = jnp.take(arrived, inverse, axis=0).reshape(tok_dev, tokens.shape[1])
    inner_dev = x_weight.shape[1]
    heads_dev = step_weight.shape[1]
    head_dim = inner_dev // heads_dev
    state_dim = shared_weight.shape[1] // 2
    w_full = lax.all_gather(shared_weight, "fsdp", axis=0, tiled=True)
    weight_list = (x_weight, z_weight, step_weight, w_full)
    feature_part = lax.all_gather(stream_block, "fsdp", axis=1, tiled=True)
    x_acc, z_acc, step_acc, bc_acc = tuple(
        (
            jnp.dot(feature_part, weight, preferred_element_type=jnp.float32)
            for weight in weight_list
        )
    )
    x_raw = x_acc.astype(jnp.bfloat16)
    z_raw = z_acc.astype(jnp.bfloat16)
    bc_raw = bc_acc.astype(jnp.bfloat16)
    step_size = jax.nn.softplus(step_acc + step_bias[None, :])
    mixed_in = jnp.concatenate([x_raw, bc_raw], axis=1)
    conv_width = conv_heads.shape[0]
    prior_rows = shifted(mixed_in[tok_dev - conv_width + 1 :], "seq", 1)
    first_pos = own_index * tok_dev
    positions = first_pos - (conv_width - 1) + jnp.arange(tok_dev + conv_width - 1, dtype=jnp.int32)
    seg_ext = segment_of(positions, lengths)
    extended = jnp.concatenate([prior_rows, mixed_in], axis=0).astype(jnp.float32)
    activated = jax.nn.silu(
        causal_conv(
            extended, seg_ext, jnp.concatenate([conv_heads, conv_shared], axis=1), conv_width
        )
    )
    segment_ids = seg_ext[conv_width - 1 :]
    seg_before = jnp.where(own_index == 0, -1, seg_ext[conv_width - 2])
    x_heads = activated[:, :inner_dev].reshape(tok_dev, heads_dev, head_dim)
    b_rows = activated[:, inner_dev : inner_dev + state_dim]
    c_rows = activated[:, inner_dev + state_dim :]
    intra, state_out, carry_in, block_decay = local_terms(
        x_heads, b_rows, c_rows, step_size, decay_log, segment_ids, seg_before
    )
    packed = jnp.concatenate(
        [state_out, jnp.broadcast_to(block_decay[:, None, None], (heads_dev, 1, state_dim))], axis=1
    )
    state_in = exclusive_scan(packed, "seq")[:, :head_dim, :]
    incoming = jnp.einsum("tn,hpn->thp", c_rows, state_in, precision=precise)
    y_block = intra + carry_in[:, :, None] * incoming + skip_gain[None, :, None] * x_heads
    gated = (y_block.reshape(tok_dev, inner_dev) * jax.nn.silu(z_raw.astype(jnp.float32))).astype(
        jnp.bfloat16
    )
    ordered = gated.reshape(seq_count, piece_rows, inner_dev)
    outgoing = jnp.take(ordered, dealt_row, axis=0)
    returned = lax.all_to_all(outgoing, "seq", split_axis=0, concat_axis=0, tiled=True)
    return returned.reshape(tok_dev, inner_dev)


def solution(mesh):
    return jax.shard_map(
        per_device,
        mesh=mesh,
        in_specs=(
            P("seq", "fsdp"),
            P(),
            P(),
            P(None, "fsdp"),
            P(None, "fsdp"),
            P("fsdp", None),
            P(None, "fsdp"),
            P(None, "fsdp"),
            P(),
            P("fsdp"),
            P("fsdp"),
            P("fsdp"),
        ),
        out_specs=P("seq", "fsdp"),
        check_vma=False,
    )
```

```python
import jax
import jax.numpy as jnp
from jax import lax
from jax.sharding import PartitionSpec as P

precise = lax.Precision.HIGHEST


def shifted(array, axis, by):
    count = lax.axis_size(axis)
    pairs = [(i, i + by) for i in range(count) if 0 <= i + by < count]
    return lax.ppermute(array, axis, pairs)


def combine_packed(earlier, later):
    rows = later.shape[1] - 1
    d_e, d_l = earlier[:, rows:, :], later[:, rows:, :]
    return jnp.concatenate([d_l * earlier[:, :rows, :] + later[:, :rows, :], d_e * d_l], axis=1)


def received(packed, axis, by):
    place = lax.axis_index(axis)
    rows = packed.shape[1] - 1
    decay = packed[:, rows:, :]
    high = decay.astype(jnp.bfloat16)
    low = (decay - high.astype(jnp.float32)).astype(jnp.bfloat16)
    wire = jnp.concatenate([packed[:, :rows, :].astype(jnp.bfloat16), high, low], axis=1)
    got = shifted(wire, axis, by).astype(jnp.float32)
    missing = (place < by).astype(jnp.float32)
    decay_got = got[:, rows : rows + 1, :] + got[:, rows + 1 :, :] + missing
    return jnp.concatenate([got[:, :rows, :], decay_got], axis=1)


def exclusive_scan(packed, axis):
    count = lax.axis_size(axis)
    if count == 1:
        return received(packed, axis, 1)
    held = received(packed, axis, 1)
    if count > 2:
        held = combine_packed(received(packed, axis, 2), held)
    cover = 2
    while cover < count - 1:
        held = combine_packed(received(held, axis, cover), held)
        cover *= 2
    return held


def segment_of(positions, lengths):
    prompt_ends = jnp.cumsum(lengths)
    counted = (positions[:, None] >= prompt_ends[None, :]).astype(jnp.int32)
    return jnp.sum(counted, axis=1)


def causal_conv(extended, segment_ids, weights, conv_width):
    out_rows = extended.shape[0] - conv_width + 1
    target = segment_ids[conv_width - 1 :]
    running = jnp.zeros((out_rows, extended.shape[1]), jnp.float32)
    for tap_index in range(conv_width):
        matched = (segment_ids[tap_index : tap_index + out_rows] == target).astype(jnp.float32)
        running = (
            running
            + weights[tap_index][None, :]
            * extended[tap_index : tap_index + out_rows]
            * matched[:, None]
        )
    return running


def local_terms(x_heads, b_rows, c_rows, step_size, decay_log, segment_ids, seg_before):
    log_decay = -jnp.exp(decay_log)[None, :] * step_size
    cum_decay = jnp.cumsum(log_decay, axis=0)
    positions_in = jnp.arange(x_heads.shape[0], dtype=jnp.int32)
    same_prompt = (segment_ids[:, None] == segment_ids[None, :]) & (
        positions_in[:, None] >= positions_in[None, :]
    )
    decay_gap = cum_decay.T[:, :, None] - cum_decay.T[:, None, :]
    decay_matrix = jnp.exp(jnp.where(same_prompt[None], decay_gap, -jnp.inf))
    scores = jnp.dot(c_rows, b_rows.T, precision=precise)
    x_step = x_heads * step_size[:, :, None]
    intra = jnp.einsum("hts,shp->thp", scores[None] * decay_matrix, x_step, precision=precise)
    to_end = jnp.exp(
        jnp.where(
            (segment_ids == segment_ids[-1])[:, None], cum_decay[-1][None, :] - cum_decay, -jnp.inf
        )
    )
    state_out = jnp.einsum("shp,sn->hpn", x_step * to_end[:, :, None], b_rows, precision=precise)
    carried = segment_ids == seg_before
    carry_in = jnp.exp(jnp.where(carried[:, None], cum_decay, -jnp.inf))
    block_decay = jnp.where(carried[-1], jnp.exp(cum_decay[-1]), 0.0)
    return (intra, state_out, carry_in, block_decay)


def per_device(
    tokens,
    deal_order,
    lengths,
    x_weight,
    z_weight,
    shared_weight,
    step_weight,
    conv_heads,
    conv_shared,
    step_bias,
    decay_log,
    skip_gain,
):
    seq_count = lax.axis_size("seq")
    own_index = lax.axis_index("seq")
    tok_dev = tokens.shape[0]
    piece_rows = tok_dev // seq_count
    slot_rows = tokens.reshape(seq_count, piece_rows, tokens.shape[1])
    arrived = lax.all_to_all(slot_rows, "seq", split_axis=0, concat_axis=0, tiled=True)
    dealt_row = lax.dynamic_slice_in_dim(deal_order, own_index, 1, 0)[0]
    inverse = jnp.argsort(dealt_row)
    stream_block = jnp.take(arrived, inverse, axis=0).reshape(tok_dev, tokens.shape[1])
    inner_dev = x_weight.shape[1]
    heads_dev = step_weight.shape[1]
    head_dim = inner_dev // heads_dev
    state_dim = shared_weight.shape[1] // 2
    w_full = lax.all_gather(shared_weight, "fsdp", axis=0, tiled=True)
    weight_list = (x_weight, z_weight, step_weight, w_full)
    feature_part = lax.all_gather(stream_block, "fsdp", axis=1, tiled=True)
    x_acc, z_acc, step_acc, bc_acc = tuple(
        (
            jnp.dot(feature_part, weight, preferred_element_type=jnp.float32)
            for weight in weight_list
        )
    )
    x_raw = x_acc.astype(jnp.bfloat16)
    z_raw = z_acc.astype(jnp.bfloat16)
    bc_raw = bc_acc.astype(jnp.bfloat16)
    step_size = jax.nn.softplus(step_acc + step_bias[None, :])
    mixed_in = jnp.concatenate([x_raw, bc_raw], axis=1)
    conv_width = conv_heads.shape[0]
    prior_rows = shifted(mixed_in[tok_dev - conv_width + 1 :], "seq", 1)
    first_pos = own_index * tok_dev
    positions = first_pos - (conv_width - 1) + jnp.arange(tok_dev + conv_width - 1, dtype=jnp.int32)
    seg_ext = segment_of(positions, lengths)
    extended = jnp.concatenate([prior_rows, mixed_in], axis=0).astype(jnp.float32)
    activated = jax.nn.silu(
        causal_conv(
            extended, seg_ext, jnp.concatenate([conv_heads, conv_shared], axis=1), conv_width
        )
    )
    segment_ids = seg_ext[conv_width - 1 :]
    seg_before = jnp.where(own_index == 0, -1, seg_ext[conv_width - 2])
    x_heads = activated[:, :inner_dev].reshape(tok_dev, heads_dev, head_dim)
    b_rows = activated[:, inner_dev : inner_dev + state_dim]
    c_rows = activated[:, inner_dev + state_dim :]
    intra, state_out, carry_in, block_decay = local_terms(
        x_heads, b_rows, c_rows, step_size, decay_log, segment_ids, seg_before
    )
    packed = jnp.concatenate(
        [state_out, jnp.broadcast_to(block_decay[:, None, None], (heads_dev, 1, state_dim))], axis=1
    )
    state_in = exclusive_scan(packed, "seq")[:, :head_dim, :]
    incoming = jnp.einsum("tn,hpn->thp", c_rows, state_in, precision=precise)
    y_block = intra + carry_in[:, :, None] * incoming + skip_gain[None, :, None] * x_heads
    gated = (y_block.reshape(tok_dev, inner_dev) * jax.nn.silu(z_raw.astype(jnp.float32))).astype(
        jnp.bfloat16
    )
    ordered = gated.reshape(seq_count, piece_rows, inner_dev)
    outgoing = jnp.take(ordered, dealt_row, axis=0)
    returned = lax.all_to_all(outgoing, "seq", split_axis=0, concat_axis=0, tiled=True)
    return returned.reshape(tok_dev, inner_dev)


def solution(mesh):
    return jax.shard_map(
        per_device,
        mesh=mesh,
        in_specs=(
            P("seq", "fsdp"),
            P(),
            P(),
            P(None, "fsdp"),
            P(None, "fsdp"),
            P("fsdp", None),
            P(None, "fsdp"),
            P(None, "fsdp"),
            P(),
            P("fsdp"),
            P("fsdp"),
            P("fsdp"),
        ),
        out_specs=P("seq", "fsdp"),
        check_vma=False,
    )
```

```python
import jax
import jax.numpy as jnp
from jax import lax
from jax.sharding import PartitionSpec as P

precise = lax.Precision.HIGHEST


def shifted(array, axis, by):
    count = lax.axis_size(axis)
    pairs = [(i, i + by) for i in range(count) if 0 <= i + by < count]
    return lax.ppermute(array, axis, pairs)


def combine_packed(earlier, later):
    rows = later.shape[1] - 1
    d_e, d_l = earlier[:, rows:, :], later[:, rows:, :]
    return jnp.concatenate([d_l * earlier[:, :rows, :] + later[:, :rows, :], d_e * d_l], axis=1)


def received(packed, axis, by):
    place = lax.axis_index(axis)
    rows = packed.shape[1] - 1
    decay = packed[:, rows:, :]
    high = decay.astype(jnp.bfloat16)
    low = (decay - high.astype(jnp.float32)).astype(jnp.bfloat16)
    wire = jnp.concatenate([packed[:, :rows, :].astype(jnp.bfloat16), high, low], axis=1)
    got = shifted(wire, axis, by).astype(jnp.float32)
    missing = (place < by).astype(jnp.float32)
    decay_got = got[:, rows : rows + 1, :] + got[:, rows + 1 :, :] + missing
    return jnp.concatenate([got[:, :rows, :], decay_got], axis=1)


def exclusive_scan(packed, axis):
    count = lax.axis_size(axis)
    if count == 1:
        return received(packed, axis, 1)
    held = received(packed, axis, 1)
    if count > 2:
        held = combine_packed(received(packed, axis, 2), held)
    cover = 2
    while cover < count - 1:
        held = combine_packed(received(held, axis, cover), held)
        cover *= 2
    return held


def segment_of(positions, lengths):
    prompt_ends = jnp.cumsum(lengths)
    counted = (positions[:, None] >= prompt_ends[None, :]).astype(jnp.int32)
    return jnp.sum(counted, axis=1)


def causal_conv(extended, segment_ids, weights, conv_width):
    out_rows = extended.shape[0] - conv_width + 1
    target = segment_ids[conv_width - 1 :]
    running = jnp.zeros((out_rows, extended.shape[1]), jnp.float32)
    for tap_index in range(conv_width):
        matched = (segment_ids[tap_index : tap_index + out_rows] == target).astype(jnp.float32)
        running = (
            running
            + weights[tap_index][None, :]
            * extended[tap_index : tap_index + out_rows]
            * matched[:, None]
        )
    return running


def local_terms(x_heads, b_rows, c_rows, step_size, decay_log, segment_ids, seg_before):
    log_decay = -jnp.exp(decay_log)[None, :] * step_size
    cum_decay = jnp.cumsum(log_decay, axis=0)
    positions_in = jnp.arange(x_heads.shape[0], dtype=jnp.int32)
    same_prompt = (segment_ids[:, None] == segment_ids[None, :]) & (
        positions_in[:, None] >= positions_in[None, :]
    )
    decay_gap = cum_decay.T[:, :, None] - cum_decay.T[:, None, :]
    decay_matrix = jnp.exp(jnp.where(same_prompt[None], decay_gap, -jnp.inf))
    scores = jnp.dot(c_rows, b_rows.T, precision=precise)
    x_step = x_heads * step_size[:, :, None]
    intra = jnp.einsum("hts,shp->thp", scores[None] * decay_matrix, x_step, precision=precise)
    to_end = jnp.exp(
        jnp.where(
            (segment_ids == segment_ids[-1])[:, None], cum_decay[-1][None, :] - cum_decay, -jnp.inf
        )
    )
    state_out = jnp.einsum("shp,sn->hpn", x_step * to_end[:, :, None], b_rows, precision=precise)
    carried = segment_ids == seg_before
    carry_in = jnp.exp(jnp.where(carried[:, None], cum_decay, -jnp.inf))
    block_decay = jnp.where(carried[-1], jnp.exp(cum_decay[-1]), 0.0)
    return (intra, state_out, carry_in, block_decay)


def per_device(
    tokens,
    deal_order,
    lengths,
    x_weight,
    z_weight,
    shared_weight,
    step_weight,
    conv_heads,
    conv_shared,
    step_bias,
    decay_log,
    skip_gain,
):
    seq_count = lax.axis_size("seq")
    own_index = lax.axis_index("seq")
    tok_dev = tokens.shape[0]
    piece_rows = tok_dev // seq_count
    slot_rows = tokens.reshape(seq_count, piece_rows, tokens.shape[1])
    arrived = lax.all_to_all(slot_rows, "seq", split_axis=0, concat_axis=0, tiled=True)
    dealt_row = lax.dynamic_slice_in_dim(deal_order, own_index, 1, 0)[0]
    inverse = jnp.argsort(dealt_row)
    stream_block = jnp.take(arrived, inverse, axis=0).reshape(tok_dev, tokens.shape[1])
    inner_dev = x_weight.shape[1]
    heads_dev = step_weight.shape[1]
    head_dim = inner_dev // heads_dev
    state_dim = shared_weight.shape[1] // 2
    w_full = lax.all_gather(shared_weight, "fsdp", axis=0, tiled=True)
    w_full, stream_block = lax.optimization_barrier((w_full, stream_block))
    weight_list = (x_weight, z_weight, step_weight, w_full)
    feature_part = lax.all_gather(stream_block, "fsdp", axis=1, tiled=True)
    x_acc, z_acc, step_acc, bc_acc = tuple(
        (
            jnp.dot(feature_part, weight, preferred_element_type=jnp.float32)
            for weight in weight_list
        )
    )
    x_raw = x_acc.astype(jnp.bfloat16)
    z_raw = z_acc.astype(jnp.bfloat16)
    bc_raw = bc_acc.astype(jnp.bfloat16)
    step_size = jax.nn.softplus(step_acc + step_bias[None, :])
    mixed_in = jnp.concatenate([x_raw, bc_raw], axis=1)
    conv_width = conv_heads.shape[0]
    prior_rows = shifted(mixed_in[tok_dev - conv_width + 1 :], "seq", 1)
    first_pos = own_index * tok_dev
    positions = first_pos - (conv_width - 1) + jnp.arange(tok_dev + conv_width - 1, dtype=jnp.int32)
    seg_ext = segment_of(positions, lengths)
    extended = jnp.concatenate([prior_rows, mixed_in], axis=0).astype(jnp.float32)
    activated = jax.nn.silu(
        causal_conv(
            extended, seg_ext, jnp.concatenate([conv_heads, conv_shared], axis=1), conv_width
        )
    )
    segment_ids = seg_ext[conv_width - 1 :]
    seg_before = jnp.where(own_index == 0, -1, seg_ext[conv_width - 2])
    x_heads = activated[:, :inner_dev].reshape(tok_dev, heads_dev, head_dim)
    b_rows = activated[:, inner_dev : inner_dev + state_dim]
    c_rows = activated[:, inner_dev + state_dim :]
    intra, state_out, carry_in, block_decay = local_terms(
        x_heads, b_rows, c_rows, step_size, decay_log, segment_ids, seg_before
    )
    packed = jnp.concatenate(
        [state_out, jnp.broadcast_to(block_decay[:, None, None], (heads_dev, 1, state_dim))], axis=1
    )
    state_in = exclusive_scan(packed, "seq")[:, :head_dim, :]
    incoming = jnp.einsum("tn,hpn->thp", c_rows, state_in, precision=precise)
    y_block = intra + carry_in[:, :, None] * incoming + skip_gain[None, :, None] * x_heads
    gated = (y_block.reshape(tok_dev, inner_dev) * jax.nn.silu(z_raw.astype(jnp.float32))).astype(
        jnp.bfloat16
    )
    ordered = gated.reshape(seq_count, piece_rows, inner_dev)
    outgoing = jnp.take(ordered, dealt_row, axis=0)
    returned = lax.all_to_all(outgoing, "seq", split_axis=0, concat_axis=0, tiled=True)
    return returned.reshape(tok_dev, inner_dev)


def solution(mesh):
    return jax.shard_map(
        per_device,
        mesh=mesh,
        in_specs=(
            P("seq", "fsdp"),
            P(),
            P(),
            P(None, "fsdp"),
            P(None, "fsdp"),
            P("fsdp", None),
            P(None, "fsdp"),
            P(None, "fsdp"),
            P(),
            P("fsdp"),
            P("fsdp"),
            P("fsdp"),
        ),
        out_specs=P("seq", "fsdp"),
        check_vma=False,
    )
```

```python
import jax
import jax.numpy as jnp
from jax import lax
from jax.sharding import PartitionSpec as P

precise = lax.Precision.HIGHEST


def shifted(array, axis, by):
    count = lax.axis_size(axis)
    pairs = [(i, i + by) for i in range(count) if 0 <= i + by < count]
    return lax.ppermute(array, axis, pairs)


def combine_packed(earlier, later):
    rows = later.shape[1] - 1
    d_e, d_l = earlier[:, rows:, :], later[:, rows:, :]
    return jnp.concatenate([d_l * earlier[:, :rows, :] + later[:, :rows, :], d_e * d_l], axis=1)


def received(packed, axis, by):
    place = lax.axis_index(axis)
    rows = packed.shape[1] - 1
    decay = packed[:, rows:, :]
    high = decay.astype(jnp.bfloat16)
    low = (decay - high.astype(jnp.float32)).astype(jnp.bfloat16)
    wire = jnp.concatenate([packed[:, :rows, :].astype(jnp.bfloat16), high, low], axis=1)
    got = shifted(wire, axis, by).astype(jnp.float32)
    missing = (place < by).astype(jnp.float32)
    decay_got = got[:, rows : rows + 1, :] + got[:, rows + 1 :, :] + missing
    return jnp.concatenate([got[:, :rows, :], decay_got], axis=1)


def exclusive_scan(packed, axis):
    count = lax.axis_size(axis)
    if count == 1:
        return received(packed, axis, 1)
    held = received(packed, axis, 1)
    if count > 2:
        held = combine_packed(received(packed, axis, 2), held)
    cover = 2
    while cover < count - 1:
        held = combine_packed(received(held, axis, cover), held)
        cover *= 2
    return held


def gather_columns(block, axis):
    count = lax.axis_size(axis)
    if count & (count - 1):
        return lax.all_gather(block, axis, axis=1, tiled=True)
    place = lax.axis_index(axis)
    held, codes = block[None], [0]
    bit = count // 2
    while bit >= 1:
        other = lax.ppermute(held, axis, [(i, i ^ bit) for i in range(count)])
        held = jnp.concatenate([held, other], axis=0)
        codes = codes + [c ^ bit for c in codes]
        bit //= 2
    where_code = [0] * count
    for position, code in enumerate(codes):
        where_code[code] = position
    order = jnp.asarray(where_code, jnp.int32)[jnp.bitwise_xor(jnp.arange(count, dtype=jnp.int32), place)]
    ordered = jnp.take(held, order, axis=0)
    return ordered.transpose(1, 0, 2).reshape(block.shape[0], count * block.shape[1])


def segment_of(positions, lengths):
    prompt_ends = jnp.cumsum(lengths)
    counted = (positions[:, None] >= prompt_ends[None, :]).astype(jnp.int32)
    return jnp.sum(counted, axis=1)


def causal_conv(extended, segment_ids, weights, conv_width):
    out_rows = extended.shape[0] - conv_width + 1
    target = segment_ids[conv_width - 1 :]
    running = jnp.zeros((out_rows, extended.shape[1]), jnp.float32)
    for tap_index in range(conv_width):
        matched = (segment_ids[tap_index : tap_index + out_rows] == target).astype(jnp.float32)
        running = (
            running
            + weights[tap_index][None, :]
            * extended[tap_index : tap_index + out_rows]
            * matched[:, None]
        )
    return running


def local_terms(x_heads, b_rows, c_rows, step_size, decay_log, segment_ids, seg_before):
    log_decay = -jnp.exp(decay_log)[None, :] * step_size
    cum_decay = jnp.cumsum(log_decay, axis=0)
    positions_in = jnp.arange(x_heads.shape[0], dtype=jnp.int32)
    same_prompt = (segment_ids[:, None] == segment_ids[None, :]) & (
        positions_in[:, None] >= positions_in[None, :]
    )
    decay_gap = cum_decay.T[:, :, None] - cum_decay.T[:, None, :]
    decay_matrix = jnp.exp(jnp.where(same_prompt[None], decay_gap, -jnp.inf))
    scores = jnp.dot(c_rows, b_rows.T, precision=precise)
    x_step = x_heads * step_size[:, :, None]
    intra = jnp.einsum("hts,shp->thp", scores[None] * decay_matrix, x_step, precision=precise)
    to_end = jnp.exp(
        jnp.where(
            (segment_ids == segment_ids[-1])[:, None], cum_decay[-1][None, :] - cum_decay, -jnp.inf
        )
    )
    state_out = jnp.einsum("shp,sn->hpn", x_step * to_end[:, :, None], b_rows, precision=precise)
    carried = segment_ids == seg_before
    carry_in = jnp.exp(jnp.where(carried[:, None], cum_decay, -jnp.inf))
    block_decay = jnp.where(carried[-1], jnp.exp(cum_decay[-1]), 0.0)
    return (intra, state_out, carry_in, block_decay)


def per_device(
    tokens,
    deal_order,
    lengths,
    x_weight,
    z_weight,
    shared_weight,
    step_weight,
    conv_heads,
    conv_shared,
    step_bias,
    decay_log,
    skip_gain,
):
    seq_count = lax.axis_size("seq")
    own_index = lax.axis_index("seq")
    tok_dev = tokens.shape[0]
    piece_rows = tok_dev // seq_count
    slot_rows = tokens.reshape(seq_count, piece_rows, tokens.shape[1])
    arrived = lax.all_to_all(slot_rows, "seq", split_axis=0, concat_axis=0, tiled=True)
    dealt_row = lax.dynamic_slice_in_dim(deal_order, own_index, 1, 0)[0]
    inverse = jnp.argsort(dealt_row)
    stream_block = jnp.take(arrived, inverse, axis=0).reshape(tok_dev, tokens.shape[1])
    inner_dev = x_weight.shape[1]
    heads_dev = step_weight.shape[1]
    head_dim = inner_dev // heads_dev
    state_dim = shared_weight.shape[1] // 2
    w_full = lax.all_gather(shared_weight, "fsdp", axis=0, tiled=True)
    weight_list = (x_weight, z_weight, step_weight, w_full)
    feature_part = gather_columns(stream_block, "fsdp")
    x_acc, z_acc, step_acc, bc_acc = tuple(
        (
            jnp.dot(feature_part, weight, preferred_element_type=jnp.float32)
            for weight in weight_list
        )
    )
    x_raw = x_acc.astype(jnp.bfloat16)
    z_raw = z_acc.astype(jnp.bfloat16)
    bc_raw = bc_acc.astype(jnp.bfloat16)
    step_size = jax.nn.softplus(step_acc + step_bias[None, :])
    mixed_in = jnp.concatenate([x_raw, bc_raw], axis=1)
    conv_width = conv_heads.shape[0]
    prior_rows = shifted(mixed_in[tok_dev - conv_width + 1 :], "seq", 1)
    first_pos = own_index * tok_dev
    positions = first_pos - (conv_width - 1) + jnp.arange(tok_dev + conv_width - 1, dtype=jnp.int32)
    seg_ext = segment_of(positions, lengths)
    extended = jnp.concatenate([prior_rows, mixed_in], axis=0).astype(jnp.float32)
    activated = jax.nn.silu(
        causal_conv(
            extended, seg_ext, jnp.concatenate([conv_heads, conv_shared], axis=1), conv_width
        )
    )
    segment_ids = seg_ext[conv_width - 1 :]
    seg_before = jnp.where(own_index == 0, -1, seg_ext[conv_width - 2])
    x_heads = activated[:, :inner_dev].reshape(tok_dev, heads_dev, head_dim)
    b_rows = activated[:, inner_dev : inner_dev + state_dim]
    c_rows = activated[:, inner_dev + state_dim :]
    intra, state_out, carry_in, block_decay = local_terms(
        x_heads, b_rows, c_rows, step_size, decay_log, segment_ids, seg_before
    )
    packed = jnp.concatenate(
        [state_out, jnp.broadcast_to(block_decay[:, None, None], (heads_dev, 1, state_dim))], axis=1
    )
    state_in = exclusive_scan(packed, "seq")[:, :head_dim, :]
    incoming = jnp.einsum("tn,hpn->thp", c_rows, state_in, precision=precise)
    y_block = intra + carry_in[:, :, None] * incoming + skip_gain[None, :, None] * x_heads
    gated = (y_block.reshape(tok_dev, inner_dev) * jax.nn.silu(z_raw.astype(jnp.float32))).astype(
        jnp.bfloat16
    )
    ordered = gated.reshape(seq_count, piece_rows, inner_dev)
    outgoing = jnp.take(ordered, dealt_row, axis=0)
    returned = lax.all_to_all(outgoing, "seq", split_axis=0, concat_axis=0, tiled=True)
    return returned.reshape(tok_dev, inner_dev)


def solution(mesh):
    return jax.shard_map(
        per_device,
        mesh=mesh,
        in_specs=(
            P("seq", "fsdp"),
            P(),
            P(),
            P(None, "fsdp"),
            P(None, "fsdp"),
            P("fsdp", None),
            P(None, "fsdp"),
            P(None, "fsdp"),
            P(),
            P("fsdp"),
            P("fsdp"),
            P("fsdp"),
        ),
        out_specs=P("seq", "fsdp"),
        check_vma=False,
    )
```

```python
import jax
import jax.numpy as jnp
from jax import lax
from jax.sharding import PartitionSpec as P

precise = lax.Precision.HIGHEST


def shifted(array, axis, by):
    count = lax.axis_size(axis)
    pairs = [(i, i + by) for i in range(count) if 0 <= i + by < count]
    return lax.ppermute(array, axis, pairs)


def combine_packed(earlier, later):
    rows = later.shape[1] - 1
    d_e, d_l = earlier[:, rows:, :], later[:, rows:, :]
    return jnp.concatenate([d_l * earlier[:, :rows, :] + later[:, :rows, :], d_e * d_l], axis=1)


def received(packed, axis, by):
    place = lax.axis_index(axis)
    rows = packed.shape[1] - 1
    decay = packed[:, rows:, :]
    high = decay.astype(jnp.bfloat16)
    low = (decay - high.astype(jnp.float32)).astype(jnp.bfloat16)
    wire = jnp.concatenate([packed[:, :rows, :].astype(jnp.bfloat16), high, low], axis=1)
    got = shifted(wire, axis, by).astype(jnp.float32)
    missing = (place < by).astype(jnp.float32)
    decay_got = got[:, rows : rows + 1, :] + got[:, rows + 1 :, :] + missing
    return jnp.concatenate([got[:, :rows, :], decay_got], axis=1)


def exclusive_scan(packed, axis):
    count = lax.axis_size(axis)
    if count == 1:
        return received(packed, axis, 1)
    held = received(packed, axis, 1)
    if count > 2:
        held = combine_packed(received(packed, axis, 2), held)
    cover = 2
    while cover < count - 1:
        held = combine_packed(received(held, axis, cover), held)
        cover *= 2
    return held


def gather_blocks(block, axis):
    count = lax.axis_size(axis)
    if count & (count - 1):
        return lax.all_gather(block, axis, axis=0, tiled=False)
    place = lax.axis_index(axis)
    held, codes = block[None], [0]
    bit = count // 2
    while bit >= 1:
        other = lax.ppermute(held, axis, [(i, i ^ bit) for i in range(count)])
        held = jnp.concatenate([held, other], axis=0)
        codes = codes + [c ^ bit for c in codes]
        bit //= 2
    where_code = [0] * count
    for position, code in enumerate(codes):
        where_code[code] = position
    order = jnp.asarray(where_code, jnp.int32)[jnp.bitwise_xor(jnp.arange(count, dtype=jnp.int32), place)]
    return jnp.take(held, order, axis=0)


def gather_columns(block, axis):
    stacked = gather_blocks(block, axis)
    return stacked.transpose(1, 0, 2).reshape(block.shape[0], stacked.shape[0] * block.shape[1])


def segment_of(positions, lengths):
    prompt_ends = jnp.cumsum(lengths)
    counted = (positions[:, None] >= prompt_ends[None, :]).astype(jnp.int32)
    return jnp.sum(counted, axis=1)


def causal_conv(extended, segment_ids, weights, conv_width):
    out_rows = extended.shape[0] - conv_width + 1
    target = segment_ids[conv_width - 1 :]
    running = jnp.zeros((out_rows, extended.shape[1]), jnp.float32)
    for tap_index in range(conv_width):
        matched = (segment_ids[tap_index : tap_index + out_rows] == target).astype(jnp.float32)
        running = (
            running
            + weights[tap_index][None, :]
            * extended[tap_index : tap_index + out_rows]
            * matched[:, None]
        )
    return running


def local_terms(x_heads, b_rows, c_rows, step_size, decay_log, segment_ids, seg_before):
    log_decay = -jnp.exp(decay_log)[None, :] * step_size
    cum_decay = jnp.cumsum(log_decay, axis=0)
    positions_in = jnp.arange(x_heads.shape[0], dtype=jnp.int32)
    same_prompt = (segment_ids[:, None] == segment_ids[None, :]) & (
        positions_in[:, None] >= positions_in[None, :]
    )
    decay_gap = cum_decay.T[:, :, None] - cum_decay.T[:, None, :]
    decay_matrix = jnp.exp(jnp.where(same_prompt[None], decay_gap, -jnp.inf))
    scores = jnp.dot(c_rows, b_rows.T, precision=precise)
    x_step = x_heads * step_size[:, :, None]
    intra = jnp.einsum("hts,shp->thp", scores[None] * decay_matrix, x_step, precision=precise)
    to_end = jnp.exp(
        jnp.where(
            (segment_ids == segment_ids[-1])[:, None], cum_decay[-1][None, :] - cum_decay, -jnp.inf
        )
    )
    state_out = jnp.einsum("shp,sn->hpn", x_step * to_end[:, :, None], b_rows, precision=precise)
    carried = segment_ids == seg_before
    carry_in = jnp.exp(jnp.where(carried[:, None], cum_decay, -jnp.inf))
    block_decay = jnp.where(carried[-1], jnp.exp(cum_decay[-1]), 0.0)
    return (intra, state_out, carry_in, block_decay)


def per_device(
    tokens,
    deal_order,
    lengths,
    x_weight,
    z_weight,
    shared_weight,
    step_weight,
    conv_heads,
    conv_shared,
    step_bias,
    decay_log,
    skip_gain,
):
    seq_count = lax.axis_size("seq")
    own_index = lax.axis_index("seq")
    tok_dev = tokens.shape[0]
    piece_rows = tok_dev // seq_count
    slot_rows = tokens.reshape(seq_count, piece_rows, tokens.shape[1])
    arrived = lax.all_to_all(slot_rows, "seq", split_axis=0, concat_axis=0, tiled=True)
    dealt_row = lax.dynamic_slice_in_dim(deal_order, own_index, 1, 0)[0]
    inverse = jnp.argsort(dealt_row)
    stream_block = jnp.take(arrived, inverse, axis=0).reshape(tok_dev, tokens.shape[1])
    inner_dev = x_weight.shape[1]
    heads_dev = step_weight.shape[1]
    head_dim = inner_dev // heads_dev
    state_dim = shared_weight.shape[1] // 2
    w_full = gather_blocks(shared_weight, "fsdp").reshape(-1, shared_weight.shape[1])
    weight_list = (x_weight, z_weight, step_weight, w_full)
    feature_part = gather_columns(stream_block, "fsdp")
    x_acc, z_acc, step_acc, bc_acc = tuple(
        (
            jnp.dot(feature_part, weight, preferred_element_type=jnp.float32)
            for weight in weight_list
        )
    )
    x_raw = x_acc.astype(jnp.bfloat16)
    z_raw = z_acc.astype(jnp.bfloat16)
    bc_raw = bc_acc.astype(jnp.bfloat16)
    step_size = jax.nn.softplus(step_acc + step_bias[None, :])
    mixed_in = jnp.concatenate([x_raw, bc_raw], axis=1)
    conv_width = conv_heads.shape[0]
    prior_rows = shifted(mixed_in[tok_dev - conv_width + 1 :], "seq", 1)
    first_pos = own_index * tok_dev
    positions = first_pos - (conv_width - 1) + jnp.arange(tok_dev + conv_width - 1, dtype=jnp.int32)
    seg_ext = segment_of(positions, lengths)
    extended = jnp.concatenate([prior_rows, mixed_in], axis=0).astype(jnp.float32)
    activated = jax.nn.silu(
        causal_conv(
            extended, seg_ext, jnp.concatenate([conv_heads, conv_shared], axis=1), conv_width
        )
    )
    segment_ids = seg_ext[conv_width - 1 :]
    seg_before = jnp.where(own_index == 0, -1, seg_ext[conv_width - 2])
    x_heads = activated[:, :inner_dev].reshape(tok_dev, heads_dev, head_dim)
    b_rows = activated[:, inner_dev : inner_dev + state_dim]
    c_rows = activated[:, inner_dev + state_dim :]
    intra, state_out, carry_in, block_decay = local_terms(
        x_heads, b_rows, c_rows, step_size, decay_log, segment_ids, seg_before
    )
    packed = jnp.concatenate(
        [state_out, jnp.broadcast_to(block_decay[:, None, None], (heads_dev, 1, state_dim))], axis=1
    )
    state_in = exclusive_scan(packed, "seq")[:, :head_dim, :]
    incoming = jnp.einsum("tn,hpn->thp", c_rows, state_in, precision=precise)
    y_block = intra + carry_in[:, :, None] * incoming + skip_gain[None, :, None] * x_heads
    gated = (y_block.reshape(tok_dev, inner_dev) * jax.nn.silu(z_raw.astype(jnp.float32))).astype(
        jnp.bfloat16
    )
    ordered = gated.reshape(seq_count, piece_rows, inner_dev)
    outgoing = jnp.take(ordered, dealt_row, axis=0)
    returned = lax.all_to_all(outgoing, "seq", split_axis=0, concat_axis=0, tiled=True)
    return returned.reshape(tok_dev, inner_dev)


def solution(mesh):
    return jax.shard_map(
        per_device,
        mesh=mesh,
        in_specs=(
            P("seq", "fsdp"),
            P(),
            P(),
            P(None, "fsdp"),
            P(None, "fsdp"),
            P("fsdp", None),
            P(None, "fsdp"),
            P(None, "fsdp"),
            P(),
            P("fsdp"),
            P("fsdp"),
            P("fsdp"),
        ),
        out_specs=P("seq", "fsdp"),
        check_vma=False,
    )
```

```python
import jax
import jax.numpy as jnp
from jax import lax
from jax.sharding import PartitionSpec as P

precise = lax.Precision.HIGHEST


def shifted(array, axis, by):
    count = lax.axis_size(axis)
    pairs = [(i, i + by) for i in range(count) if 0 <= i + by < count]
    return lax.ppermute(array, axis, pairs)


def combine_packed(earlier, later):
    rows = later.shape[1] - 1
    d_e, d_l = earlier[:, rows:, :], later[:, rows:, :]
    return jnp.concatenate([d_l * earlier[:, :rows, :] + later[:, :rows, :], d_e * d_l], axis=1)


def received(packed, axis, by):
    place = lax.axis_index(axis)
    rows = packed.shape[1] - 1
    decay = packed[:, rows:, :]
    high = decay.astype(jnp.bfloat16)
    low = (decay - high.astype(jnp.float32)).astype(jnp.bfloat16)
    wire = jnp.concatenate([packed[:, :rows, :].astype(jnp.bfloat16), high, low], axis=1)
    got = shifted(wire, axis, by).astype(jnp.float32)
    missing = (place < by).astype(jnp.float32)
    decay_got = got[:, rows : rows + 1, :] + got[:, rows + 1 :, :] + missing
    return jnp.concatenate([got[:, :rows, :], decay_got], axis=1)


def exclusive_scan(packed, axis):
    count = lax.axis_size(axis)
    if count == 1:
        return received(packed, axis, 1)
    held = received(packed, axis, 1)
    if count > 2:
        held = combine_packed(received(packed, axis, 2), held)
    cover = 2
    while cover < count - 1:
        held = combine_packed(received(held, axis, cover), held)
        cover *= 2
    return held


def exchange(block, axis, dim):
    count = lax.axis_size(axis)
    if count & (count - 1):
        return lax.all_gather(block, axis, axis=dim, tiled=True), None
    held, codes = block, [0]
    bit = count // 2
    while bit >= 1:
        other = lax.ppermute(held, axis, [(i, i ^ bit) for i in range(count)])
        held = jnp.concatenate([held, other], axis=dim)
        codes = codes + [c ^ bit for c in codes]
        bit //= 2
    return held, codes


def to_natural(held, codes, axis, dim):
    if codes is None:
        return held
    count = len(codes)
    width = held.shape[dim] // count
    where_code = [0] * count
    for position, code in enumerate(codes):
        where_code[code] = position
    table = jnp.asarray(where_code, jnp.int32)
    place = lax.axis_index(axis)
    parts = [
        lax.dynamic_slice_in_dim(held, table[jnp.bitwise_xor(index, place)] * width, width, axis=dim)
        for index in range(count)
    ]
    return jnp.concatenate(parts, axis=dim)


def segment_of(positions, lengths):
    prompt_ends = jnp.cumsum(lengths)
    counted = (positions[:, None] >= prompt_ends[None, :]).astype(jnp.int32)
    return jnp.sum(counted, axis=1)


def causal_conv(extended, segment_ids, weights, conv_width):
    out_rows = extended.shape[0] - conv_width + 1
    target = segment_ids[conv_width - 1 :]
    running = jnp.zeros((out_rows, extended.shape[1]), jnp.float32)
    for tap_index in range(conv_width):
        matched = (segment_ids[tap_index : tap_index + out_rows] == target).astype(jnp.float32)
        running = (
            running
            + weights[tap_index][None, :]
            * extended[tap_index : tap_index + out_rows]
            * matched[:, None]
        )
    return running


def local_terms(x_heads, b_rows, c_rows, step_size, decay_log, segment_ids, seg_before):
    log_decay = -jnp.exp(decay_log)[None, :] * step_size
    cum_decay = jnp.cumsum(log_decay, axis=0)
    positions_in = jnp.arange(x_heads.shape[0], dtype=jnp.int32)
    same_prompt = (segment_ids[:, None] == segment_ids[None, :]) & (
        positions_in[:, None] >= positions_in[None, :]
    )
    decay_gap = cum_decay.T[:, :, None] - cum_decay.T[:, None, :]
    decay_matrix = jnp.exp(jnp.where(same_prompt[None], decay_gap, -jnp.inf))
    scores = jnp.dot(c_rows, b_rows.T, precision=precise)
    x_step = x_heads * step_size[:, :, None]
    intra = jnp.einsum("hts,shp->thp", scores[None] * decay_matrix, x_step, precision=precise)
    to_end = jnp.exp(
        jnp.where(
            (segment_ids == segment_ids[-1])[:, None], cum_decay[-1][None, :] - cum_decay, -jnp.inf
        )
    )
    state_out = jnp.einsum("shp,sn->hpn", x_step * to_end[:, :, None], b_rows, precision=precise)
    carried = segment_ids == seg_before
    carry_in = jnp.exp(jnp.where(carried[:, None], cum_decay, -jnp.inf))
    block_decay = jnp.where(carried[-1], jnp.exp(cum_decay[-1]), 0.0)
    return (intra, state_out, carry_in, block_decay)


def per_device(
    tokens,
    deal_order,
    lengths,
    x_weight,
    z_weight,
    shared_weight,
    step_weight,
    conv_heads,
    conv_shared,
    step_bias,
    decay_log,
    skip_gain,
):
    seq_count = lax.axis_size("seq")
    own_index = lax.axis_index("seq")
    tok_dev = tokens.shape[0]
    piece_rows = tok_dev // seq_count
    slot_rows = tokens.reshape(seq_count, piece_rows, tokens.shape[1])
    arrived = lax.all_to_all(slot_rows, "seq", split_axis=0, concat_axis=0, tiled=True)
    dealt_row = lax.dynamic_slice_in_dim(deal_order, own_index, 1, 0)[0]
    inverse = jnp.argsort(dealt_row)
    stream_block = jnp.take(arrived, inverse, axis=0).reshape(tok_dev, tokens.shape[1])
    inner_dev = x_weight.shape[1]
    heads_dev = step_weight.shape[1]
    head_dim = inner_dev // heads_dev
    state_dim = shared_weight.shape[1] // 2
    w_held, _ = exchange(shared_weight, "fsdp", 0)
    feature_held, codes = exchange(stream_block, "fsdp", 1)
    feature_part = to_natural(feature_held, codes, "fsdp", 1)
    x_acc, z_acc, step_acc = tuple(
        (
            jnp.dot(feature_part, weight, preferred_element_type=jnp.float32)
            for weight in (x_weight, z_weight, step_weight)
        )
    )
    bc_acc = jnp.dot(feature_held, w_held, preferred_element_type=jnp.float32)
    x_raw = x_acc.astype(jnp.bfloat16)
    z_raw = z_acc.astype(jnp.bfloat16)
    bc_raw = bc_acc.astype(jnp.bfloat16)
    step_size = jax.nn.softplus(step_acc + step_bias[None, :])
    mixed_in = jnp.concatenate([x_raw, bc_raw], axis=1)
    conv_width = conv_heads.shape[0]
    prior_rows = shifted(mixed_in[tok_dev - conv_width + 1 :], "seq", 1)
    first_pos = own_index * tok_dev
    positions = first_pos - (conv_width - 1) + jnp.arange(tok_dev + conv_width - 1, dtype=jnp.int32)
    seg_ext = segment_of(positions, lengths)
    extended = jnp.concatenate([prior_rows, mixed_in], axis=0).astype(jnp.float32)
    activated = jax.nn.silu(
        causal_conv(
            extended, seg_ext, jnp.concatenate([conv_heads, conv_shared], axis=1), conv_width
        )
    )
    segment_ids = seg_ext[conv_width - 1 :]
    seg_before = jnp.where(own_index == 0, -1, seg_ext[conv_width - 2])
    x_heads = activated[:, :inner_dev].reshape(tok_dev, heads_dev, head_dim)
    b_rows = activated[:, inner_dev : inner_dev + state_dim]
    c_rows = activated[:, inner_dev + state_dim :]
    intra, state_out, carry_in, block_decay = local_terms(
        x_heads, b_rows, c_rows, step_size, decay_log, segment_ids, seg_before
    )
    packed = jnp.concatenate(
        [state_out, jnp.broadcast_to(block_decay[:, None, None], (heads_dev, 1, state_dim))], axis=1
    )
    state_in = exclusive_scan(packed, "seq")[:, :head_dim, :]
    incoming = jnp.einsum("tn,hpn->thp", c_rows, state_in, precision=precise)
    y_block = intra + carry_in[:, :, None] * incoming + skip_gain[None, :, None] * x_heads
    gated = (y_block.reshape(tok_dev, inner_dev) * jax.nn.silu(z_raw.astype(jnp.float32))).astype(
        jnp.bfloat16
    )
    ordered = gated.reshape(seq_count, piece_rows, inner_dev)
    outgoing = jnp.take(ordered, dealt_row, axis=0)
    returned = lax.all_to_all(outgoing, "seq", split_axis=0, concat_axis=0, tiled=True)
    return returned.reshape(tok_dev, inner_dev)


def solution(mesh):
    return jax.shard_map(
        per_device,
        mesh=mesh,
        in_specs=(
            P("seq", "fsdp"),
            P(),
            P(),
            P(None, "fsdp"),
            P(None, "fsdp"),
            P("fsdp", None),
            P(None, "fsdp"),
            P(None, "fsdp"),
            P(),
            P("fsdp"),
            P("fsdp"),
            P("fsdp"),
        ),
        out_specs=P("seq", "fsdp"),
        check_vma=False,
    )
```

```python
import jax
import jax.numpy as jnp
from jax import lax
from jax.sharding import PartitionSpec as P

precise = lax.Precision.HIGHEST


def shifted(array, axis, by):
    count = lax.axis_size(axis)
    pairs = [(i, i + by) for i in range(count) if 0 <= i + by < count]
    return lax.ppermute(array, axis, pairs)


def combine_packed(earlier, later):
    rows = later.shape[1] - 1
    d_e, d_l = earlier[:, rows:, :], later[:, rows:, :]
    return jnp.concatenate([d_l * earlier[:, :rows, :] + later[:, :rows, :], d_e * d_l], axis=1)


def received(packed, axis, by):
    place = lax.axis_index(axis)
    rows = packed.shape[1] - 1
    decay = jnp.broadcast_to(packed[:, rows:, :1], (packed.shape[0], 1, packed.shape[2]))
    high = decay.astype(jnp.bfloat16)
    low = (decay - high.astype(jnp.float32)).astype(jnp.bfloat16)
    wire = jnp.concatenate([packed[:, :rows, :].astype(jnp.bfloat16), high, low], axis=1)
    got = shifted(wire, axis, by).astype(jnp.float32)
    missing = (place < by).astype(jnp.float32)
    decay_got = got[:, rows : rows + 1, :] + got[:, rows + 1 :, :] + missing
    return jnp.concatenate([got[:, :rows, :], decay_got], axis=1)


def exclusive_scan(packed, axis, side):
    count = lax.axis_size(axis)
    if count == 1:
        return received(packed, axis, 1), side
    held = received(packed, axis, 1)
    if count > 2:
        held = combine_packed(received(packed, axis, 2), held)
    cover = 2
    while cover < count - 1:
        if cover * 2 >= count - 1:
            held, side = lax.optimization_barrier((held, side))
        held = combine_packed(received(held, axis, cover), held)
        cover *= 2
    return held, side


def exchange(block, axis, dim):
    count = lax.axis_size(axis)
    if count & (count - 1):
        return lax.all_gather(block, axis, axis=dim, tiled=True), None
    held, codes = block, [0]
    bit = count // 2
    while bit >= 1:
        other = lax.ppermute(held, axis, [(i, i ^ bit) for i in range(count)])
        held = jnp.concatenate([held, other], axis=dim)
        codes = codes + [c ^ bit for c in codes]
        bit //= 2
    return held, codes


def to_natural(held, codes, axis, dim):
    if codes is None:
        return held
    count = len(codes)
    width = held.shape[dim] // count
    where_code = [0] * count
    for position, code in enumerate(codes):
        where_code[code] = position
    table = jnp.asarray(where_code, jnp.int32)
    place = lax.axis_index(axis)
    parts = [
        lax.dynamic_slice_in_dim(held, table[jnp.bitwise_xor(index, place)] * width, width, axis=dim)
        for index in range(count)
    ]
    return jnp.concatenate(parts, axis=dim)


def segment_of(positions, lengths):
    prompt_ends = jnp.cumsum(lengths)
    counted = (positions[:, None] >= prompt_ends[None, :]).astype(jnp.int32)
    return jnp.sum(counted, axis=1)


def causal_conv(extended, segment_ids, weights, conv_width):
    out_rows = extended.shape[0] - conv_width + 1
    target = segment_ids[conv_width - 1 :]
    running = jnp.zeros((out_rows, extended.shape[1]), jnp.float32)
    for tap_index in range(conv_width):
        matched = (segment_ids[tap_index : tap_index + out_rows] == target).astype(jnp.float32)
        running = (
            running
            + weights[tap_index][None, :]
            * extended[tap_index : tap_index + out_rows]
            * matched[:, None]
        )
    return running


def local_terms(x_heads, b_rows, c_rows, step_size, decay_log, segment_ids, seg_before):
    log_decay = -jnp.exp(decay_log)[None, :] * step_size
    positions_in = jnp.arange(x_heads.shape[0], dtype=jnp.int32)
    lower = (positions_in[:, None] >= positions_in[None, :]).astype(jnp.float32)
    cum_decay = jnp.dot(lower, log_decay, precision=precise)
    same_prompt = (segment_ids[:, None] == segment_ids[None, :]) & (
        positions_in[:, None] >= positions_in[None, :]
    )
    decay_gap = cum_decay.T[:, :, None] - cum_decay.T[:, None, :]
    decay_matrix = jnp.exp(jnp.where(same_prompt[None], decay_gap, -jnp.inf))
    scores = jnp.dot(c_rows, b_rows.T, precision=precise)
    x_step = x_heads * step_size[:, :, None]
    intra = jnp.einsum("hts,shp->thp", scores[None] * decay_matrix, x_step, precision=precise)
    to_end = jnp.exp(
        jnp.where(
            (segment_ids == segment_ids[-1])[:, None], cum_decay[-1][None, :] - cum_decay, -jnp.inf
        )
    )
    state_out = jnp.einsum("shp,sn->hpn", x_step * to_end[:, :, None], b_rows, precision=precise)
    carried = segment_ids == seg_before
    carry_in = jnp.exp(jnp.where(carried[:, None], cum_decay, -jnp.inf))
    block_decay = jnp.where(carried[-1], jnp.exp(cum_decay[-1]), 0.0)
    return (intra, state_out, carry_in, block_decay)


def per_device(
    tokens,
    deal_order,
    lengths,
    x_weight,
    z_weight,
    shared_weight,
    step_weight,
    conv_heads,
    conv_shared,
    step_bias,
    decay_log,
    skip_gain,
):
    seq_count = lax.axis_size("seq")
    own_index = lax.axis_index("seq")
    tok_dev = tokens.shape[0]
    piece_rows = tok_dev // seq_count
    slot_rows = tokens.reshape(seq_count, piece_rows, tokens.shape[1])
    arrived = lax.all_to_all(slot_rows, "seq", split_axis=0, concat_axis=0, tiled=True)
    dealt_row = lax.dynamic_slice_in_dim(deal_order, own_index, 1, 0)[0]
    inverse = jnp.argsort(dealt_row)
    stream_block = jnp.take(arrived, inverse, axis=0).reshape(tok_dev, tokens.shape[1])
    inner_dev = x_weight.shape[1]
    heads_dev = step_weight.shape[1]
    head_dim = inner_dev // heads_dev
    state_dim = shared_weight.shape[1] // 2
    w_held, _ = exchange(shared_weight, "fsdp", 0)
    feature_held, codes = exchange(stream_block, "fsdp", 1)
    feature_part = to_natural(feature_held, codes, "fsdp", 1)
    x_acc, z_acc, step_acc = tuple(
        (
            jnp.dot(feature_part, weight, preferred_element_type=jnp.float32)
            for weight in (x_weight, z_weight, step_weight)
        )
    )
    bc_acc = jnp.dot(feature_held, w_held, preferred_element_type=jnp.float32)
    x_raw = x_acc.astype(jnp.bfloat16)
    z_raw = z_acc.astype(jnp.bfloat16)
    bc_raw = bc_acc.astype(jnp.bfloat16)
    step_size = jax.nn.softplus(step_acc + step_bias[None, :])
    mixed_in = jnp.concatenate([x_raw, bc_raw], axis=1)
    conv_width = conv_heads.shape[0]
    prior_rows = shifted(mixed_in[tok_dev - conv_width + 1 :], "seq", 1)
    first_pos = own_index * tok_dev
    positions = first_pos - (conv_width - 1) + jnp.arange(tok_dev + conv_width - 1, dtype=jnp.int32)
    seg_ext = segment_of(positions, lengths)
    extended = jnp.concatenate([prior_rows, mixed_in], axis=0).astype(jnp.float32)
    activated = jax.nn.silu(
        causal_conv(
            extended, seg_ext, jnp.concatenate([conv_heads, conv_shared], axis=1), conv_width
        )
    )
    segment_ids = seg_ext[conv_width - 1 :]
    seg_before = jnp.where(own_index == 0, -1, seg_ext[conv_width - 2])
    x_heads = activated[:, :inner_dev].reshape(tok_dev, heads_dev, head_dim)
    b_rows = activated[:, inner_dev : inner_dev + state_dim]
    c_rows = activated[:, inner_dev + state_dim :]
    intra, state_out, carry_in, block_decay = local_terms(
        x_heads, b_rows, c_rows, step_size, decay_log, segment_ids, seg_before
    )
    packed = jnp.concatenate(
        [state_out, jnp.broadcast_to(block_decay[:, None, None], (heads_dev, 1, state_dim))], axis=1
    )
    local_y = intra + skip_gain[None, :, None] * x_heads
    gate = jax.nn.silu(z_raw.astype(jnp.float32)).reshape(tok_dev, heads_dev, head_dim)
    scanned, (local_y, gate, carry_in) = exclusive_scan(packed, "seq", (local_y, gate, carry_in))
    state_in = scanned[:, :head_dim, :]
    incoming = jnp.einsum("tn,hpn->thp", c_rows, state_in, precision=precise)
    y_block = local_y + carry_in[:, :, None] * incoming
    gated = (y_block * gate).reshape(tok_dev, inner_dev).astype(jnp.bfloat16)
    ordered = gated.reshape(seq_count, piece_rows, inner_dev)
    outgoing = jnp.take(ordered, dealt_row, axis=0)
    returned = lax.all_to_all(outgoing, "seq", split_axis=0, concat_axis=0, tiled=True)
    return returned.reshape(tok_dev, inner_dev)


def solution(mesh):
    return jax.shard_map(
        per_device,
        mesh=mesh,
        in_specs=(
            P("seq", "fsdp"),
            P(),
            P(),
            P(None, "fsdp"),
            P(None, "fsdp"),
            P("fsdp", None),
            P(None, "fsdp"),
            P(None, "fsdp"),
            P(),
            P("fsdp"),
            P("fsdp"),
            P("fsdp"),
        ),
        out_specs=P("seq", "fsdp"),
        check_vma=False,
    )
```

```python
import jax
import jax.numpy as jnp
from jax import lax
from jax.sharding import PartitionSpec as P

precise = lax.Precision.HIGHEST


def shifted(array, axis, by):
    count = lax.axis_size(axis)
    pairs = [(i, i + by) for i in range(count) if 0 <= i + by < count]
    return lax.ppermute(array, axis, pairs)


def combine_packed(earlier, later):
    rows = later.shape[1] - 1
    d_e, d_l = earlier[:, rows:, :], later[:, rows:, :]
    return jnp.concatenate([d_l * earlier[:, :rows, :] + later[:, :rows, :], d_e * d_l], axis=1)


def received(packed, axis, by):
    place = lax.axis_index(axis)
    rows = packed.shape[1] - 1
    decay = jnp.broadcast_to(packed[:, rows:, :1], (packed.shape[0], 1, packed.shape[2]))
    high = decay.astype(jnp.bfloat16)
    low = (decay - high.astype(jnp.float32)).astype(jnp.bfloat16)
    wire = jnp.concatenate([packed[:, :rows, :].astype(jnp.bfloat16), high, low], axis=1)
    got = shifted(wire, axis, by).astype(jnp.float32)
    missing = (place < by).astype(jnp.float32)
    decay_got = got[:, rows : rows + 1, :] + got[:, rows + 1 :, :] + missing
    return jnp.concatenate([got[:, :rows, :], decay_got], axis=1)


def exclusive_scan(packed, axis, side):
    count = lax.axis_size(axis)
    if count == 1:
        return received(packed, axis, 1), side
    held = received(packed, axis, 1)
    if count > 2:
        held = combine_packed(received(packed, axis, 2), held)
    cover = 2
    while cover < count - 1:
        if cover * 2 >= count - 1:
            held, side = lax.optimization_barrier((held, side))
        held = combine_packed(received(held, axis, cover), held)
        cover *= 2
    return held, side


def exchange(block, axis, dim):
    count = lax.axis_size(axis)
    if count & (count - 1):
        return lax.all_gather(block, axis, axis=dim, tiled=True), None
    held, codes = block, [0]
    bit = count // 2
    while bit >= 1:
        other = lax.ppermute(held, axis, [(i, i ^ bit) for i in range(count)])
        held = jnp.concatenate([held, other], axis=dim)
        codes = codes + [c ^ bit for c in codes]
        bit //= 2
    return held, codes


def to_natural(held, codes, axis, dim):
    if codes is None:
        return held
    count = len(codes)
    width = held.shape[dim] // count
    where_code = [0] * count
    for position, code in enumerate(codes):
        where_code[code] = position
    table = jnp.asarray(where_code, jnp.int32)
    place = lax.axis_index(axis)
    parts = [
        lax.dynamic_slice_in_dim(held, table[jnp.bitwise_xor(index, place)] * width, width, axis=dim)
        for index in range(count)
    ]
    return jnp.concatenate(parts, axis=dim)


def segment_of(positions, lengths):
    prompt_ends = jnp.cumsum(lengths)
    counted = (positions[:, None] >= prompt_ends[None, :]).astype(jnp.int32)
    return jnp.sum(counted, axis=1)


def causal_conv(extended, segment_ids, weights, conv_width):
    out_rows = extended.shape[0] - conv_width + 1
    target = segment_ids[conv_width - 1 :]
    running = jnp.zeros((out_rows, extended.shape[1]), jnp.float32)
    for tap_index in range(conv_width):
        matched = (segment_ids[tap_index : tap_index + out_rows] == target).astype(jnp.float32)
        running = (
            running
            + weights[tap_index][None, :]
            * extended[tap_index : tap_index + out_rows]
            * matched[:, None]
        )
    return running


def local_terms(x_heads, b_rows, c_rows, step_size, decay_log, segment_ids, seg_before):
    log_decay = -jnp.exp(decay_log)[None, :] * step_size
    positions_in = jnp.arange(x_heads.shape[0], dtype=jnp.int32)
    lower = (positions_in[:, None] >= positions_in[None, :]).astype(jnp.float32)
    cum_decay = jnp.dot(lower, log_decay, precision=precise)
    same_prompt = (segment_ids[:, None] == segment_ids[None, :]) & (
        positions_in[:, None] >= positions_in[None, :]
    )
    decay_gap = cum_decay.T[:, :, None] - cum_decay.T[:, None, :]
    decay_matrix = jnp.exp(jnp.where(same_prompt[None], decay_gap, -jnp.inf))
    scores = jnp.dot(c_rows, b_rows.T, precision=precise)
    x_step = x_heads * step_size[:, :, None]
    intra = jnp.einsum("hts,shp->thp", scores[None] * decay_matrix, x_step, precision=precise)
    to_end = jnp.exp(
        jnp.where(
            (segment_ids == segment_ids[-1])[:, None], cum_decay[-1][None, :] - cum_decay, -jnp.inf
        )
    )
    state_out = jnp.einsum("shp,sn->hpn", x_step * to_end[:, :, None], b_rows, precision=precise)
    carried = segment_ids == seg_before
    carry_in = jnp.exp(jnp.where(carried[:, None], cum_decay, -jnp.inf))
    block_decay = jnp.where(carried[-1], jnp.exp(cum_decay[-1]), 0.0)
    return (intra, state_out, carry_in, block_decay)


def per_device(
    tokens,
    deal_order,
    lengths,
    x_weight,
    z_weight,
    shared_weight,
    step_weight,
    conv_heads,
    conv_shared,
    step_bias,
    decay_log,
    skip_gain,
):
    seq_count = lax.axis_size("seq")
    own_index = lax.axis_index("seq")
    tok_dev = tokens.shape[0]
    piece_rows = tok_dev // seq_count
    conv_width = conv_heads.shape[0]
    halo = conv_width - 1
    slot_rows = tokens.reshape(seq_count, piece_rows, tokens.shape[1])
    tail = min(halo, piece_rows)
    tail_pad = 16 if piece_rows % 16 == 0 and tail <= 16 else tail
    tails = jnp.roll(slot_rows[:, piece_rows - tail :, :], 1, axis=0)
    tails = jnp.pad(tails, ((0, 0), (0, tail_pad - tail), (0, 0)))
    outgoing_rows = jnp.concatenate([slot_rows, tails], axis=1)
    arrived = lax.all_to_all(outgoing_rows, "seq", split_axis=0, concat_axis=0, tiled=True)
    dealt_row = lax.dynamic_slice_in_dim(deal_order, own_index, 1, 0)[0]
    inverse = jnp.argsort(dealt_row)
    stream_block = jnp.take(arrived[:, :piece_rows, :], inverse, axis=0).reshape(tok_dev, tokens.shape[1])
    prior_row = lax.dynamic_slice_in_dim(deal_order, (own_index + seq_count - 1) % seq_count, 1, 0)[0]
    inverse_prior = jnp.argsort(prior_row)
    block_rows = [tok_dev - halo + r for r in range(halo)]
    pieces = jnp.asarray([b // piece_rows for b in block_rows], jnp.int32)
    within = jnp.asarray([b % piece_rows - (piece_rows - tail) for b in block_rows], jnp.int32)
    tail_in = arrived[:, piece_rows : piece_rows + tail, :].reshape(seq_count * tail, tokens.shape[1])
    halo_rows = jnp.take(tail_in, inverse_prior[pieces] * tail + within, axis=0)
    halo_rows = jnp.where(own_index > 0, halo_rows, jnp.zeros_like(halo_rows))
    extended_rows = jnp.concatenate([stream_block, halo_rows], axis=0)
    inner_dev = x_weight.shape[1]
    heads_dev = step_weight.shape[1]
    head_dim = inner_dev // heads_dev
    state_dim = shared_weight.shape[1] // 2
    w_held, _ = exchange(shared_weight, "fsdp", 0)
    feature_held, codes = exchange(extended_rows, "fsdp", 1)
    feature_ext = to_natural(feature_held, codes, "fsdp", 1)
    feature_part = feature_ext[:tok_dev]
    x_ext = jnp.dot(feature_ext, x_weight, preferred_element_type=jnp.float32)
    z_acc, step_acc = tuple(
        (
            jnp.dot(feature_part, weight, preferred_element_type=jnp.float32)
            for weight in (z_weight, step_weight)
        )
    )
    bc_ext = jnp.dot(feature_held, w_held, preferred_element_type=jnp.float32)
    z_raw = z_acc.astype(jnp.bfloat16)
    step_size = jax.nn.softplus(step_acc + step_bias[None, :])
    mixed_ext = jnp.concatenate([x_ext.astype(jnp.bfloat16), bc_ext.astype(jnp.bfloat16)], axis=1)
    first_pos = own_index * tok_dev
    positions = first_pos - (conv_width - 1) + jnp.arange(tok_dev + conv_width - 1, dtype=jnp.int32)
    seg_ext = segment_of(positions, lengths)
    extended = jnp.concatenate([mixed_ext[tok_dev:], mixed_ext[:tok_dev]], axis=0).astype(jnp.float32)
    activated = jax.nn.silu(
        causal_conv(
            extended, seg_ext, jnp.concatenate([conv_heads, conv_shared], axis=1), conv_width
        )
    )
    segment_ids = seg_ext[conv_width - 1 :]
    seg_before = jnp.where(own_index == 0, -1, seg_ext[conv_width - 2])
    x_heads = activated[:, :inner_dev].reshape(tok_dev, heads_dev, head_dim)
    b_rows = activated[:, inner_dev : inner_dev + state_dim]
    c_rows = activated[:, inner_dev + state_dim :]
    intra, state_out, carry_in, block_decay = local_terms(
        x_heads, b_rows, c_rows, step_size, decay_log, segment_ids, seg_before
    )
    packed = jnp.concatenate(
        [state_out, jnp.broadcast_to(block_decay[:, None, None], (heads_dev, 1, state_dim))], axis=1
    )
    local_y = intra + skip_gain[None, :, None] * x_heads
    gate = jax.nn.silu(z_raw.astype(jnp.float32)).reshape(tok_dev, heads_dev, head_dim)
    scanned, (local_y, gate, carry_in) = exclusive_scan(packed, "seq", (local_y, gate, carry_in))
    state_in = scanned[:, :head_dim, :]
    incoming = jnp.einsum("tn,hpn->thp", c_rows, state_in, precision=precise)
    y_block = local_y + carry_in[:, :, None] * incoming
    gated = (y_block * gate).reshape(tok_dev, inner_dev).astype(jnp.bfloat16)
    ordered = gated.reshape(seq_count, piece_rows, inner_dev)
    outgoing = jnp.take(ordered, dealt_row, axis=0)
    returned = lax.all_to_all(outgoing, "seq", split_axis=0, concat_axis=0, tiled=True)
    return returned.reshape(tok_dev, inner_dev)


def solution(mesh):
    return jax.shard_map(
        per_device,
        mesh=mesh,
        in_specs=(
            P("seq", "fsdp"),
            P(),
            P(),
            P(None, "fsdp"),
            P(None, "fsdp"),
            P("fsdp", None),
            P(None, "fsdp"),
            P(None, "fsdp"),
            P(),
            P("fsdp"),
            P("fsdp"),
            P("fsdp"),
        ),
        out_specs=P("seq", "fsdp"),
        check_vma=False,
    )
```

```python
import jax
import jax.numpy as jnp
from jax import lax
from jax.sharding import PartitionSpec as P

precise = lax.Precision.HIGHEST


def shifted(array, axis, by):
    count = lax.axis_size(axis)
    pairs = [(i, i + by) for i in range(count) if 0 <= i + by < count]
    return lax.ppermute(array, axis, pairs)


def combine_packed(earlier, later):
    rows = later.shape[1] - 2
    d_e, d_l = earlier[:, rows : rows + 1, :], later[:, rows : rows + 1, :]
    state = d_l * earlier[:, :rows, :] + later[:, :rows, :]
    decay = d_e * d_l
    return jnp.concatenate([state, decay, decay], axis=1)


def received(packed, axis, by):
    place = lax.axis_index(axis)
    rows = packed.shape[1] - 2
    row = lax.broadcasted_iota(jnp.int32, packed.shape, 1)
    high = packed.astype(jnp.bfloat16)
    low = (packed - high.astype(jnp.float32)).astype(jnp.bfloat16)
    wire = jnp.where(row == rows + 1, low, high)
    got = shifted(wire, axis, by).astype(jnp.float32)
    missing = (place < by).astype(jnp.float32)
    decay = got[:, rows : rows + 1, :] + got[:, rows + 1 :, :] + missing
    return jnp.concatenate([got[:, :rows, :], decay, decay], axis=1)


def exclusive_scan(packed, axis, side):
    count = lax.axis_size(axis)
    if count == 1:
        return received(packed, axis, 1), side
    held = received(packed, axis, 1)
    if count > 2:
        held = combine_packed(received(packed, axis, 2), held)
    cover = 2
    while cover < count - 1:
        if cover * 2 >= count - 1:
            held, side = lax.optimization_barrier((held, side))
        held = combine_packed(received(held, axis, cover), held)
        cover *= 2
    return held, side


def exchange(block, axis, dim):
    count = lax.axis_size(axis)
    if count & (count - 1):
        return lax.all_gather(block, axis, axis=dim, tiled=True), None
    held, codes = block, [0]
    bit = count // 2
    while bit >= 1:
        other = lax.ppermute(held, axis, [(i, i ^ bit) for i in range(count)])
        held = jnp.concatenate([held, other], axis=dim)
        codes = codes + [c ^ bit for c in codes]
        bit //= 2
    return held, codes


def to_natural(held, codes, axis, dim):
    if codes is None:
        return held
    count = len(codes)
    width = held.shape[dim] // count
    where_code = [0] * count
    for position, code in enumerate(codes):
        where_code[code] = position
    table = jnp.asarray(where_code, jnp.int32)
    place = lax.axis_index(axis)
    parts = [
        lax.dynamic_slice_in_dim(held, table[jnp.bitwise_xor(index, place)] * width, width, axis=dim)
        for index in range(count)
    ]
    return jnp.concatenate(parts, axis=dim)


def segment_of(positions, lengths):
    prompt_ends = jnp.cumsum(lengths)
    counted = (positions[:, None] >= prompt_ends[None, :]).astype(jnp.int32)
    return jnp.sum(counted, axis=1)


def causal_conv(extended, segment_ids, weights, conv_width):
    out_rows = extended.shape[0] - conv_width + 1
    target = segment_ids[conv_width - 1 :]
    running = jnp.zeros((out_rows, extended.shape[1]), jnp.float32)
    for tap_index in range(conv_width):
        matched = (segment_ids[tap_index : tap_index + out_rows] == target).astype(jnp.float32)
        running = (
            running
            + weights[tap_index][None, :]
            * extended[tap_index : tap_index + out_rows]
            * matched[:, None]
        )
    return running


def local_terms(x_heads, b_rows, c_rows, step_size, decay_log, segment_ids, seg_before):
    log_decay = -jnp.exp(decay_log)[None, :] * step_size
    positions_in = jnp.arange(x_heads.shape[0], dtype=jnp.int32)
    lower = (positions_in[:, None] >= positions_in[None, :]).astype(jnp.float32)
    cum_decay = jnp.dot(lower, log_decay, precision=precise)
    same_prompt = (segment_ids[:, None] == segment_ids[None, :]) & (
        positions_in[:, None] >= positions_in[None, :]
    )
    decay_gap = cum_decay.T[:, :, None] - cum_decay.T[:, None, :]
    decay_matrix = jnp.exp(jnp.where(same_prompt[None], decay_gap, -jnp.inf))
    scores = jnp.dot(c_rows, b_rows.T, precision=precise)
    x_step = x_heads * step_size[:, :, None]
    intra = jnp.einsum("hts,shp->thp", scores[None] * decay_matrix, x_step, precision=precise)
    to_end = jnp.exp(
        jnp.where(
            (segment_ids == segment_ids[-1])[:, None], cum_decay[-1][None, :] - cum_decay, -jnp.inf
        )
    )
    state_out = jnp.einsum("shp,sn->hpn", x_step * to_end[:, :, None], b_rows, precision=precise)
    carried = segment_ids == seg_before
    carry_in = jnp.exp(jnp.where(carried[:, None], cum_decay, -jnp.inf))
    block_decay = jnp.where(carried[-1], jnp.exp(cum_decay[-1]), 0.0)
    return (intra, state_out, carry_in, block_decay)


def per_device(
    tokens,
    deal_order,
    lengths,
    x_weight,
    z_weight,
    shared_weight,
    step_weight,
    conv_heads,
    conv_shared,
    step_bias,
    decay_log,
    skip_gain,
):
    seq_count = lax.axis_size("seq")
    own_index = lax.axis_index("seq")
    tok_dev = tokens.shape[0]
    piece_rows = tok_dev // seq_count
    slot_rows = tokens.reshape(seq_count, piece_rows, tokens.shape[1])
    arrived = lax.all_to_all(slot_rows, "seq", split_axis=0, concat_axis=0, tiled=True)
    dealt_row = lax.dynamic_slice_in_dim(deal_order, own_index, 1, 0)[0]
    inverse = jnp.argsort(dealt_row)
    stream_block = jnp.take(arrived, inverse, axis=0).reshape(tok_dev, tokens.shape[1])
    inner_dev = x_weight.shape[1]
    heads_dev = step_weight.shape[1]
    head_dim = inner_dev // heads_dev
    state_dim = shared_weight.shape[1] // 2
    w_held, _ = exchange(shared_weight, "fsdp", 0)
    feature_held, codes = exchange(stream_block, "fsdp", 1)
    feature_part = to_natural(feature_held, codes, "fsdp", 1)
    x_acc, z_acc, step_acc = tuple(
        (
            jnp.dot(feature_part, weight, preferred_element_type=jnp.float32)
            for weight in (x_weight, z_weight, step_weight)
        )
    )
    bc_acc = jnp.dot(feature_held, w_held, preferred_element_type=jnp.float32)
    x_raw = x_acc.astype(jnp.bfloat16)
    z_raw = z_acc.astype(jnp.bfloat16)
    bc_raw = bc_acc.astype(jnp.bfloat16)
    step_size = jax.nn.softplus(step_acc + step_bias[None, :])
    mixed_in = jnp.concatenate([x_raw, bc_raw], axis=1)
    conv_width = conv_heads.shape[0]
    prior_rows = shifted(mixed_in[tok_dev - conv_width + 1 :], "seq", 1)
    first_pos = own_index * tok_dev
    positions = first_pos - (conv_width - 1) + jnp.arange(tok_dev + conv_width - 1, dtype=jnp.int32)
    seg_ext = segment_of(positions, lengths)
    extended = jnp.concatenate([prior_rows, mixed_in], axis=0).astype(jnp.float32)
    activated = jax.nn.silu(
        causal_conv(
            extended, seg_ext, jnp.concatenate([conv_heads, conv_shared], axis=1), conv_width
        )
    )
    segment_ids = seg_ext[conv_width - 1 :]
    seg_before = jnp.where(own_index == 0, -1, seg_ext[conv_width - 2])
    x_heads = activated[:, :inner_dev].reshape(tok_dev, heads_dev, head_dim)
    b_rows = activated[:, inner_dev : inner_dev + state_dim]
    c_rows = activated[:, inner_dev + state_dim :]
    intra, state_out, carry_in, block_decay = local_terms(
        x_heads, b_rows, c_rows, step_size, decay_log, segment_ids, seg_before
    )
    decay_rows = jnp.broadcast_to(block_decay[:, None, None], (heads_dev, 2, state_dim))
    packed = jnp.concatenate([state_out, decay_rows], axis=1)
    local_y = intra + skip_gain[None, :, None] * x_heads
    gate = jax.nn.silu(z_raw.astype(jnp.float32)).reshape(tok_dev, heads_dev, head_dim)
    scanned, (local_y, gate, carry_in) = exclusive_scan(packed, "seq", (local_y, gate, carry_in))
    state_in = scanned[:, :head_dim, :]
    incoming = jnp.einsum("tn,hpn->thp", c_rows, state_in, precision=precise)
    y_block = local_y + carry_in[:, :, None] * incoming
    gated = (y_block * gate).reshape(tok_dev, inner_dev).astype(jnp.bfloat16)
    ordered = gated.reshape(seq_count, piece_rows, inner_dev)
    outgoing = jnp.take(ordered, dealt_row, axis=0)
    returned = lax.all_to_all(outgoing, "seq", split_axis=0, concat_axis=0, tiled=True)
    return returned.reshape(tok_dev, inner_dev)


def solution(mesh):
    return jax.shard_map(
        per_device,
        mesh=mesh,
        in_specs=(
            P("seq", "fsdp"),
            P(),
            P(),
            P(None, "fsdp"),
            P(None, "fsdp"),
            P("fsdp", None),
            P(None, "fsdp"),
            P(None, "fsdp"),
            P(),
            P("fsdp"),
            P("fsdp"),
            P("fsdp"),
        ),
        out_specs=P("seq", "fsdp"),
        check_vma=False,
    )
```

```python
import jax
import jax.numpy as jnp
from jax import lax
from jax.sharding import PartitionSpec as P

precise = lax.Precision.HIGHEST


def shifted(array, axis, by):
    count = lax.axis_size(axis)
    pairs = [(i, i + by) for i in range(count) if 0 <= i + by < count]
    return lax.ppermute(array, axis, pairs)


def combine_packed(earlier, later):
    rows = later.shape[1] - 2
    d_e, d_l = earlier[:, rows : rows + 1, :], later[:, rows : rows + 1, :]
    state = d_l * earlier[:, :rows, :] + later[:, :rows, :]
    decay = d_e * d_l
    return jnp.concatenate([state, decay, decay], axis=1)


def received(packed, axis, by):
    place = lax.axis_index(axis)
    rows = packed.shape[1] - 2
    row = lax.broadcasted_iota(jnp.int32, packed.shape, 1)
    high = packed.astype(jnp.bfloat16)
    low = (packed - high.astype(jnp.float32)).astype(jnp.bfloat16)
    wire = jnp.where(row == rows + 1, low, high)
    got = shifted(wire, axis, by).astype(jnp.float32)
    missing = (place < by).astype(jnp.float32)
    decay = got[:, rows : rows + 1, :] + got[:, rows + 1 :, :] + missing
    return jnp.concatenate([got[:, :rows, :], decay, decay], axis=1)


def exclusive_scan(packed, axis, side):
    count = lax.axis_size(axis)
    if count == 1:
        return received(packed, axis, 1), side
    held = received(packed, axis, 1)
    if count > 2:
        held = combine_packed(received(packed, axis, 2), held)
    cover = 2
    while cover < count - 1:
        if cover * 2 >= count - 1:
            held, side = lax.optimization_barrier((held, side))
        held = combine_packed(received(held, axis, cover), held)
        cover *= 2
    return held, side


def exchange(block, axis, dim):
    count = lax.axis_size(axis)
    if count & (count - 1):
        return lax.all_gather(block, axis, axis=dim, tiled=True), None
    held, codes = block, [0]
    bit = count // 2
    while bit >= 1:
        other = lax.ppermute(held, axis, [(i, i ^ bit) for i in range(count)])
        held = jnp.concatenate([held, other], axis=dim)
        codes = codes + [c ^ bit for c in codes]
        bit //= 2
    return held, codes


def to_natural(held, codes, axis, dim):
    if codes is None:
        return held
    count = len(codes)
    width = held.shape[dim] // count
    where_code = [0] * count
    for position, code in enumerate(codes):
        where_code[code] = position
    table = jnp.asarray(where_code, jnp.int32)
    place = lax.axis_index(axis)
    parts = [
        lax.dynamic_slice_in_dim(held, table[jnp.bitwise_xor(index, place)] * width, width, axis=dim)
        for index in range(count)
    ]
    return jnp.concatenate(parts, axis=dim)


def summed_columns(partial, axis):
    count = lax.axis_size(axis)
    if count & (count - 1) or partial.shape[1] % 2:
        return lax.psum(partial, axis).astype(jnp.bfloat16)
    if count == 1:
        return partial.astype(jnp.bfloat16)
    place = lax.axis_index(axis)
    half = partial.shape[1] // 2
    side = place % 2
    kept = lax.dynamic_slice_in_dim(partial, side * half, half, axis=1)
    sent = lax.dynamic_slice_in_dim(partial, (1 - side) * half, half, axis=1)
    kept = kept + lax.ppermute(sent, axis, [(i, i ^ 1) for i in range(count)])
    bit = 2
    while bit < count:
        kept = kept + lax.ppermute(kept, axis, [(i, i ^ bit) for i in range(count)])
        bit *= 2
    kept = kept.astype(jnp.bfloat16)
    other = lax.ppermute(kept, axis, [(i, i ^ 1) for i in range(count)])
    both = jnp.concatenate([kept, other], axis=1)
    return jnp.where(side == 0, both, jnp.concatenate([other, kept], axis=1))


def segment_of(positions, lengths):
    prompt_ends = jnp.cumsum(lengths)
    counted = (positions[:, None] >= prompt_ends[None, :]).astype(jnp.int32)
    return jnp.sum(counted, axis=1)


def causal_conv(extended, segment_ids, weights, conv_width):
    out_rows = extended.shape[0] - conv_width + 1
    target = segment_ids[conv_width - 1 :]
    running = jnp.zeros((out_rows, extended.shape[1]), jnp.float32)
    for tap_index in range(conv_width):
        matched = (segment_ids[tap_index : tap_index + out_rows] == target).astype(jnp.float32)
        running = (
            running
            + weights[tap_index][None, :]
            * extended[tap_index : tap_index + out_rows]
            * matched[:, None]
        )
    return running


def local_terms(x_heads, b_rows, c_rows, step_size, decay_log, segment_ids, seg_before):
    log_decay = -jnp.exp(decay_log)[None, :] * step_size
    positions_in = jnp.arange(x_heads.shape[0], dtype=jnp.int32)
    lower = (positions_in[:, None] >= positions_in[None, :]).astype(jnp.float32)
    cum_decay = jnp.dot(lower, log_decay, precision=precise)
    same_prompt = (segment_ids[:, None] == segment_ids[None, :]) & (
        positions_in[:, None] >= positions_in[None, :]
    )
    decay_gap = cum_decay.T[:, :, None] - cum_decay.T[:, None, :]
    decay_matrix = jnp.exp(jnp.where(same_prompt[None], decay_gap, -jnp.inf))
    scores = jnp.dot(c_rows, b_rows.T, precision=precise)
    x_step = x_heads * step_size[:, :, None]
    intra = jnp.einsum("hts,shp->thp", scores[None] * decay_matrix, x_step, precision=precise)
    to_end = jnp.exp(
        jnp.where(
            (segment_ids == segment_ids[-1])[:, None], cum_decay[-1][None, :] - cum_decay, -jnp.inf
        )
    )
    state_out = jnp.einsum("shp,sn->hpn", x_step * to_end[:, :, None], b_rows, precision=precise)
    carried = segment_ids == seg_before
    carry_in = jnp.exp(jnp.where(carried[:, None], cum_decay, -jnp.inf))
    block_decay = jnp.where(carried[-1], jnp.exp(cum_decay[-1]), 0.0)
    return (intra, state_out, carry_in, block_decay)


def per_device(
    tokens,
    deal_order,
    lengths,
    x_weight,
    z_weight,
    shared_weight,
    step_weight,
    conv_heads,
    conv_shared,
    step_bias,
    decay_log,
    skip_gain,
):
    seq_count = lax.axis_size("seq")
    own_index = lax.axis_index("seq")
    tok_dev = tokens.shape[0]
    piece_rows = tok_dev // seq_count
    slot_rows = tokens.reshape(seq_count, piece_rows, tokens.shape[1])
    arrived = lax.all_to_all(slot_rows, "seq", split_axis=0, concat_axis=0, tiled=True)
    dealt_row = lax.dynamic_slice_in_dim(deal_order, own_index, 1, 0)[0]
    inverse = jnp.argsort(dealt_row)
    stream_block = jnp.take(arrived, inverse, axis=0).reshape(tok_dev, tokens.shape[1])
    inner_dev = x_weight.shape[1]
    heads_dev = step_weight.shape[1]
    head_dim = inner_dev // heads_dev
    state_dim = shared_weight.shape[1] // 2
    bc_partial = jnp.dot(stream_block, shared_weight, preferred_element_type=jnp.float32)
    bc_raw = summed_columns(bc_partial, "fsdp")
    feature_held, codes = exchange(stream_block, "fsdp", 1)
    feature_part = to_natural(feature_held, codes, "fsdp", 1)
    x_acc, z_acc, step_acc = tuple(
        (
            jnp.dot(feature_part, weight, preferred_element_type=jnp.float32)
            for weight in (x_weight, z_weight, step_weight)
        )
    )
    x_raw = x_acc.astype(jnp.bfloat16)
    z_raw = z_acc.astype(jnp.bfloat16)
    step_size = jax.nn.softplus(step_acc + step_bias[None, :])
    mixed_in = jnp.concatenate([x_raw, bc_raw], axis=1)
    conv_width = conv_heads.shape[0]
    prior_rows = shifted(mixed_in[tok_dev - conv_width + 1 :], "seq", 1)
    first_pos = own_index * tok_dev
    positions = first_pos - (conv_width - 1) + jnp.arange(tok_dev + conv_width - 1, dtype=jnp.int32)
    seg_ext = segment_of(positions, lengths)
    extended = jnp.concatenate([prior_rows, mixed_in], axis=0).astype(jnp.float32)
    activated = jax.nn.silu(
        causal_conv(
            extended, seg_ext, jnp.concatenate([conv_heads, conv_shared], axis=1), conv_width
        )
    )
    segment_ids = seg_ext[conv_width - 1 :]
    seg_before = jnp.where(own_index == 0, -1, seg_ext[conv_width - 2])
    x_heads = activated[:, :inner_dev].reshape(tok_dev, heads_dev, head_dim)
    b_rows = activated[:, inner_dev : inner_dev + state_dim]
    c_rows = activated[:, inner_dev + state_dim :]
    intra, state_out, carry_in, block_decay = local_terms(
        x_heads, b_rows, c_rows, step_size, decay_log, segment_ids, seg_before
    )
    decay_rows = jnp.broadcast_to(block_decay[:, None, None], (heads_dev, 2, state_dim))
    packed = jnp.concatenate([state_out, decay_rows], axis=1)
    local_y = intra + skip_gain[None, :, None] * x_heads
    gate = jax.nn.silu(z_raw.astype(jnp.float32)).reshape(tok_dev, heads_dev, head_dim)
    scanned, (local_y, gate, carry_in) = exclusive_scan(packed, "seq", (local_y, gate, carry_in))
    state_in = scanned[:, :head_dim, :]
    incoming = jnp.einsum("tn,hpn->thp", c_rows, state_in, precision=precise)
    y_block = local_y + carry_in[:, :, None] * incoming
    gated = (y_block * gate).reshape(tok_dev, inner_dev).astype(jnp.bfloat16)
    ordered = gated.reshape(seq_count, piece_rows, inner_dev)
    outgoing = jnp.take(ordered, dealt_row, axis=0)
    returned = lax.all_to_all(outgoing, "seq", split_axis=0, concat_axis=0, tiled=True)
    return returned.reshape(tok_dev, inner_dev)


def solution(mesh):
    return jax.shard_map(
        per_device,
        mesh=mesh,
        in_specs=(
            P("seq", "fsdp"),
            P(),
            P(),
            P(None, "fsdp"),
            P(None, "fsdp"),
            P("fsdp", None),
            P(None, "fsdp"),
            P(None, "fsdp"),
            P(),
            P("fsdp"),
            P("fsdp"),
            P("fsdp"),
        ),
        out_specs=P("seq", "fsdp"),
        check_vma=False,
    )
```

```python
import jax
import jax.numpy as jnp
from jax import lax
from jax.sharding import PartitionSpec as P

precise = lax.Precision.HIGHEST


def shifted(array, axis, by):
    count = lax.axis_size(axis)
    pairs = [(i, i + by) for i in range(count) if 0 <= i + by < count]
    return lax.ppermute(array, axis, pairs)


def combine_packed(earlier, later):
    rows = later.shape[1] - 2
    d_e, d_l = earlier[:, rows : rows + 1, :], later[:, rows : rows + 1, :]
    state = d_l * earlier[:, :rows, :] + later[:, :rows, :]
    decay = d_e * d_l
    return jnp.concatenate([state, decay, decay], axis=1)


def received(packed, axis, by):
    place = lax.axis_index(axis)
    rows = packed.shape[1] - 2
    row = lax.broadcasted_iota(jnp.int32, packed.shape, 1)
    high = packed.astype(jnp.bfloat16)
    low = (packed - high.astype(jnp.float32)).astype(jnp.bfloat16)
    wire = jnp.where(row == rows + 1, low, high)
    got = shifted(wire, axis, by).astype(jnp.float32)
    missing = (place < by).astype(jnp.float32)
    decay = got[:, rows : rows + 1, :] + got[:, rows + 1 :, :] + missing
    return jnp.concatenate([got[:, :rows, :], decay, decay], axis=1)


def exclusive_scan(packed, axis, side):
    count = lax.axis_size(axis)
    if count == 1:
        return received(packed, axis, 1), side
    held = received(packed, axis, 1)
    if count > 2:
        held = combine_packed(received(packed, axis, 2), held)
    cover = 2
    while cover < count - 1:
        if cover * 2 >= count - 1:
            held, side = lax.optimization_barrier((held, side))
        held = combine_packed(received(held, axis, cover), held)
        cover *= 2
    return held, side


def exchange(block, axis, dim):
    count = lax.axis_size(axis)
    if count & (count - 1):
        return lax.all_gather(block, axis, axis=dim, tiled=True), None
    held, codes = block, [0]
    bit = count // 2
    while bit >= 1:
        other = lax.ppermute(held, axis, [(i, i ^ bit) for i in range(count)])
        held = jnp.concatenate([held, other], axis=dim)
        codes = codes + [c ^ bit for c in codes]
        bit //= 2
    return held, codes


def to_natural(held, codes, axis, dim):
    if codes is None:
        return held
    count = len(codes)
    width = held.shape[dim] // count
    where_code = [0] * count
    for position, code in enumerate(codes):
        where_code[code] = position
    table = jnp.asarray(where_code, jnp.int32)
    place = lax.axis_index(axis)
    parts = [
        lax.dynamic_slice_in_dim(held, table[jnp.bitwise_xor(index, place)] * width, width, axis=dim)
        for index in range(count)
    ]
    return jnp.concatenate(parts, axis=dim)


def summed_columns(partial, axis):
    count = lax.axis_size(axis)
    if count & (count - 1) or partial.shape[1] % 2:
        return lax.psum(partial, axis).astype(jnp.bfloat16)
    if count == 1:
        return partial.astype(jnp.bfloat16)
    place = lax.axis_index(axis)
    half = partial.shape[1] // 2
    side = place % 2
    kept = lax.dynamic_slice_in_dim(partial, side * half, half, axis=1)
    sent = lax.dynamic_slice_in_dim(partial, (1 - side) * half, half, axis=1)
    kept = kept + lax.ppermute(sent, axis, [(i, i ^ 1) for i in range(count)])
    bit = 2
    while bit < count:
        kept = kept + lax.ppermute(kept, axis, [(i, i ^ bit) for i in range(count)])
        bit *= 2
    kept = kept.astype(jnp.bfloat16)
    other = lax.ppermute(kept, axis, [(i, i ^ 1) for i in range(count)])
    both = jnp.concatenate([kept, other], axis=1)
    return jnp.where(side == 0, both, jnp.concatenate([other, kept], axis=1))


def scattered_columns(partial, axis):
    count = lax.axis_size(axis)
    place = lax.axis_index(axis)
    bit = 1
    while bit < count:
        half = partial.shape[1] // 2
        side = (place // bit) % 2
        kept = lax.dynamic_slice_in_dim(partial, side * half, half, axis=1)
        sent = lax.dynamic_slice_in_dim(partial, (1 - side) * half, half, axis=1)
        partial = kept + lax.ppermute(sent, axis, [(i, i ^ bit) for i in range(count)])
        bit *= 2
    return partial.astype(jnp.bfloat16)


def bit_reversed(index, count):
    out, bit, top = 0, 1, count // 2
    while bit < count:
        if index & bit:
            out += top
        bit *= 2
        top //= 2
    return out


def segment_of(positions, lengths):
    prompt_ends = jnp.cumsum(lengths)
    counted = (positions[:, None] >= prompt_ends[None, :]).astype(jnp.int32)
    return jnp.sum(counted, axis=1)


def causal_conv(extended, segment_ids, weights, conv_width):
    out_rows = extended.shape[0] - conv_width + 1
    target = segment_ids[conv_width - 1 :]
    running = jnp.zeros((out_rows, extended.shape[1]), jnp.float32)
    for tap_index in range(conv_width):
        matched = (segment_ids[tap_index : tap_index + out_rows] == target).astype(jnp.float32)
        running = (
            running
            + weights[tap_index][None, :]
            * extended[tap_index : tap_index + out_rows]
            * matched[:, None]
        )
    return running


def local_terms(x_heads, b_rows, c_rows, step_size, decay_log, segment_ids, seg_before):
    log_decay = -jnp.exp(decay_log)[None, :] * step_size
    positions_in = jnp.arange(x_heads.shape[0], dtype=jnp.int32)
    lower = (positions_in[:, None] >= positions_in[None, :]).astype(jnp.float32)
    cum_decay = jnp.dot(lower, log_decay, precision=precise)
    same_prompt = (segment_ids[:, None] == segment_ids[None, :]) & (
        positions_in[:, None] >= positions_in[None, :]
    )
    decay_gap = cum_decay.T[:, :, None] - cum_decay.T[:, None, :]
    decay_matrix = jnp.exp(jnp.where(same_prompt[None], decay_gap, -jnp.inf))
    scores = jnp.dot(c_rows, b_rows.T, precision=precise)
    x_step = x_heads * step_size[:, :, None]
    intra = jnp.einsum("hts,shp->thp", scores[None] * decay_matrix, x_step, precision=precise)
    to_end = jnp.exp(
        jnp.where(
            (segment_ids == segment_ids[-1])[:, None], cum_decay[-1][None, :] - cum_decay, -jnp.inf
        )
    )
    state_out = jnp.einsum("shp,sn->hpn", x_step * to_end[:, :, None], b_rows, precision=precise)
    carried = segment_ids == seg_before
    carry_in = jnp.exp(jnp.where(carried[:, None], cum_decay, -jnp.inf))
    block_decay = jnp.where(carried[-1], jnp.exp(cum_decay[-1]), 0.0)
    return (intra, state_out, carry_in, block_decay)


def per_device(
    tokens,
    deal_order,
    lengths,
    x_weight,
    z_weight,
    shared_weight,
    step_weight,
    conv_heads,
    conv_shared,
    step_bias,
    decay_log,
    skip_gain,
):
    seq_count = lax.axis_size("seq")
    own_index = lax.axis_index("seq")
    tok_dev = tokens.shape[0]
    piece_rows = tok_dev // seq_count
    model_cols = tokens.shape[1]
    fsdp_count = lax.axis_size("fsdp")
    fsdp_place = lax.axis_index("fsdp")
    split_ok = fsdp_count & (fsdp_count - 1) == 0 and shared_weight.shape[1] % fsdp_count == 0
    if split_ok:
        bc_quarter = scattered_columns(
            jnp.dot(tokens, shared_weight, preferred_element_type=jnp.float32), "fsdp"
        )
        quarter = bc_quarter.shape[1]
        sent_rows = jnp.concatenate([tokens, bc_quarter], axis=1)
    else:
        quarter = 0
        sent_rows = tokens
    width = sent_rows.shape[1]
    slot_rows = sent_rows.reshape(seq_count, piece_rows, width)
    arrived = lax.all_to_all(slot_rows, "seq", split_axis=0, concat_axis=0, tiled=True)
    dealt_row = lax.dynamic_slice_in_dim(deal_order, own_index, 1, 0)[0]
    inverse = jnp.argsort(dealt_row)
    stream_block = jnp.take(arrived, inverse, axis=0).reshape(tok_dev, width)
    inner_dev = x_weight.shape[1]
    heads_dev = step_weight.shape[1]
    head_dim = inner_dev // heads_dev
    state_dim = shared_weight.shape[1] // 2
    feature_held, codes = exchange(stream_block, "fsdp", 1)
    if codes is None:
        codes = list(range(fsdp_count))
        fsdp_place = 0
    where_code = [0] * fsdp_count
    for position, code in enumerate(codes):
        where_code[code] = position
    table = jnp.asarray(where_code, jnp.int32)

    def piece_of(source, start, size):
        position = table[jnp.bitwise_xor(source, fsdp_place)]
        return lax.dynamic_slice_in_dim(feature_held, position * width + start, size, axis=1)

    feature_part = jnp.concatenate(
        [piece_of(index, 0, model_cols) for index in range(fsdp_count)], axis=1
    )
    if split_ok:
        bc_raw = jnp.concatenate(
            [
                piece_of(bit_reversed(block, fsdp_count), model_cols, quarter)
                for block in range(fsdp_count)
            ],
            axis=1,
        )
    else:
        bc_raw = jnp.dot(
            feature_part,
            lax.all_gather(shared_weight, "fsdp", axis=0, tiled=True),
            preferred_element_type=jnp.float32,
        ).astype(jnp.bfloat16)
    x_acc, z_acc, step_acc = tuple(
        (
            jnp.dot(feature_part, weight, preferred_element_type=jnp.float32)
            for weight in (x_weight, z_weight, step_weight)
        )
    )
    x_raw = x_acc.astype(jnp.bfloat16)
    z_raw = z_acc.astype(jnp.bfloat16)
    step_size = jax.nn.softplus(step_acc + step_bias[None, :])
    mixed_in = jnp.concatenate([x_raw, bc_raw], axis=1)
    conv_width = conv_heads.shape[0]
    prior_rows = shifted(mixed_in[tok_dev - conv_width + 1 :], "seq", 1)
    first_pos = own_index * tok_dev
    positions = first_pos - (conv_width - 1) + jnp.arange(tok_dev + conv_width - 1, dtype=jnp.int32)
    seg_ext = segment_of(positions, lengths)
    extended = jnp.concatenate([prior_rows, mixed_in], axis=0).astype(jnp.float32)
    activated = jax.nn.silu(
        causal_conv(
            extended, seg_ext, jnp.concatenate([conv_heads, conv_shared], axis=1), conv_width
        )
    )
    segment_ids = seg_ext[conv_width - 1 :]
    seg_before = jnp.where(own_index == 0, -1, seg_ext[conv_width - 2])
    x_heads = activated[:, :inner_dev].reshape(tok_dev, heads_dev, head_dim)
    b_rows = activated[:, inner_dev : inner_dev + state_dim]
    c_rows = activated[:, inner_dev + state_dim :]
    intra, state_out, carry_in, block_decay = local_terms(
        x_heads, b_rows, c_rows, step_size, decay_log, segment_ids, seg_before
    )
    decay_rows = jnp.broadcast_to(block_decay[:, None, None], (heads_dev, 2, state_dim))
    packed = jnp.concatenate([state_out, decay_rows], axis=1)
    local_y = intra + skip_gain[None, :, None] * x_heads
    gate = jax.nn.silu(z_raw.astype(jnp.float32)).reshape(tok_dev, heads_dev, head_dim)
    scanned, (local_y, gate, carry_in) = exclusive_scan(packed, "seq", (local_y, gate, carry_in))
    state_in = scanned[:, :head_dim, :]
    incoming = jnp.einsum("tn,hpn->thp", c_rows, state_in, precision=precise)
    y_block = local_y + carry_in[:, :, None] * incoming
    gated = (y_block * gate).reshape(tok_dev, inner_dev).astype(jnp.bfloat16)
    ordered = gated.reshape(seq_count, piece_rows, inner_dev)
    outgoing = jnp.take(ordered, dealt_row, axis=0)
    returned = lax.all_to_all(outgoing, "seq", split_axis=0, concat_axis=0, tiled=True)
    return returned.reshape(tok_dev, inner_dev)


def solution(mesh):
    return jax.shard_map(
        per_device,
        mesh=mesh,
        in_specs=(
            P("seq", "fsdp"),
            P(),
            P(),
            P(None, "fsdp"),
            P(None, "fsdp"),
            P("fsdp", None),
            P(None, "fsdp"),
            P(None, "fsdp"),
            P(),
            P("fsdp"),
            P("fsdp"),
            P("fsdp"),
        ),
        out_specs=P("seq", "fsdp"),
        check_vma=False,
    )
```

```python
import jax
import jax.numpy as jnp
from jax import lax
from jax.sharding import PartitionSpec as P

precise = lax.Precision.HIGHEST


def shifted(array, axis, by):
    count = lax.axis_size(axis)
    pairs = [(i, i + by) for i in range(count) if 0 <= i + by < count]
    return lax.ppermute(array, axis, pairs)


def combine_packed(earlier, later):
    rows = later.shape[1] - 2
    d_e, d_l = earlier[:, rows : rows + 1, :], later[:, rows : rows + 1, :]
    state = d_l * earlier[:, :rows, :] + later[:, :rows, :]
    decay = d_e * d_l
    return jnp.concatenate([state, decay, decay], axis=1)


def received(packed, axis, by):
    place = lax.axis_index(axis)
    rows = packed.shape[1] - 2
    row = lax.broadcasted_iota(jnp.int32, packed.shape, 1)
    high = packed.astype(jnp.bfloat16)
    low = (packed - high.astype(jnp.float32)).astype(jnp.bfloat16)
    wire = jnp.where(row == rows + 1, low, high)
    got = shifted(wire, axis, by).astype(jnp.float32)
    missing = (place < by).astype(jnp.float32)
    decay = got[:, rows : rows + 1, :] + got[:, rows + 1 :, :] + missing
    return jnp.concatenate([got[:, :rows, :], decay, decay], axis=1)


def exclusive_scan(packed, axis, side):
    count = lax.axis_size(axis)
    if count == 1:
        return received(packed, axis, 1), side
    held = received(packed, axis, 1)
    if count > 2:
        held = combine_packed(received(packed, axis, 2), held)
    cover = 2
    while cover < count - 1:
        if cover * 2 >= count - 1:
            held, side = lax.optimization_barrier((held, side))
        held = combine_packed(received(held, axis, cover), held)
        cover *= 2
    return held, side


def exchange(block, axis, dim):
    count = lax.axis_size(axis)
    if count & (count - 1):
        return lax.all_gather(block, axis, axis=dim, tiled=True), None
    held, codes = block, [0]
    bit = count // 2
    while bit >= 1:
        other = lax.ppermute(held, axis, [(i, i ^ bit) for i in range(count)])
        held = jnp.concatenate([held, other], axis=dim)
        codes = codes + [c ^ bit for c in codes]
        bit //= 2
    return held, codes


def to_natural(held, codes, axis, dim):
    if codes is None:
        return held
    count = len(codes)
    width = held.shape[dim] // count
    where_code = [0] * count
    for position, code in enumerate(codes):
        where_code[code] = position
    table = jnp.asarray(where_code, jnp.int32)
    place = lax.axis_index(axis)
    parts = [
        lax.dynamic_slice_in_dim(held, table[jnp.bitwise_xor(index, place)] * width, width, axis=dim)
        for index in range(count)
    ]
    return jnp.concatenate(parts, axis=dim)


def summed_columns(partial, axis):
    count = lax.axis_size(axis)
    if count & (count - 1) or partial.shape[1] % 2:
        return lax.psum(partial, axis).astype(jnp.bfloat16)
    if count == 1:
        return partial.astype(jnp.bfloat16)
    place = lax.axis_index(axis)
    half = partial.shape[1] // 2
    side = place % 2
    kept = lax.dynamic_slice_in_dim(partial, side * half, half, axis=1)
    sent = lax.dynamic_slice_in_dim(partial, (1 - side) * half, half, axis=1)
    kept = kept + lax.ppermute(sent, axis, [(i, i ^ 1) for i in range(count)])
    bit = 2
    while bit < count:
        kept = kept + lax.ppermute(kept, axis, [(i, i ^ bit) for i in range(count)])
        bit *= 2
    kept = kept.astype(jnp.bfloat16)
    other = lax.ppermute(kept, axis, [(i, i ^ 1) for i in range(count)])
    both = jnp.concatenate([kept, other], axis=1)
    return jnp.where(side == 0, both, jnp.concatenate([other, kept], axis=1))


def scattered_columns(partial, axis):
    count = lax.axis_size(axis)
    place = lax.axis_index(axis)
    bit = 1
    while bit < count:
        half = partial.shape[1] // 2
        side = (place // bit) % 2
        kept = lax.dynamic_slice_in_dim(partial, side * half, half, axis=1)
        sent = lax.dynamic_slice_in_dim(partial, (1 - side) * half, half, axis=1)
        partial = kept + lax.ppermute(sent, axis, [(i, i ^ bit) for i in range(count)])
        bit *= 2
    return partial.astype(jnp.bfloat16)


def bit_reversed(index, count):
    out, bit, top = 0, 1, count // 2
    while bit < count:
        if index & bit:
            out += top
        bit *= 2
        top //= 2
    return out


def segment_of(positions, lengths):
    prompt_ends = jnp.cumsum(lengths)
    counted = (positions[:, None] >= prompt_ends[None, :]).astype(jnp.int32)
    return jnp.sum(counted, axis=1)


def causal_conv(extended, segment_ids, weights, conv_width):
    out_rows = extended.shape[0] - conv_width + 1
    target = segment_ids[conv_width - 1 :]
    running = jnp.zeros((out_rows, extended.shape[1]), jnp.float32)
    for tap_index in range(conv_width):
        matched = (segment_ids[tap_index : tap_index + out_rows] == target).astype(jnp.float32)
        running = (
            running
            + weights[tap_index][None, :]
            * extended[tap_index : tap_index + out_rows]
            * matched[:, None]
        )
    return running


def local_terms(x_heads, b_rows, c_rows, step_size, decay_log, segment_ids, seg_before):
    log_decay = -jnp.exp(decay_log)[None, :] * step_size
    positions_in = jnp.arange(x_heads.shape[0], dtype=jnp.int32)
    lower = (positions_in[:, None] >= positions_in[None, :]).astype(jnp.float32)
    cum_decay = jnp.dot(lower, log_decay, precision=precise)
    same_prompt = (segment_ids[:, None] == segment_ids[None, :]) & (
        positions_in[:, None] >= positions_in[None, :]
    )
    decay_gap = cum_decay.T[:, :, None] - cum_decay.T[:, None, :]
    decay_matrix = jnp.exp(jnp.where(same_prompt[None], decay_gap, -jnp.inf))
    scores = jnp.dot(c_rows, b_rows.T, precision=precise)
    x_step = x_heads * step_size[:, :, None]
    intra = jnp.einsum("hts,shp->thp", scores[None] * decay_matrix, x_step, precision=precise)
    to_end = jnp.exp(
        jnp.where(
            (segment_ids == segment_ids[-1])[:, None], cum_decay[-1][None, :] - cum_decay, -jnp.inf
        )
    )
    state_out = jnp.einsum("shp,sn->hpn", x_step * to_end[:, :, None], b_rows, precision=precise)
    carried = segment_ids == seg_before
    carry_in = jnp.exp(jnp.where(carried[:, None], cum_decay, -jnp.inf))
    block_decay = jnp.where(carried[-1], jnp.exp(cum_decay[-1]), 0.0)
    return (intra, state_out, carry_in, block_decay)


def per_device(
    tokens,
    deal_order,
    lengths,
    x_weight,
    z_weight,
    shared_weight,
    step_weight,
    conv_heads,
    conv_shared,
    step_bias,
    decay_log,
    skip_gain,
):
    seq_count = lax.axis_size("seq")
    own_index = lax.axis_index("seq")
    tok_dev = tokens.shape[0]
    piece_rows = tok_dev // seq_count
    model_cols = tokens.shape[1]
    fsdp_count = lax.axis_size("fsdp")
    fsdp_place = lax.axis_index("fsdp")
    split_ok = fsdp_count & (fsdp_count - 1) == 0 and shared_weight.shape[1] % fsdp_count == 0
    if split_ok:
        bc_quarter = scattered_columns(
            jnp.dot(tokens, shared_weight, preferred_element_type=jnp.float32), "fsdp"
        )
        quarter = bc_quarter.shape[1]
        sent_rows = jnp.concatenate([tokens, bc_quarter], axis=1)
    else:
        quarter = 0
        sent_rows = tokens
    width = sent_rows.shape[1]
    conv_width = conv_heads.shape[0]
    halo = conv_width - 1
    tail = min(halo, piece_rows)
    slot_rows = sent_rows.reshape(seq_count, piece_rows, width)
    tails = jnp.roll(slot_rows[:, piece_rows - tail :, :], 1, axis=0).reshape(seq_count, tail * width)
    tail_cols = -(-tail * width // piece_rows)
    tail_pad = -(-tail_cols // 128) * 128
    tails = jnp.pad(tails, ((0, 0), (0, tail_cols * piece_rows - tail * width)))
    tails = jnp.pad(tails.reshape(seq_count, piece_rows, tail_cols), ((0, 0), (0, 0), (0, tail_pad - tail_cols)))
    arrived = lax.all_to_all(
        jnp.concatenate([slot_rows, tails], axis=2), "seq", split_axis=0, concat_axis=0, tiled=True
    )
    dealt_row = lax.dynamic_slice_in_dim(deal_order, own_index, 1, 0)[0]
    inverse = jnp.argsort(dealt_row)
    stream_block = jnp.take(arrived[:, :, :width], inverse, axis=0).reshape(tok_dev, width)
    tail_in = arrived[:, :, width : width + tail_cols].reshape(seq_count, piece_rows * tail_cols)
    tail_in = tail_in[:, : tail * width].reshape(seq_count * tail, width)
    prior_row = lax.dynamic_slice_in_dim(deal_order, (own_index + seq_count - 1) % seq_count, 1, 0)[0]
    inverse_prior = jnp.argsort(prior_row)
    block_rows = [tok_dev - halo + r for r in range(halo)]
    pieces = jnp.asarray([b // piece_rows for b in block_rows], jnp.int32)
    within = jnp.asarray([b % piece_rows - (piece_rows - tail) for b in block_rows], jnp.int32)
    halo_rows = jnp.take(tail_in, inverse_prior[pieces] * tail + within, axis=0)
    halo_rows = jnp.where(own_index > 0, halo_rows, jnp.zeros_like(halo_rows))
    halo_cols = -(-halo * width // tok_dev)
    halo_pad = -(-halo_cols // 128) * 128
    halo_flat = jnp.pad(halo_rows.reshape(halo * width), (0, halo_cols * tok_dev - halo * width))
    halo_block = jnp.pad(halo_flat.reshape(tok_dev, halo_cols), ((0, 0), (0, halo_pad - halo_cols)))
    inner_dev = x_weight.shape[1]
    heads_dev = step_weight.shape[1]
    head_dim = inner_dev // heads_dev
    state_dim = shared_weight.shape[1] // 2
    span = width + halo_pad
    feature_held, codes = exchange(jnp.concatenate([stream_block, halo_block], axis=1), "fsdp", 1)
    if codes is None:
        codes = list(range(fsdp_count))
        fsdp_place = 0
    where_code = [0] * fsdp_count
    for position, code in enumerate(codes):
        where_code[code] = position
    table = jnp.asarray(where_code, jnp.int32)

    def piece_of(source, start, size):
        position = table[jnp.bitwise_xor(source, fsdp_place)]
        return lax.dynamic_slice_in_dim(feature_held, position * span + start, size, axis=1)

    def halo_of(source):
        cols = piece_of(source, width, halo_cols).reshape(tok_dev * halo_cols)
        return cols[: halo * width].reshape(halo, width)

    feature_part = jnp.concatenate(
        [piece_of(index, 0, model_cols) for index in range(fsdp_count)], axis=1
    )
    halo_parts = [halo_of(index) for index in range(fsdp_count)]
    halo_features = jnp.concatenate([part[:, :model_cols] for part in halo_parts], axis=1)
    if split_ok:
        bc_raw = jnp.concatenate(
            [
                piece_of(bit_reversed(block, fsdp_count), model_cols, quarter)
                for block in range(fsdp_count)
            ],
            axis=1,
        )
        halo_bc = jnp.concatenate(
            [halo_parts[bit_reversed(block, fsdp_count)][:, model_cols:] for block in range(fsdp_count)],
            axis=1,
        )
    else:
        w_full = lax.all_gather(shared_weight, "fsdp", axis=0, tiled=True)
        bc_raw = jnp.dot(feature_part, w_full, preferred_element_type=jnp.float32).astype(jnp.bfloat16)
        halo_bc = jnp.dot(halo_features, w_full, preferred_element_type=jnp.float32).astype(jnp.bfloat16)
    halo_x = jnp.dot(halo_features, x_weight, preferred_element_type=jnp.float32).astype(jnp.bfloat16)
    prior_rows = jnp.concatenate([halo_x, halo_bc], axis=1)
    x_acc, z_acc, step_acc = tuple(
        (
            jnp.dot(feature_part, weight, preferred_element_type=jnp.float32)
            for weight in (x_weight, z_weight, step_weight)
        )
    )
    x_raw = x_acc.astype(jnp.bfloat16)
    z_raw = z_acc.astype(jnp.bfloat16)
    step_size = jax.nn.softplus(step_acc + step_bias[None, :])
    mixed_in = jnp.concatenate([x_raw, bc_raw], axis=1)
    first_pos = own_index * tok_dev
    positions = first_pos - (conv_width - 1) + jnp.arange(tok_dev + conv_width - 1, dtype=jnp.int32)
    seg_ext = segment_of(positions, lengths)
    extended = jnp.concatenate([prior_rows, mixed_in], axis=0).astype(jnp.float32)
    activated = jax.nn.silu(
        causal_conv(
            extended, seg_ext, jnp.concatenate([conv_heads, conv_shared], axis=1), conv_width
        )
    )
    segment_ids = seg_ext[conv_width - 1 :]
    seg_before = jnp.where(own_index == 0, -1, seg_ext[conv_width - 2])
    x_heads = activated[:, :inner_dev].reshape(tok_dev, heads_dev, head_dim)
    b_rows = activated[:, inner_dev : inner_dev + state_dim]
    c_rows = activated[:, inner_dev + state_dim :]
    intra, state_out, carry_in, block_decay = local_terms(
        x_heads, b_rows, c_rows, step_size, decay_log, segment_ids, seg_before
    )
    decay_rows = jnp.broadcast_to(block_decay[:, None, None], (heads_dev, 2, state_dim))
    packed = jnp.concatenate([state_out, decay_rows], axis=1)
    local_y = intra + skip_gain[None, :, None] * x_heads
    gate = jax.nn.silu(z_raw.astype(jnp.float32)).reshape(tok_dev, heads_dev, head_dim)
    scanned, (local_y, gate, carry_in) = exclusive_scan(packed, "seq", (local_y, gate, carry_in))
    state_in = scanned[:, :head_dim, :]
    incoming = jnp.einsum("tn,hpn->thp", c_rows, state_in, precision=precise)
    y_block = local_y + carry_in[:, :, None] * incoming
    gated = (y_block * gate).reshape(tok_dev, inner_dev).astype(jnp.bfloat16)
    ordered = gated.reshape(seq_count, piece_rows, inner_dev)
    outgoing = jnp.take(ordered, dealt_row, axis=0)
    returned = lax.all_to_all(outgoing, "seq", split_axis=0, concat_axis=0, tiled=True)
    return returned.reshape(tok_dev, inner_dev)


def solution(mesh):
    return jax.shard_map(
        per_device,
        mesh=mesh,
        in_specs=(
            P("seq", "fsdp"),
            P(),
            P(),
            P(None, "fsdp"),
            P(None, "fsdp"),
            P("fsdp", None),
            P(None, "fsdp"),
            P(None, "fsdp"),
            P(),
            P("fsdp"),
            P("fsdp"),
            P("fsdp"),
        ),
        out_specs=P("seq", "fsdp"),
        check_vma=False,
    )
```

```python
import jax
import jax.numpy as jnp
from jax import lax
from jax.sharding import PartitionSpec as P

precise = lax.Precision.HIGHEST


def shifted(array, axis, by):
    count = lax.axis_size(axis)
    pairs = [(i, i + by) for i in range(count) if 0 <= i + by < count]
    return lax.ppermute(array, axis, pairs)


def combine_packed(earlier, later, heads):
    extra = -(-2 * heads // 16) * 16
    rows = later.shape[0] - extra
    d_e = earlier[rows : rows + heads]
    d_l = later[rows : rows + heads]
    head_dim = rows // heads
    state = d_l[:, None, :] * earlier[:rows].reshape(heads, head_dim, -1) + later[:rows].reshape(heads, head_dim, -1)
    decay = d_e * d_l
    spare = jnp.zeros((extra - 2 * heads, later.shape[1]), later.dtype)
    return jnp.concatenate([state.reshape(rows, -1), decay, decay, spare], axis=0)


def received(packed, axis, by, heads):
    place = lax.axis_index(axis)
    extra = -(-2 * heads // 16) * 16
    rows = packed.shape[0] - extra
    row = lax.broadcasted_iota(jnp.int32, packed.shape, 0)
    high = packed.astype(jnp.bfloat16)
    low = (packed - high.astype(jnp.float32)).astype(jnp.bfloat16)
    wire = jnp.where((row >= rows + heads) & (row < rows + 2 * heads), low, high)
    got = shifted(wire, axis, by).astype(jnp.float32)
    missing = (place < by).astype(jnp.float32)
    decay = got[rows : rows + heads] + got[rows + heads : rows + 2 * heads] + missing
    spare = jnp.zeros((extra - 2 * heads, packed.shape[1]), packed.dtype)
    return jnp.concatenate([got[:rows], decay, decay, spare], axis=0)


def exclusive_scan(packed, axis, side, heads):
    count = lax.axis_size(axis)
    if count == 1:
        return received(packed, axis, 1, heads), side
    held = received(packed, axis, 1, heads)
    if count > 2:
        held = combine_packed(received(packed, axis, 2, heads), held, heads)
    cover = 2
    while cover < count - 1:
        if cover * 2 >= count - 1:
            held, side = lax.optimization_barrier((held, side))
        held = combine_packed(received(held, axis, cover, heads), held, heads)
        cover *= 2
    return held, side


def exchange(block, axis, dim):
    count = lax.axis_size(axis)
    if count & (count - 1):
        return lax.all_gather(block, axis, axis=dim, tiled=True), None
    held, codes = block, [0]
    bit = count // 2
    while bit >= 1:
        other = lax.ppermute(held, axis, [(i, i ^ bit) for i in range(count)])
        held = jnp.concatenate([held, other], axis=dim)
        codes = codes + [c ^ bit for c in codes]
        bit //= 2
    return held, codes


def to_natural(held, codes, axis, dim):
    if codes is None:
        return held
    count = len(codes)
    width = held.shape[dim] // count
    where_code = [0] * count
    for position, code in enumerate(codes):
        where_code[code] = position
    table = jnp.asarray(where_code, jnp.int32)
    place = lax.axis_index(axis)
    parts = [
        lax.dynamic_slice_in_dim(held, table[jnp.bitwise_xor(index, place)] * width, width, axis=dim)
        for index in range(count)
    ]
    return jnp.concatenate(parts, axis=dim)


def summed_columns(partial, axis):
    count = lax.axis_size(axis)
    if count & (count - 1) or partial.shape[1] % 2:
        return lax.psum(partial, axis).astype(jnp.bfloat16)
    if count == 1:
        return partial.astype(jnp.bfloat16)
    place = lax.axis_index(axis)
    half = partial.shape[1] // 2
    side = place % 2
    kept = lax.dynamic_slice_in_dim(partial, side * half, half, axis=1)
    sent = lax.dynamic_slice_in_dim(partial, (1 - side) * half, half, axis=1)
    kept = kept + lax.ppermute(sent, axis, [(i, i ^ 1) for i in range(count)])
    bit = 2
    while bit < count:
        kept = kept + lax.ppermute(kept, axis, [(i, i ^ bit) for i in range(count)])
        bit *= 2
    kept = kept.astype(jnp.bfloat16)
    other = lax.ppermute(kept, axis, [(i, i ^ 1) for i in range(count)])
    both = jnp.concatenate([kept, other], axis=1)
    return jnp.where(side == 0, both, jnp.concatenate([other, kept], axis=1))


def segment_of(positions, lengths):
    prompt_ends = jnp.cumsum(lengths)
    counted = (positions[:, None] >= prompt_ends[None, :]).astype(jnp.int32)
    return jnp.sum(counted, axis=1)


def causal_conv(extended, segment_ids, weights, conv_width):
    out_rows = extended.shape[0] - conv_width + 1
    target = segment_ids[conv_width - 1 :]
    running = jnp.zeros((out_rows, extended.shape[1]), jnp.float32)
    for tap_index in range(conv_width):
        matched = (segment_ids[tap_index : tap_index + out_rows] == target).astype(jnp.float32)
        running = (
            running
            + weights[tap_index][None, :]
            * extended[tap_index : tap_index + out_rows]
            * matched[:, None]
        )
    return running


def local_terms(x_heads, b_rows, c_rows, step_size, decay_log, segment_ids, seg_before):
    log_decay = -jnp.exp(decay_log)[None, :] * step_size
    positions_in = jnp.arange(x_heads.shape[0], dtype=jnp.int32)
    lower = (positions_in[:, None] >= positions_in[None, :]).astype(jnp.float32)
    cum_decay = jnp.dot(lower, log_decay, precision=precise)
    same_prompt = (segment_ids[:, None] == segment_ids[None, :]) & (
        positions_in[:, None] >= positions_in[None, :]
    )
    decay_gap = cum_decay.T[:, :, None] - cum_decay.T[:, None, :]
    decay_matrix = jnp.exp(jnp.where(same_prompt[None], decay_gap, -jnp.inf))
    scores = jnp.dot(c_rows, b_rows.T, precision=precise)
    x_step = x_heads * step_size[:, :, None]
    intra = jnp.einsum("hts,shp->thp", scores[None] * decay_matrix, x_step, precision=precise)
    to_end = jnp.exp(
        jnp.where(
            (segment_ids == segment_ids[-1])[:, None], cum_decay[-1][None, :] - cum_decay, -jnp.inf
        )
    )
    state_out = jnp.einsum("shp,sn->hpn", x_step * to_end[:, :, None], b_rows, precision=precise)
    carried = segment_ids == seg_before
    carry_in = jnp.exp(jnp.where(carried[:, None], cum_decay, -jnp.inf))
    block_decay = jnp.where(carried[-1], jnp.exp(cum_decay[-1]), 0.0)
    return (intra, state_out, carry_in, block_decay)


def per_device(
    tokens,
    deal_order,
    lengths,
    x_weight,
    z_weight,
    shared_weight,
    step_weight,
    conv_heads,
    conv_shared,
    step_bias,
    decay_log,
    skip_gain,
):
    seq_count = lax.axis_size("seq")
    own_index = lax.axis_index("seq")
    tok_dev = tokens.shape[0]
    piece_rows = tok_dev // seq_count
    slot_rows = tokens.reshape(seq_count, piece_rows, tokens.shape[1])
    arrived = lax.all_to_all(slot_rows, "seq", split_axis=0, concat_axis=0, tiled=True)
    dealt_row = lax.dynamic_slice_in_dim(deal_order, own_index, 1, 0)[0]
    inverse = jnp.argsort(dealt_row)
    stream_block = jnp.take(arrived, inverse, axis=0).reshape(tok_dev, tokens.shape[1])
    inner_dev = x_weight.shape[1]
    heads_dev = step_weight.shape[1]
    head_dim = inner_dev // heads_dev
    state_dim = shared_weight.shape[1] // 2
    bc_partial = jnp.dot(stream_block, shared_weight, preferred_element_type=jnp.float32)
    bc_raw = summed_columns(bc_partial, "fsdp")
    feature_held, codes = exchange(stream_block, "fsdp", 1)
    feature_part = to_natural(feature_held, codes, "fsdp", 1)
    x_acc, z_acc, step_acc = tuple(
        (
            jnp.dot(feature_part, weight, preferred_element_type=jnp.float32)
            for weight in (x_weight, z_weight, step_weight)
        )
    )
    x_raw = x_acc.astype(jnp.bfloat16)
    z_raw = z_acc.astype(jnp.bfloat16)
    step_size = jax.nn.softplus(step_acc + step_bias[None, :])
    mixed_in = jnp.concatenate([x_raw, bc_raw], axis=1)
    conv_width = conv_heads.shape[0]
    prior_rows = shifted(mixed_in[tok_dev - conv_width + 1 :], "seq", 1)
    first_pos = own_index * tok_dev
    positions = first_pos - (conv_width - 1) + jnp.arange(tok_dev + conv_width - 1, dtype=jnp.int32)
    seg_ext = segment_of(positions, lengths)
    extended = jnp.concatenate([prior_rows, mixed_in], axis=0).astype(jnp.float32)
    activated = jax.nn.silu(
        causal_conv(
            extended, seg_ext, jnp.concatenate([conv_heads, conv_shared], axis=1), conv_width
        )
    )
    segment_ids = seg_ext[conv_width - 1 :]
    seg_before = jnp.where(own_index == 0, -1, seg_ext[conv_width - 2])
    x_heads = activated[:, :inner_dev].reshape(tok_dev, heads_dev, head_dim)
    b_rows = activated[:, inner_dev : inner_dev + state_dim]
    c_rows = activated[:, inner_dev + state_dim :]
    intra, state_out, carry_in, block_decay = local_terms(
        x_heads, b_rows, c_rows, step_size, decay_log, segment_ids, seg_before
    )
    decay_rows = jnp.broadcast_to(block_decay[:, None], (heads_dev, state_dim))
    spare = jnp.zeros((-(-2 * heads_dev // 16) * 16 - 2 * heads_dev, state_dim), jnp.float32)
    packed = jnp.concatenate(
        [state_out.reshape(heads_dev * head_dim, state_dim), decay_rows, decay_rows, spare], axis=0
    )
    gate = jax.nn.silu(z_raw.astype(jnp.float32)).reshape(tok_dev, heads_dev, head_dim)
    local_gated = (intra + skip_gain[None, :, None] * x_heads) * gate
    carry_gated = carry_in[:, :, None] * gate

    def dealt(rows):
        return jnp.take(rows.reshape((seq_count, piece_rows) + rows.shape[1:]), dealt_row, axis=0).reshape(
            rows.shape
        )

    side = (dealt(local_gated), dealt(carry_gated), dealt(c_rows))
    scanned, (local_gated, carry_gated, c_dealt) = exclusive_scan(packed, "seq", side, heads_dev)
    state_in = scanned[: heads_dev * head_dim].reshape(heads_dev, head_dim, state_dim)
    incoming = jnp.einsum("tn,hpn->thp", c_dealt, state_in, precision=precise)
    outgoing = (local_gated + carry_gated * incoming).astype(jnp.bfloat16).reshape(
        seq_count, piece_rows, inner_dev
    )
    returned = lax.all_to_all(outgoing, "seq", split_axis=0, concat_axis=0, tiled=True)
    return returned.reshape(tok_dev, inner_dev)


def solution(mesh):
    return jax.shard_map(
        per_device,
        mesh=mesh,
        in_specs=(
            P("seq", "fsdp"),
            P(),
            P(),
            P(None, "fsdp"),
            P(None, "fsdp"),
            P("fsdp", None),
            P(None, "fsdp"),
            P(None, "fsdp"),
            P(),
            P("fsdp"),
            P("fsdp"),
            P("fsdp"),
        ),
        out_specs=P("seq", "fsdp"),
        check_vma=False,
    )
```

```python
import jax
import jax.numpy as jnp
from jax import lax
from jax.sharding import PartitionSpec as P

precise = lax.Precision.HIGHEST


def shifted(array, axis, by):
    count = lax.axis_size(axis)
    pairs = [(i, i + by) for i in range(count) if 0 <= i + by < count]
    return lax.ppermute(array, axis, pairs)


def combine_packed(earlier, later, heads):
    extra = -(-2 * heads // 16) * 16
    rows = later.shape[0] - extra
    d_e = earlier[rows : rows + heads]
    d_l = later[rows : rows + heads]
    head_dim = rows // heads
    state = d_l[:, None, :] * earlier[:rows].reshape(heads, head_dim, -1) + later[:rows].reshape(heads, head_dim, -1)
    decay = d_e * d_l
    spare = jnp.zeros((extra - 2 * heads, later.shape[1]), later.dtype)
    return jnp.concatenate([state.reshape(rows, -1), decay, decay, spare], axis=0)


def received(packed, axis, by, heads):
    place = lax.axis_index(axis)
    extra = -(-2 * heads // 16) * 16
    rows = packed.shape[0] - extra
    row = lax.broadcasted_iota(jnp.int32, packed.shape, 0)
    high = packed.astype(jnp.bfloat16)
    low = (packed - high.astype(jnp.float32)).astype(jnp.bfloat16)
    wire = jnp.where((row >= rows + heads) & (row < rows + 2 * heads), low, high)
    got = shifted(wire, axis, by).astype(jnp.float32)
    missing = (place < by).astype(jnp.float32)
    decay = got[rows : rows + heads] + got[rows + heads : rows + 2 * heads] + missing
    spare = jnp.zeros((extra - 2 * heads, packed.shape[1]), packed.dtype)
    return jnp.concatenate([got[:rows], decay, decay, spare], axis=0)


def exclusive_scan(packed, axis, side, heads):
    count = lax.axis_size(axis)
    if count == 1:
        return received(packed, axis, 1, heads), side
    held = received(packed, axis, 1, heads)
    if count > 2:
        held = combine_packed(received(packed, axis, 2, heads), held, heads)
    cover = 2
    while cover < count - 1:
        if cover * 2 >= count - 1:
            held, side = lax.optimization_barrier((held, side))
        held = combine_packed(received(held, axis, cover, heads), held, heads)
        cover *= 2
    return held, side


def exchange(block, axis, dim):
    count = lax.axis_size(axis)
    if count & (count - 1):
        return lax.all_gather(block, axis, axis=dim, tiled=True), None
    held, codes = block, [0]
    bit = count // 2
    while bit >= 1:
        other = lax.ppermute(held, axis, [(i, i ^ bit) for i in range(count)])
        held = jnp.concatenate([held, other], axis=dim)
        codes = codes + [c ^ bit for c in codes]
        bit //= 2
    return held, codes


def to_natural(held, codes, axis, dim):
    if codes is None:
        return held
    count = len(codes)
    width = held.shape[dim] // count
    where_code = [0] * count
    for position, code in enumerate(codes):
        where_code[code] = position
    table = jnp.asarray(where_code, jnp.int32)
    place = lax.axis_index(axis)
    parts = [
        lax.dynamic_slice_in_dim(held, table[jnp.bitwise_xor(index, place)] * width, width, axis=dim)
        for index in range(count)
    ]
    return jnp.concatenate(parts, axis=dim)


def summed_columns(partial, axis):
    count = lax.axis_size(axis)
    if count & (count - 1) or partial.shape[1] % 2:
        return lax.psum(partial, axis).astype(jnp.bfloat16)
    if count == 1:
        return partial.astype(jnp.bfloat16)
    place = lax.axis_index(axis)
    half = partial.shape[1] // 2
    side = place % 2
    kept = lax.dynamic_slice_in_dim(partial, side * half, half, axis=1)
    sent = lax.dynamic_slice_in_dim(partial, (1 - side) * half, half, axis=1)
    kept = kept + lax.ppermute(sent, axis, [(i, i ^ 1) for i in range(count)])
    bit = 2
    while bit < count:
        kept = kept + lax.ppermute(kept, axis, [(i, i ^ bit) for i in range(count)])
        bit *= 2
    kept = kept.astype(jnp.bfloat16)
    other = lax.ppermute(kept, axis, [(i, i ^ 1) for i in range(count)])
    both = jnp.concatenate([kept, other], axis=1)
    return jnp.where(side == 0, both, jnp.concatenate([other, kept], axis=1))


def segment_of(positions, lengths):
    prompt_ends = jnp.cumsum(lengths)
    counted = (positions[:, None] >= prompt_ends[None, :]).astype(jnp.int32)
    return jnp.sum(counted, axis=1)


def causal_conv(extended, segment_ids, weights, conv_width):
    out_rows = extended.shape[0] - conv_width + 1
    target = segment_ids[conv_width - 1 :]
    running = jnp.zeros((out_rows, extended.shape[1]), jnp.float32)
    for tap_index in range(conv_width):
        matched = (segment_ids[tap_index : tap_index + out_rows] == target).astype(jnp.float32)
        running = (
            running
            + weights[tap_index][None, :]
            * extended[tap_index : tap_index + out_rows]
            * matched[:, None]
        )
    return running


def local_terms(x_heads, b_rows, c_rows, step_size, decay_log, segment_ids, seg_before):
    log_decay = -jnp.exp(decay_log)[None, :] * step_size
    positions_in = jnp.arange(x_heads.shape[0], dtype=jnp.int32)
    lower = (positions_in[:, None] >= positions_in[None, :]).astype(jnp.float32)
    cum_decay = jnp.dot(lower, log_decay, precision=precise)
    same_prompt = (segment_ids[:, None] == segment_ids[None, :]) & (
        positions_in[:, None] >= positions_in[None, :]
    )
    decay_gap = cum_decay.T[:, :, None] - cum_decay.T[:, None, :]
    decay_matrix = jnp.exp(jnp.where(same_prompt[None], decay_gap, -jnp.inf))
    scores = jnp.dot(c_rows, b_rows.T, precision=precise)
    x_step = x_heads * step_size[:, :, None]
    intra = jnp.einsum("hts,shp->thp", scores[None] * decay_matrix, x_step, precision=precise)
    to_end = jnp.exp(
        jnp.where(
            (segment_ids == segment_ids[-1])[:, None], cum_decay[-1][None, :] - cum_decay, -jnp.inf
        )
    )
    state_out = jnp.einsum("shp,sn->hpn", x_step * to_end[:, :, None], b_rows, precision=precise)
    carried = segment_ids == seg_before
    carry_in = jnp.exp(jnp.where(carried[:, None], cum_decay, -jnp.inf))
    block_decay = jnp.where(carried[-1], jnp.exp(cum_decay[-1]), 0.0)
    return (intra, state_out, carry_in, block_decay)


def per_device(
    tokens,
    deal_order,
    lengths,
    x_weight,
    z_weight,
    shared_weight,
    step_weight,
    conv_heads,
    conv_shared,
    step_bias,
    decay_log,
    skip_gain,
):
    seq_count = lax.axis_size("seq")
    own_index = lax.axis_index("seq")
    tok_dev = tokens.shape[0]
    piece_rows = tok_dev // seq_count
    slot_rows = tokens.reshape(seq_count, piece_rows, tokens.shape[1])
    arrived = lax.all_to_all(slot_rows, "seq", split_axis=0, concat_axis=0, tiled=True)
    dealt_row = lax.dynamic_slice_in_dim(deal_order, own_index, 1, 0)[0]
    inverse = jnp.argsort(dealt_row)
    stream_block = jnp.take(arrived, inverse, axis=0).reshape(tok_dev, tokens.shape[1])
    inner_dev = x_weight.shape[1]
    heads_dev = step_weight.shape[1]
    head_dim = inner_dev // heads_dev
    state_dim = shared_weight.shape[1] // 2
    bc_partial = jnp.dot(stream_block, shared_weight, preferred_element_type=jnp.float32)
    bc_raw = summed_columns(bc_partial, "fsdp")
    feature_held, codes = exchange(stream_block, "fsdp", 1)
    feature_part = to_natural(feature_held, codes, "fsdp", 1)
    x_acc, z_acc, step_acc = tuple(
        (
            jnp.dot(feature_part, weight, preferred_element_type=jnp.float32)
            for weight in (x_weight, z_weight, step_weight)
        )
    )
    x_raw = x_acc.astype(jnp.bfloat16)
    z_raw = z_acc.astype(jnp.bfloat16)
    step_size = jax.nn.softplus(step_acc + step_bias[None, :])
    mixed_in = jnp.concatenate([x_raw, bc_raw], axis=1)
    conv_width = conv_heads.shape[0]
    prior_rows = shifted(mixed_in[tok_dev - conv_width + 1 :], "seq", 1)
    first_pos = own_index * tok_dev
    positions = first_pos - (conv_width - 1) + jnp.arange(tok_dev + conv_width - 1, dtype=jnp.int32)
    seg_ext = segment_of(positions, lengths)
    extended = jnp.concatenate([prior_rows, mixed_in], axis=0).astype(jnp.float32)
    activated = jax.nn.silu(
        causal_conv(
            extended, seg_ext, jnp.concatenate([conv_heads, conv_shared], axis=1), conv_width
        )
    )
    segment_ids = seg_ext[conv_width - 1 :]
    seg_before = jnp.where(own_index == 0, -1, seg_ext[conv_width - 2])
    x_heads = activated[:, :inner_dev].reshape(tok_dev, heads_dev, head_dim)
    b_rows = activated[:, inner_dev : inner_dev + state_dim]
    c_rows = activated[:, inner_dev + state_dim :]
    intra, state_out, carry_in, block_decay = local_terms(
        x_heads, b_rows, c_rows, step_size, decay_log, segment_ids, seg_before
    )
    decay_rows = jnp.broadcast_to(block_decay[:, None], (heads_dev, state_dim))
    spare = jnp.zeros((-(-2 * heads_dev // 16) * 16 - 2 * heads_dev, state_dim), jnp.float32)
    packed = jnp.concatenate(
        [state_out.reshape(heads_dev * head_dim, state_dim), decay_rows, decay_rows, spare], axis=0
    )
    local_y = intra + skip_gain[None, :, None] * x_heads
    gate = jax.nn.silu(z_raw.astype(jnp.float32)).reshape(tok_dev, heads_dev, head_dim)
    scanned, (local_y, gate, carry_in) = exclusive_scan(packed, "seq", (local_y, gate, carry_in), heads_dev)
    state_in = scanned[: heads_dev * head_dim].reshape(heads_dev, head_dim, state_dim)
    incoming = jnp.einsum("tn,hpn->thp", c_rows, state_in, precision=precise)
    y_block = local_y + carry_in[:, :, None] * incoming
    gated = (y_block * gate).reshape(tok_dev, inner_dev).astype(jnp.bfloat16)
    ordered = gated.reshape(seq_count, piece_rows, inner_dev)
    outgoing = jnp.take(ordered, dealt_row, axis=0)
    returned = lax.all_to_all(outgoing, "seq", split_axis=0, concat_axis=0, tiled=True)
    return returned.reshape(tok_dev, inner_dev)


def solution(mesh):
    return jax.shard_map(
        per_device,
        mesh=mesh,
        in_specs=(
            P("seq", "fsdp"),
            P(),
            P(),
            P(None, "fsdp"),
            P(None, "fsdp"),
            P("fsdp", None),
            P(None, "fsdp"),
            P(None, "fsdp"),
            P(),
            P("fsdp"),
            P("fsdp"),
            P("fsdp"),
        ),
        out_specs=P("seq", "fsdp"),
        check_vma=False,
    )
```

```python
import jax
import jax.numpy as jnp
from jax import lax
from jax.sharding import PartitionSpec as P

precise = lax.Precision.HIGHEST


def shifted(array, axis, by):
    count = lax.axis_size(axis)
    pairs = [(i, i + by) for i in range(count) if 0 <= i + by < count]
    return lax.ppermute(array, axis, pairs)


def combine_packed(earlier, later, heads):
    extra = -(-2 * heads // 16) * 16
    rows = later.shape[0] - extra
    d_e = earlier[rows : rows + heads]
    d_l = later[rows : rows + heads]
    head_dim = rows // heads
    state = d_l[:, None, :] * earlier[:rows].reshape(heads, head_dim, -1) + later[:rows].reshape(heads, head_dim, -1)
    decay = d_e * d_l
    spare = jnp.zeros((extra - 2 * heads, later.shape[1]), later.dtype)
    return jnp.concatenate([state.reshape(rows, -1), decay, decay, spare], axis=0)


def received(packed, axis, by, heads):
    place = lax.axis_index(axis)
    extra = -(-2 * heads // 16) * 16
    rows = packed.shape[0] - extra
    row = lax.broadcasted_iota(jnp.int32, packed.shape, 0)
    high = packed.astype(jnp.bfloat16)
    low = (packed - high.astype(jnp.float32)).astype(jnp.bfloat16)
    wire = jnp.where((row >= rows + heads) & (row < rows + 2 * heads), low, high)
    got = shifted(wire, axis, by).astype(jnp.float32)
    missing = (place < by).astype(jnp.float32)
    decay = got[rows : rows + heads] + got[rows + heads : rows + 2 * heads] + missing
    spare = jnp.zeros((extra - 2 * heads, packed.shape[1]), packed.dtype)
    return jnp.concatenate([got[:rows], decay, decay, spare], axis=0)


def exclusive_scan(packed, axis, side, heads):
    count = lax.axis_size(axis)
    if count == 1:
        return received(packed, axis, 1, heads), side
    held = received(packed, axis, 1, heads)
    if count > 2:
        held = combine_packed(received(packed, axis, 2, heads), held, heads)
    cover = 2
    while cover < count - 1:
        if cover * 2 >= count - 1:
            held, side = lax.optimization_barrier((held, side))
        held = combine_packed(received(held, axis, cover, heads), held, heads)
        cover *= 2
    return held, side


def exchange(block, axis, dim):
    count = lax.axis_size(axis)
    if count & (count - 1):
        return lax.all_gather(block, axis, axis=dim, tiled=True), None
    held, codes = block, [0]
    bit = count // 2
    while bit >= 1:
        other = lax.ppermute(held, axis, [(i, i ^ bit) for i in range(count)])
        held = jnp.concatenate([held, other], axis=dim)
        codes = codes + [c ^ bit for c in codes]
        bit //= 2
    return held, codes


def to_natural(held, codes, axis, dim):
    if codes is None:
        return held
    count = len(codes)
    width = held.shape[dim] // count
    where_code = [0] * count
    for position, code in enumerate(codes):
        where_code[code] = position
    table = jnp.asarray(where_code, jnp.int32)
    place = lax.axis_index(axis)
    parts = [
        lax.dynamic_slice_in_dim(held, table[jnp.bitwise_xor(index, place)] * width, width, axis=dim)
        for index in range(count)
    ]
    return jnp.concatenate(parts, axis=dim)


def summed_columns(partial, axis):
    count = lax.axis_size(axis)
    if count & (count - 1) or partial.shape[1] % 2:
        return lax.psum(partial, axis).astype(jnp.bfloat16)
    if count == 1:
        return partial.astype(jnp.bfloat16)
    place = lax.axis_index(axis)
    half = partial.shape[1] // 2
    side = place % 2
    kept = lax.dynamic_slice_in_dim(partial, side * half, half, axis=1)
    sent = lax.dynamic_slice_in_dim(partial, (1 - side) * half, half, axis=1)
    kept = kept + lax.ppermute(sent, axis, [(i, i ^ 1) for i in range(count)])
    bit = 2
    while bit < count:
        crossed = lax.ppermute(kept.astype(jnp.bfloat16), axis, [(i, i ^ bit) for i in range(count)])
        kept = kept + crossed.astype(jnp.float32)
        bit *= 2
    kept = kept.astype(jnp.bfloat16)
    other = lax.ppermute(kept, axis, [(i, i ^ 1) for i in range(count)])
    both = jnp.concatenate([kept, other], axis=1)
    return jnp.where(side == 0, both, jnp.concatenate([other, kept], axis=1))


def segment_of(positions, lengths):
    prompt_ends = jnp.cumsum(lengths)
    counted = (positions[:, None] >= prompt_ends[None, :]).astype(jnp.int32)
    return jnp.sum(counted, axis=1)


def causal_conv(extended, segment_ids, weights, conv_width):
    out_rows = extended.shape[0] - conv_width + 1
    target = segment_ids[conv_width - 1 :]
    running = jnp.zeros((out_rows, extended.shape[1]), jnp.float32)
    for tap_index in range(conv_width):
        matched = (segment_ids[tap_index : tap_index + out_rows] == target).astype(jnp.float32)
        running = (
            running
            + weights[tap_index][None, :]
            * extended[tap_index : tap_index + out_rows]
            * matched[:, None]
        )
    return running


def local_terms(x_heads, b_rows, c_rows, step_size, decay_log, segment_ids, seg_before):
    log_decay = -jnp.exp(decay_log)[None, :] * step_size
    positions_in = jnp.arange(x_heads.shape[0], dtype=jnp.int32)
    lower = (positions_in[:, None] >= positions_in[None, :]).astype(jnp.float32)
    cum_decay = jnp.dot(lower, log_decay, precision=precise)
    same_prompt = (segment_ids[:, None] == segment_ids[None, :]) & (
        positions_in[:, None] >= positions_in[None, :]
    )
    decay_gap = cum_decay.T[:, :, None] - cum_decay.T[:, None, :]
    decay_matrix = jnp.exp(jnp.where(same_prompt[None], decay_gap, -jnp.inf))
    scores = jnp.dot(c_rows, b_rows.T, precision=precise)
    x_step = x_heads * step_size[:, :, None]
    intra = jnp.einsum("hts,shp->thp", scores[None] * decay_matrix, x_step, precision=precise)
    to_end = jnp.exp(
        jnp.where(
            (segment_ids == segment_ids[-1])[:, None], cum_decay[-1][None, :] - cum_decay, -jnp.inf
        )
    )
    state_out = jnp.einsum("shp,sn->hpn", x_step * to_end[:, :, None], b_rows, precision=precise)
    carried = segment_ids == seg_before
    carry_in = jnp.exp(jnp.where(carried[:, None], cum_decay, -jnp.inf))
    block_decay = jnp.where(carried[-1], jnp.exp(cum_decay[-1]), 0.0)
    return (intra, state_out, carry_in, block_decay)


def per_device(
    tokens,
    deal_order,
    lengths,
    x_weight,
    z_weight,
    shared_weight,
    step_weight,
    conv_heads,
    conv_shared,
    step_bias,
    decay_log,
    skip_gain,
):
    seq_count = lax.axis_size("seq")
    own_index = lax.axis_index("seq")
    tok_dev = tokens.shape[0]
    piece_rows = tok_dev // seq_count
    slot_rows = tokens.reshape(seq_count, piece_rows, tokens.shape[1])
    arrived = lax.all_to_all(slot_rows, "seq", split_axis=0, concat_axis=0, tiled=True)
    dealt_row = lax.dynamic_slice_in_dim(deal_order, own_index, 1, 0)[0]
    inverse = jnp.argsort(dealt_row)
    stream_block = jnp.take(arrived, inverse, axis=0).reshape(tok_dev, tokens.shape[1])
    inner_dev = x_weight.shape[1]
    heads_dev = step_weight.shape[1]
    head_dim = inner_dev // heads_dev
    state_dim = shared_weight.shape[1] // 2
    bc_partial = jnp.dot(stream_block, shared_weight, preferred_element_type=jnp.float32)
    bc_raw = summed_columns(bc_partial, "fsdp")
    feature_held, codes = exchange(stream_block, "fsdp", 1)
    feature_part = to_natural(feature_held, codes, "fsdp", 1)
    x_acc, z_acc, step_acc = tuple(
        (
            jnp.dot(feature_part, weight, preferred_element_type=jnp.float32)
            for weight in (x_weight, z_weight, step_weight)
        )
    )
    x_raw = x_acc.astype(jnp.bfloat16)
    z_raw = z_acc.astype(jnp.bfloat16)
    step_size = jax.nn.softplus(step_acc + step_bias[None, :])
    mixed_in = jnp.concatenate([x_raw, bc_raw], axis=1)
    conv_width = conv_heads.shape[0]
    prior_rows = shifted(mixed_in[tok_dev - conv_width + 1 :], "seq", 1)
    first_pos = own_index * tok_dev
    positions = first_pos - (conv_width - 1) + jnp.arange(tok_dev + conv_width - 1, dtype=jnp.int32)
    seg_ext = segment_of(positions, lengths)
    extended = jnp.concatenate([prior_rows, mixed_in], axis=0).astype(jnp.float32)
    activated = jax.nn.silu(
        causal_conv(
            extended, seg_ext, jnp.concatenate([conv_heads, conv_shared], axis=1), conv_width
        )
    )
    segment_ids = seg_ext[conv_width - 1 :]
    seg_before = jnp.where(own_index == 0, -1, seg_ext[conv_width - 2])
    x_heads = activated[:, :inner_dev].reshape(tok_dev, heads_dev, head_dim)
    b_rows = activated[:, inner_dev : inner_dev + state_dim]
    c_rows = activated[:, inner_dev + state_dim :]
    intra, state_out, carry_in, block_decay = local_terms(
        x_heads, b_rows, c_rows, step_size, decay_log, segment_ids, seg_before
    )
    decay_rows = jnp.broadcast_to(block_decay[:, None], (heads_dev, state_dim))
    spare = jnp.zeros((-(-2 * heads_dev // 16) * 16 - 2 * heads_dev, state_dim), jnp.float32)
    packed = jnp.concatenate(
        [state_out.reshape(heads_dev * head_dim, state_dim), decay_rows, decay_rows, spare], axis=0
    )
    local_y = intra + skip_gain[None, :, None] * x_heads
    gate = jax.nn.silu(z_raw.astype(jnp.float32)).reshape(tok_dev, heads_dev, head_dim)
    scanned, (local_y, gate, carry_in) = exclusive_scan(packed, "seq", (local_y, gate, carry_in), heads_dev)
    state_in = scanned[: heads_dev * head_dim].reshape(heads_dev, head_dim, state_dim)
    incoming = jnp.einsum("tn,hpn->thp", c_rows, state_in, precision=precise)
    y_block = local_y + carry_in[:, :, None] * incoming
    gated = (y_block * gate).reshape(tok_dev, inner_dev).astype(jnp.bfloat16)
    ordered = gated.reshape(seq_count, piece_rows, inner_dev)
    outgoing = jnp.take(ordered, dealt_row, axis=0)
    returned = lax.all_to_all(outgoing, "seq", split_axis=0, concat_axis=0, tiled=True)
    return returned.reshape(tok_dev, inner_dev)


def solution(mesh):
    return jax.shard_map(
        per_device,
        mesh=mesh,
        in_specs=(
            P("seq", "fsdp"),
            P(),
            P(),
            P(None, "fsdp"),
            P(None, "fsdp"),
            P("fsdp", None),
            P(None, "fsdp"),
            P(None, "fsdp"),
            P(),
            P("fsdp"),
            P("fsdp"),
            P("fsdp"),
        ),
        out_specs=P("seq", "fsdp"),
        check_vma=False,
    )
```

```python
import jax
import jax.numpy as jnp
from jax import lax
from jax.sharding import PartitionSpec as P

precise = lax.Precision.HIGHEST


def shifted(array, axis, by):
    count = lax.axis_size(axis)
    pairs = [(i, i + by) for i in range(count) if 0 <= i + by < count]
    return lax.ppermute(array, axis, pairs)


def combine_packed(earlier, later, heads):
    extra = -(-2 * heads // 16) * 16
    rows = later.shape[0] - extra
    d_e = earlier[rows : rows + heads]
    d_l = later[rows : rows + heads]
    head_dim = rows // heads
    state = d_l[:, None, :] * earlier[:rows].reshape(heads, head_dim, -1) + later[:rows].reshape(heads, head_dim, -1)
    decay = d_e * d_l
    spare = jnp.zeros((extra - 2 * heads, later.shape[1]), later.dtype)
    return jnp.concatenate([state.reshape(rows, -1), decay, decay, spare], axis=0)


def received(packed, axis, by, heads, skip_first=False):
    place = lax.axis_index(axis)
    extra = -(-2 * heads // 16) * 16
    rows = packed.shape[0] - extra
    row = lax.broadcasted_iota(jnp.int32, packed.shape, 0)
    high = packed.astype(jnp.bfloat16)
    low = (packed - high.astype(jnp.float32)).astype(jnp.bfloat16)
    wire = jnp.where((row >= rows + heads) & (row < rows + 2 * heads), low, high)
    count = lax.axis_size(axis)
    first = 1 if skip_first else 0
    pairs = [(i, i + by) for i in range(first, count) if i + by < count]
    got = lax.ppermute(wire, axis, pairs).astype(jnp.float32)
    missing = (place < by + first).astype(jnp.float32)
    decay = got[rows : rows + heads] + got[rows + heads : rows + 2 * heads] + missing
    spare = jnp.zeros((extra - 2 * heads, packed.shape[1]), packed.dtype)
    return jnp.concatenate([got[:rows], decay, decay, spare], axis=0)


def exclusive_scan(packed, axis, side, heads):
    count = lax.axis_size(axis)
    if count == 1:
        return received(packed, axis, 1, heads), side
    held = received(packed, axis, 1, heads)
    if count > 2:
        held = combine_packed(received(packed, axis, 2, heads), held, heads)
    cover = 2
    while cover < count - 1:
        if cover * 2 >= count - 1:
            held, side = lax.optimization_barrier((held, side))
        held = combine_packed(received(held, axis, cover, heads, skip_first=True), held, heads)
        cover *= 2
    return held, side


def exchange(block, axis, dim):
    count = lax.axis_size(axis)
    if count & (count - 1):
        return lax.all_gather(block, axis, axis=dim, tiled=True), None
    held, codes = block, [0]
    bit = count // 2
    while bit >= 1:
        other = lax.ppermute(held, axis, [(i, i ^ bit) for i in range(count)])
        held = jnp.concatenate([held, other], axis=dim)
        codes = codes + [c ^ bit for c in codes]
        bit //= 2
    return held, codes


def to_natural(held, codes, axis, dim):
    if codes is None:
        return held
    count = len(codes)
    width = held.shape[dim] // count
    where_code = [0] * count
    for position, code in enumerate(codes):
        where_code[code] = position
    table = jnp.asarray(where_code, jnp.int32)
    place = lax.axis_index(axis)
    parts = [
        lax.dynamic_slice_in_dim(held, table[jnp.bitwise_xor(index, place)] * width, width, axis=dim)
        for index in range(count)
    ]
    return jnp.concatenate(parts, axis=dim)


def summed_columns(partial, axis):
    count = lax.axis_size(axis)
    if count & (count - 1) or partial.shape[1] % 2:
        return lax.psum(partial, axis).astype(jnp.bfloat16)
    if count == 1:
        return partial.astype(jnp.bfloat16)
    place = lax.axis_index(axis)
    half = partial.shape[1] // 2
    side = place % 2
    kept = lax.dynamic_slice_in_dim(partial, side * half, half, axis=1)
    sent = lax.dynamic_slice_in_dim(partial, (1 - side) * half, half, axis=1)
    kept = kept + lax.ppermute(sent, axis, [(i, i ^ 1) for i in range(count)])
    bit = 2
    while bit < count:
        kept = kept + lax.ppermute(kept, axis, [(i, i ^ bit) for i in range(count)])
        bit *= 2
    kept = kept.astype(jnp.bfloat16)
    other = lax.ppermute(kept, axis, [(i, i ^ 1) for i in range(count)])
    both = jnp.concatenate([kept, other], axis=1)
    return jnp.where(side == 0, both, jnp.concatenate([other, kept], axis=1))


def segment_of(positions, lengths):
    prompt_ends = jnp.cumsum(lengths)
    counted = (positions[:, None] >= prompt_ends[None, :]).astype(jnp.int32)
    return jnp.sum(counted, axis=1)


def causal_conv(extended, segment_ids, weights, conv_width):
    out_rows = extended.shape[0] - conv_width + 1
    target = segment_ids[conv_width - 1 :]
    running = jnp.zeros((out_rows, extended.shape[1]), jnp.float32)
    for tap_index in range(conv_width):
        matched = (segment_ids[tap_index : tap_index + out_rows] == target).astype(jnp.float32)
        running = (
            running
            + weights[tap_index][None, :]
            * extended[tap_index : tap_index + out_rows]
            * matched[:, None]
        )
    return running


def local_terms(x_heads, b_rows, c_rows, step_size, decay_log, segment_ids, seg_before):
    log_decay = -jnp.exp(decay_log)[None, :] * step_size
    positions_in = jnp.arange(x_heads.shape[0], dtype=jnp.int32)
    lower = (positions_in[:, None] >= positions_in[None, :]).astype(jnp.float32)
    cum_decay = jnp.dot(lower, log_decay, precision=precise)
    same_prompt = (segment_ids[:, None] == segment_ids[None, :]) & (
        positions_in[:, None] >= positions_in[None, :]
    )
    decay_gap = cum_decay.T[:, :, None] - cum_decay.T[:, None, :]
    decay_matrix = jnp.exp(jnp.where(same_prompt[None], decay_gap, -jnp.inf))
    scores = jnp.dot(c_rows, b_rows.T, precision=precise)
    x_step = x_heads * step_size[:, :, None]
    intra = jnp.einsum("hts,shp->thp", scores[None] * decay_matrix, x_step, precision=precise)
    to_end = jnp.exp(
        jnp.where(
            (segment_ids == segment_ids[-1])[:, None], cum_decay[-1][None, :] - cum_decay, -jnp.inf
        )
    )
    state_out = jnp.einsum("shp,sn->hpn", x_step * to_end[:, :, None], b_rows, precision=precise)
    carried = segment_ids == seg_before
    carry_in = jnp.exp(jnp.where(carried[:, None], cum_decay, -jnp.inf))
    block_decay = jnp.where(carried[-1], jnp.exp(cum_decay[-1]), 0.0)
    return (intra, state_out, carry_in, block_decay)


def per_device(
    tokens,
    deal_order,
    lengths,
    x_weight,
    z_weight,
    shared_weight,
    step_weight,
    conv_heads,
    conv_shared,
    step_bias,
    decay_log,
    skip_gain,
):
    seq_count = lax.axis_size("seq")
    own_index = lax.axis_index("seq")
    tok_dev = tokens.shape[0]
    piece_rows = tok_dev // seq_count
    slot_rows = tokens.reshape(seq_count, piece_rows, tokens.shape[1])
    arrived = lax.all_to_all(slot_rows, "seq", split_axis=0, concat_axis=0, tiled=True)
    dealt_row = lax.dynamic_slice_in_dim(deal_order, own_index, 1, 0)[0]
    inverse = jnp.argsort(dealt_row)
    stream_block = jnp.take(arrived, inverse, axis=0).reshape(tok_dev, tokens.shape[1])
    inner_dev = x_weight.shape[1]
    heads_dev = step_weight.shape[1]
    head_dim = inner_dev // heads_dev
    state_dim = shared_weight.shape[1] // 2
    bc_partial = jnp.dot(stream_block, shared_weight, preferred_element_type=jnp.float32)
    bc_raw = summed_columns(bc_partial, "fsdp")
    feature_held, codes = exchange(stream_block, "fsdp", 1)
    feature_part = to_natural(feature_held, codes, "fsdp", 1)
    x_acc, z_acc, step_acc = tuple(
        (
            jnp.dot(feature_part, weight, preferred_element_type=jnp.float32)
            for weight in (x_weight, z_weight, step_weight)
        )
    )
    x_raw = x_acc.astype(jnp.bfloat16)
    z_raw = z_acc.astype(jnp.bfloat16)
    step_size = jax.nn.softplus(step_acc + step_bias[None, :])
    mixed_in = jnp.concatenate([x_raw, bc_raw], axis=1)
    conv_width = conv_heads.shape[0]
    prior_rows = shifted(mixed_in[tok_dev - conv_width + 1 :], "seq", 1)
    first_pos = own_index * tok_dev
    positions = first_pos - (conv_width - 1) + jnp.arange(tok_dev + conv_width - 1, dtype=jnp.int32)
    seg_ext = segment_of(positions, lengths)
    extended = jnp.concatenate([prior_rows, mixed_in], axis=0).astype(jnp.float32)
    activated = jax.nn.silu(
        causal_conv(
            extended, seg_ext, jnp.concatenate([conv_heads, conv_shared], axis=1), conv_width
        )
    )
    segment_ids = seg_ext[conv_width - 1 :]
    seg_before = jnp.where(own_index == 0, -1, seg_ext[conv_width - 2])
    x_heads = activated[:, :inner_dev].reshape(tok_dev, heads_dev, head_dim)
    b_rows = activated[:, inner_dev : inner_dev + state_dim]
    c_rows = activated[:, inner_dev + state_dim :]
    intra, state_out, carry_in, block_decay = local_terms(
        x_heads, b_rows, c_rows, step_size, decay_log, segment_ids, seg_before
    )
    decay_rows = jnp.broadcast_to(block_decay[:, None], (heads_dev, state_dim))
    spare = jnp.zeros((-(-2 * heads_dev // 16) * 16 - 2 * heads_dev, state_dim), jnp.float32)
    packed = jnp.concatenate(
        [state_out.reshape(heads_dev * head_dim, state_dim), decay_rows, decay_rows, spare], axis=0
    )
    local_y = intra + skip_gain[None, :, None] * x_heads
    gate = jax.nn.silu(z_raw.astype(jnp.float32)).reshape(tok_dev, heads_dev, head_dim)
    scanned, (local_y, gate, carry_in) = exclusive_scan(packed, "seq", (local_y, gate, carry_in), heads_dev)
    state_in = scanned[: heads_dev * head_dim].reshape(heads_dev, head_dim, state_dim)
    incoming = jnp.einsum("tn,hpn->thp", c_rows, state_in, precision=precise)
    y_block = local_y + carry_in[:, :, None] * incoming
    gated = (y_block * gate).reshape(tok_dev, inner_dev).astype(jnp.bfloat16)
    ordered = gated.reshape(seq_count, piece_rows, inner_dev)
    outgoing = jnp.take(ordered, dealt_row, axis=0)
    returned = lax.all_to_all(outgoing, "seq", split_axis=0, concat_axis=0, tiled=True)
    return returned.reshape(tok_dev, inner_dev)


def solution(mesh):
    return jax.shard_map(
        per_device,
        mesh=mesh,
        in_specs=(
            P("seq", "fsdp"),
            P(),
            P(),
            P(None, "fsdp"),
            P(None, "fsdp"),
            P("fsdp", None),
            P(None, "fsdp"),
            P(None, "fsdp"),
            P(),
            P("fsdp"),
            P("fsdp"),
            P("fsdp"),
        ),
        out_specs=P("seq", "fsdp"),
        check_vma=False,
    )
```

```python
import jax
import jax.numpy as jnp
from jax import lax
from jax.sharding import PartitionSpec as P

precise = lax.Precision.HIGHEST


def shifted(array, axis, by):
    count = lax.axis_size(axis)
    pairs = [(i, i + by) for i in range(count) if 0 <= i + by < count]
    return lax.ppermute(array, axis, pairs)


def combine_packed(earlier, later, heads):
    extra = -(-2 * heads // 16) * 16
    rows = later.shape[0] - extra
    d_e = earlier[rows : rows + heads]
    d_l = later[rows : rows + heads]
    head_dim = rows // heads
    state = d_l[:, None, :] * earlier[:rows].reshape(heads, head_dim, -1) + later[:rows].reshape(heads, head_dim, -1)
    decay = d_e * d_l
    spare = jnp.zeros((extra - 2 * heads, later.shape[1]), later.dtype)
    return jnp.concatenate([state.reshape(rows, -1), decay, decay, spare], axis=0)


def received(packed, axis, by, heads):
    place = lax.axis_index(axis)
    extra = -(-2 * heads // 16) * 16
    rows = packed.shape[0] - extra
    row = lax.broadcasted_iota(jnp.int32, packed.shape, 0)
    high = packed.astype(jnp.bfloat16)
    low = (packed - high.astype(jnp.float32)).astype(jnp.bfloat16)
    wire = jnp.where((row >= rows + heads) & (row < rows + 2 * heads), low, high)
    got = shifted(wire, axis, by).astype(jnp.float32)
    missing = (place < by).astype(jnp.float32)
    decay = got[rows : rows + heads] + got[rows + heads : rows + 2 * heads] + missing
    spare = jnp.zeros((extra - 2 * heads, packed.shape[1]), packed.dtype)
    return jnp.concatenate([got[:rows], decay, decay, spare], axis=0)


def exclusive_scan(packed, axis, side, heads):
    count = lax.axis_size(axis)
    if count == 1:
        return received(packed, axis, 1, heads), side
    held = received(packed, axis, 1, heads)
    if count > 2:
        held = combine_packed(received(packed, axis, 2, heads), held, heads)
    cover = 2
    while cover < count - 1:
        if cover * 2 >= count - 1:
            held, side = lax.optimization_barrier((held, side))
        held = combine_packed(received(held, axis, cover, heads), held, heads)
        cover *= 2
    return held, side


def exchange(block, axis, dim):
    count = lax.axis_size(axis)
    if count & (count - 1):
        return lax.all_gather(block, axis, axis=dim, tiled=True), None
    held, codes = block, [0]
    bit = count // 2
    while bit >= 1:
        other = lax.ppermute(held, axis, [(i, i ^ bit) for i in range(count)])
        held = jnp.concatenate([held, other], axis=dim)
        codes = codes + [c ^ bit for c in codes]
        bit //= 2
    return held, codes


def to_natural(held, codes, axis, dim):
    if codes is None:
        return held
    count = len(codes)
    width = held.shape[dim] // count
    where_code = [0] * count
    for position, code in enumerate(codes):
        where_code[code] = position
    table = jnp.asarray(where_code, jnp.int32)
    place = lax.axis_index(axis)
    parts = [
        lax.dynamic_slice_in_dim(held, table[jnp.bitwise_xor(index, place)] * width, width, axis=dim)
        for index in range(count)
    ]
    return jnp.concatenate(parts, axis=dim)


def summed_columns(partial, axis):
    count = lax.axis_size(axis)
    if count & (count - 1) or partial.shape[1] % 2:
        return lax.psum(partial, axis).astype(jnp.bfloat16)
    if count == 1:
        return partial.astype(jnp.bfloat16)
    place = lax.axis_index(axis)
    half = partial.shape[1] // 2
    side = place % 2
    kept = lax.dynamic_slice_in_dim(partial, side * half, half, axis=1)
    sent = lax.dynamic_slice_in_dim(partial, (1 - side) * half, half, axis=1)
    kept = kept + lax.ppermute(sent, axis, [(i, i ^ 1) for i in range(count)])
    bit = 2
    while bit < count:
        kept = kept + lax.ppermute(kept, axis, [(i, i ^ bit) for i in range(count)])
        bit *= 2
    kept = kept.astype(jnp.bfloat16)
    other = lax.ppermute(kept, axis, [(i, i ^ 1) for i in range(count)])
    both = jnp.concatenate([kept, other], axis=1)
    return jnp.where(side == 0, both, jnp.concatenate([other, kept], axis=1))


def segment_of(positions, lengths):
    prompt_ends = jnp.cumsum(lengths)
    counted = (positions[:, None] >= prompt_ends[None, :]).astype(jnp.int32)
    return jnp.sum(counted, axis=1)


def causal_conv(extended, segment_ids, weights, conv_width):
    out_rows = extended.shape[0] - conv_width + 1
    target = segment_ids[conv_width - 1 :]
    running = jnp.zeros((out_rows, extended.shape[1]), jnp.float32)
    for tap_index in range(conv_width):
        matched = (segment_ids[tap_index : tap_index + out_rows] == target).astype(jnp.float32)
        running = (
            running
            + weights[tap_index][None, :]
            * extended[tap_index : tap_index + out_rows]
            * matched[:, None]
        )
    return running


def local_terms(x_heads, b_rows, c_rows, step_size, decay_log, segment_ids, seg_before):
    log_decay = -jnp.exp(decay_log)[None, :] * step_size
    positions_in = jnp.arange(x_heads.shape[0], dtype=jnp.int32)
    lower = (positions_in[:, None] >= positions_in[None, :]).astype(jnp.float32)
    cum_decay = jnp.dot(lower, log_decay, precision=precise)
    same_prompt = (segment_ids[:, None] == segment_ids[None, :]) & (
        positions_in[:, None] >= positions_in[None, :]
    )
    decay_gap = cum_decay.T[:, :, None] - cum_decay.T[:, None, :]
    decay_matrix = jnp.exp(jnp.where(same_prompt[None], decay_gap, -jnp.inf))
    scores = jnp.dot(c_rows, b_rows.T, precision=precise)
    x_step = x_heads * step_size[:, :, None]
    intra = jnp.einsum("hts,shp->thp", scores[None] * decay_matrix, x_step, precision=precise)
    to_end = jnp.exp(
        jnp.where(
            (segment_ids == segment_ids[-1])[:, None], cum_decay[-1][None, :] - cum_decay, -jnp.inf
        )
    )
    state_out = jnp.einsum("shp,sn->hpn", x_step * to_end[:, :, None], b_rows, precision=precise)
    carried = segment_ids == seg_before
    carry_in = jnp.exp(jnp.where(carried[:, None], cum_decay, -jnp.inf))
    block_decay = jnp.where(carried[-1], jnp.exp(cum_decay[-1]), 0.0)
    return (intra, state_out, carry_in, block_decay)


def per_device(
    tokens,
    deal_order,
    lengths,
    x_weight,
    z_weight,
    shared_weight,
    step_weight,
    conv_heads,
    conv_shared,
    step_bias,
    decay_log,
    skip_gain,
):
    seq_count = lax.axis_size("seq")
    own_index = lax.axis_index("seq")
    tok_dev = tokens.shape[0]
    piece_rows = tok_dev // seq_count
    slot_rows = tokens.reshape(seq_count, piece_rows, tokens.shape[1])
    arrived = lax.all_to_all(slot_rows, "seq", split_axis=0, concat_axis=0, tiled=True)
    dealt_row = lax.dynamic_slice_in_dim(deal_order, own_index, 1, 0)[0]
    inverse = jnp.argsort(dealt_row)
    stream_block = jnp.take(arrived, inverse, axis=0).reshape(tok_dev, tokens.shape[1])
    inner_dev = x_weight.shape[1]
    heads_dev = step_weight.shape[1]
    head_dim = inner_dev // heads_dev
    state_dim = shared_weight.shape[1] // 2
    bc_partial = jnp.dot(stream_block, shared_weight, preferred_element_type=jnp.float32)
    bc_raw = summed_columns(bc_partial, "fsdp")
    feature_held, codes = exchange(stream_block, "fsdp", 1)
    feature_part = to_natural(feature_held, codes, "fsdp", 1)
    x_acc, step_acc = tuple(
        (
            jnp.dot(feature_part, weight, preferred_element_type=jnp.float32)
            for weight in (x_weight, step_weight)
        )
    )
    x_raw = x_acc.astype(jnp.bfloat16)
    step_size = jax.nn.softplus(step_acc + step_bias[None, :])
    mixed_in = jnp.concatenate([x_raw, bc_raw], axis=1)
    conv_width = conv_heads.shape[0]
    prior_rows = shifted(mixed_in[tok_dev - conv_width + 1 :], "seq", 1)
    first_pos = own_index * tok_dev
    positions = first_pos - (conv_width - 1) + jnp.arange(tok_dev + conv_width - 1, dtype=jnp.int32)
    seg_ext = segment_of(positions, lengths)
    extended = jnp.concatenate([prior_rows, mixed_in], axis=0).astype(jnp.float32)
    activated = jax.nn.silu(
        causal_conv(
            extended, seg_ext, jnp.concatenate([conv_heads, conv_shared], axis=1), conv_width
        )
    )
    segment_ids = seg_ext[conv_width - 1 :]
    seg_before = jnp.where(own_index == 0, -1, seg_ext[conv_width - 2])
    x_heads = activated[:, :inner_dev].reshape(tok_dev, heads_dev, head_dim)
    b_rows = activated[:, inner_dev : inner_dev + state_dim]
    c_rows = activated[:, inner_dev + state_dim :]
    intra, state_out, carry_in, block_decay = local_terms(
        x_heads, b_rows, c_rows, step_size, decay_log, segment_ids, seg_before
    )
    decay_rows = jnp.broadcast_to(block_decay[:, None], (heads_dev, state_dim))
    spare = jnp.zeros((-(-2 * heads_dev // 16) * 16 - 2 * heads_dev, state_dim), jnp.float32)
    packed = jnp.concatenate(
        [state_out.reshape(heads_dev * head_dim, state_dim), decay_rows, decay_rows, spare], axis=0
    )
    packed, z_features = lax.optimization_barrier((packed, feature_part))
    z_raw = jnp.dot(z_features, z_weight, preferred_element_type=jnp.float32).astype(jnp.bfloat16)
    local_y = intra + skip_gain[None, :, None] * x_heads
    gate = jax.nn.silu(z_raw.astype(jnp.float32)).reshape(tok_dev, heads_dev, head_dim)
    scanned, (local_y, gate, carry_in) = exclusive_scan(packed, "seq", (local_y, gate, carry_in), heads_dev)
    state_in = scanned[: heads_dev * head_dim].reshape(heads_dev, head_dim, state_dim)
    incoming = jnp.einsum("tn,hpn->thp", c_rows, state_in, precision=precise)
    y_block = local_y + carry_in[:, :, None] * incoming
    gated = (y_block * gate).reshape(tok_dev, inner_dev).astype(jnp.bfloat16)
    ordered = gated.reshape(seq_count, piece_rows, inner_dev)
    outgoing = jnp.take(ordered, dealt_row, axis=0)
    returned = lax.all_to_all(outgoing, "seq", split_axis=0, concat_axis=0, tiled=True)
    return returned.reshape(tok_dev, inner_dev)


def solution(mesh):
    return jax.shard_map(
        per_device,
        mesh=mesh,
        in_specs=(
            P("seq", "fsdp"),
            P(),
            P(),
            P(None, "fsdp"),
            P(None, "fsdp"),
            P("fsdp", None),
            P(None, "fsdp"),
            P(None, "fsdp"),
            P(),
            P("fsdp"),
            P("fsdp"),
            P("fsdp"),
        ),
        out_specs=P("seq", "fsdp"),
        check_vma=False,
    )
```

```python
import jax
import jax.numpy as jnp
from jax import lax
from jax.sharding import PartitionSpec as P

precise = lax.Precision.HIGHEST


def shifted(array, axis, by):
    count = lax.axis_size(axis)
    pairs = [(i, i + by) for i in range(count) if 0 <= i + by < count]
    return lax.ppermute(array, axis, pairs)


def combine_packed(earlier, later, heads):
    extra = -(-2 * heads // 16) * 16
    rows = later.shape[0] - extra
    d_e = earlier[rows : rows + heads]
    d_l = later[rows : rows + heads]
    head_dim = rows // heads
    state = d_l[:, None, :] * earlier[:rows].reshape(heads, head_dim, -1) + later[:rows].reshape(heads, head_dim, -1)
    decay = d_e * d_l
    spare = jnp.zeros((extra - 2 * heads, later.shape[1]), later.dtype)
    return jnp.concatenate([state.reshape(rows, -1), decay, decay, spare], axis=0)


def received(packed, axis, by, heads):
    place = lax.axis_index(axis)
    extra = -(-2 * heads // 16) * 16
    rows = packed.shape[0] - extra
    row = lax.broadcasted_iota(jnp.int32, packed.shape, 0)
    high = packed.astype(jnp.bfloat16)
    low = (packed - high.astype(jnp.float32)).astype(jnp.bfloat16)
    wire = jnp.where((row >= rows + heads) & (row < rows + 2 * heads), low, high)
    got = shifted(wire, axis, by).astype(jnp.float32)
    missing = (place < by).astype(jnp.float32)
    decay = got[rows : rows + heads] + got[rows + heads : rows + 2 * heads] + missing
    spare = jnp.zeros((extra - 2 * heads, packed.shape[1]), packed.dtype)
    return jnp.concatenate([got[:rows], decay, decay, spare], axis=0)


def exclusive_scan(packed, axis, side, heads):
    count = lax.axis_size(axis)
    if count == 1:
        return received(packed, axis, 1, heads), side
    held = received(packed, axis, 1, heads)
    if count > 2:
        held = combine_packed(received(packed, axis, 2, heads), held, heads)
    cover = 2
    while cover < count - 1:
        if cover * 2 >= count - 1:
            held, side = lax.optimization_barrier((held, side))
        held = combine_packed(received(held, axis, cover, heads), held, heads)
        cover *= 2
    return held, side


def exchange(block, axis, dim):
    count = lax.axis_size(axis)
    if count & (count - 1):
        return lax.all_gather(block, axis, axis=dim, tiled=True), None
    held, codes = block, [0]
    bit = count // 2
    while bit >= 1:
        other = lax.ppermute(held, axis, [(i, i ^ bit) for i in range(count)])
        held = jnp.concatenate([held, other], axis=dim)
        codes = codes + [c ^ bit for c in codes]
        bit //= 2
    return held, codes


def to_natural(held, codes, axis, dim):
    if codes is None:
        return held
    count = len(codes)
    width = held.shape[dim] // count
    where_code = [0] * count
    for position, code in enumerate(codes):
        where_code[code] = position
    table = jnp.asarray(where_code, jnp.int32)
    place = lax.axis_index(axis)
    parts = [
        lax.dynamic_slice_in_dim(held, table[jnp.bitwise_xor(index, place)] * width, width, axis=dim)
        for index in range(count)
    ]
    return jnp.concatenate(parts, axis=dim)


def summed_columns(partial, axis):
    count = lax.axis_size(axis)
    if count & (count - 1) or partial.shape[1] % 2:
        return lax.psum(partial, axis).astype(jnp.bfloat16)
    if count == 1:
        return partial.astype(jnp.bfloat16)
    place = lax.axis_index(axis)
    half = partial.shape[1] // 2
    side = place % 2
    kept = lax.dynamic_slice_in_dim(partial, side * half, half, axis=1)
    sent = lax.dynamic_slice_in_dim(partial, (1 - side) * half, half, axis=1)
    kept = kept + lax.ppermute(sent, axis, [(i, i ^ 1) for i in range(count)])
    bit = 2
    while bit < count:
        kept = kept + lax.ppermute(kept, axis, [(i, i ^ bit) for i in range(count)])
        bit *= 2
    kept = kept.astype(jnp.bfloat16)
    other = lax.ppermute(kept, axis, [(i, i ^ 1) for i in range(count)])
    both = jnp.concatenate([kept, other], axis=1)
    return jnp.where(side == 0, both, jnp.concatenate([other, kept], axis=1))


def segment_of(positions, lengths):
    prompt_ends = jnp.cumsum(lengths)
    counted = (positions[:, None] >= prompt_ends[None, :]).astype(jnp.int32)
    return jnp.sum(counted, axis=1)


def causal_conv(extended, segment_ids, weights, conv_width):
    out_rows = extended.shape[0] - conv_width + 1
    target = segment_ids[conv_width - 1 :]
    running = jnp.zeros((out_rows, extended.shape[1]), jnp.float32)
    for tap_index in range(conv_width):
        matched = (segment_ids[tap_index : tap_index + out_rows] == target).astype(jnp.float32)
        running = (
            running
            + weights[tap_index][None, :]
            * extended[tap_index : tap_index + out_rows]
            * matched[:, None]
        )
    return running


def local_terms(x_heads, b_rows, c_rows, step_size, decay_log, segment_ids, seg_before):
    log_decay = -jnp.exp(decay_log)[None, :] * step_size
    positions_in = jnp.arange(x_heads.shape[0], dtype=jnp.int32)
    lower = (positions_in[:, None] >= positions_in[None, :]).astype(jnp.float32)
    cum_decay = jnp.dot(lower, log_decay, precision=precise)
    same_prompt = (segment_ids[:, None] == segment_ids[None, :]) & (
        positions_in[:, None] >= positions_in[None, :]
    )
    decay_gap = cum_decay.T[:, :, None] - cum_decay.T[:, None, :]
    decay_matrix = jnp.exp(jnp.where(same_prompt[None], decay_gap, -jnp.inf))
    scores = jnp.dot(c_rows, b_rows.T, precision=precise)
    x_step = x_heads * step_size[:, :, None]
    intra = jnp.einsum("hts,shp->thp", scores[None] * decay_matrix, x_step, precision=precise)
    to_end = jnp.exp(
        jnp.where(
            (segment_ids == segment_ids[-1])[:, None], cum_decay[-1][None, :] - cum_decay, -jnp.inf
        )
    )
    state_out = jnp.einsum("shp,sn->hpn", x_step * to_end[:, :, None], b_rows)
    carried = segment_ids == seg_before
    carry_in = jnp.exp(jnp.where(carried[:, None], cum_decay, -jnp.inf))
    block_decay = jnp.where(carried[-1], jnp.exp(cum_decay[-1]), 0.0)
    return (intra, state_out, carry_in, block_decay)


def per_device(
    tokens,
    deal_order,
    lengths,
    x_weight,
    z_weight,
    shared_weight,
    step_weight,
    conv_heads,
    conv_shared,
    step_bias,
    decay_log,
    skip_gain,
):
    seq_count = lax.axis_size("seq")
    own_index = lax.axis_index("seq")
    tok_dev = tokens.shape[0]
    piece_rows = tok_dev // seq_count
    slot_rows = tokens.reshape(seq_count, piece_rows, tokens.shape[1])
    arrived = lax.all_to_all(slot_rows, "seq", split_axis=0, concat_axis=0, tiled=True)
    dealt_row = lax.dynamic_slice_in_dim(deal_order, own_index, 1, 0)[0]
    inverse = jnp.argsort(dealt_row)
    stream_block = jnp.take(arrived, inverse, axis=0).reshape(tok_dev, tokens.shape[1])
    inner_dev = x_weight.shape[1]
    heads_dev = step_weight.shape[1]
    head_dim = inner_dev // heads_dev
    state_dim = shared_weight.shape[1] // 2
    bc_partial = jnp.dot(stream_block, shared_weight, preferred_element_type=jnp.float32)
    bc_raw = summed_columns(bc_partial, "fsdp")
    feature_held, codes = exchange(stream_block, "fsdp", 1)
    feature_part = to_natural(feature_held, codes, "fsdp", 1)
    x_acc, z_acc, step_acc = tuple(
        (
            jnp.dot(feature_part, weight, preferred_element_type=jnp.float32)
            for weight in (x_weight, z_weight, step_weight)
        )
    )
    x_raw = x_acc.astype(jnp.bfloat16)
    z_raw = z_acc.astype(jnp.bfloat16)
    step_size = jax.nn.softplus(step_acc + step_bias[None, :])
    mixed_in = jnp.concatenate([x_raw, bc_raw], axis=1)
    conv_width = conv_heads.shape[0]
    prior_rows = shifted(mixed_in[tok_dev - conv_width + 1 :], "seq", 1)
    first_pos = own_index * tok_dev
    positions = first_pos - (conv_width - 1) + jnp.arange(tok_dev + conv_width - 1, dtype=jnp.int32)
    seg_ext = segment_of(positions, lengths)
    extended = jnp.concatenate([prior_rows, mixed_in], axis=0).astype(jnp.float32)
    activated = jax.nn.silu(
        causal_conv(
            extended, seg_ext, jnp.concatenate([conv_heads, conv_shared], axis=1), conv_width
        )
    )
    segment_ids = seg_ext[conv_width - 1 :]
    seg_before = jnp.where(own_index == 0, -1, seg_ext[conv_width - 2])
    x_heads = activated[:, :inner_dev].reshape(tok_dev, heads_dev, head_dim)
    b_rows = activated[:, inner_dev : inner_dev + state_dim]
    c_rows = activated[:, inner_dev + state_dim :]
    intra, state_out, carry_in, block_decay = local_terms(
        x_heads, b_rows, c_rows, step_size, decay_log, segment_ids, seg_before
    )
    decay_rows = jnp.broadcast_to(block_decay[:, None], (heads_dev, state_dim))
    spare = jnp.zeros((-(-2 * heads_dev // 16) * 16 - 2 * heads_dev, state_dim), jnp.float32)
    packed = jnp.concatenate(
        [state_out.reshape(heads_dev * head_dim, state_dim), decay_rows, decay_rows, spare], axis=0
    )
    local_y = intra + skip_gain[None, :, None] * x_heads
    gate = jax.nn.silu(z_raw.astype(jnp.float32)).reshape(tok_dev, heads_dev, head_dim)
    scanned, (local_y, gate, carry_in) = exclusive_scan(packed, "seq", (local_y, gate, carry_in), heads_dev)
    state_in = scanned[: heads_dev * head_dim].reshape(heads_dev, head_dim, state_dim)
    incoming = jnp.einsum("tn,hpn->thp", c_rows, state_in, precision=lax.Precision.HIGH)
    y_block = local_y + carry_in[:, :, None] * incoming
    gated = (y_block * gate).reshape(tok_dev, inner_dev).astype(jnp.bfloat16)
    ordered = gated.reshape(seq_count, piece_rows, inner_dev)
    outgoing = jnp.take(ordered, dealt_row, axis=0)
    returned = lax.all_to_all(outgoing, "seq", split_axis=0, concat_axis=0, tiled=True)
    return returned.reshape(tok_dev, inner_dev)


def solution(mesh):
    return jax.shard_map(
        per_device,
        mesh=mesh,
        in_specs=(
            P("seq", "fsdp"),
            P(),
            P(),
            P(None, "fsdp"),
            P(None, "fsdp"),
            P("fsdp", None),
            P(None, "fsdp"),
            P(None, "fsdp"),
            P(),
            P("fsdp"),
            P("fsdp"),
            P("fsdp"),
        ),
        out_specs=P("seq", "fsdp"),
        check_vma=False,
    )
```

```python
import jax
import jax.numpy as jnp
from jax import lax
from jax.sharding import PartitionSpec as P

precise = lax.Precision.HIGHEST


def shifted(array, axis, by):
    count = lax.axis_size(axis)
    pairs = [(i, i + by) for i in range(count) if 0 <= i + by < count]
    return lax.ppermute(array, axis, pairs)


def combine_packed(earlier, later, heads):
    extra = -(-2 * heads // 16) * 16
    rows = later.shape[0] - extra
    d_e = earlier[rows : rows + heads]
    d_l = later[rows : rows + heads]
    head_dim = rows // heads
    state = d_l[:, None, :] * earlier[:rows].reshape(heads, head_dim, -1) + later[:rows].reshape(heads, head_dim, -1)
    decay = d_e * d_l
    spare = jnp.zeros((extra - 2 * heads, later.shape[1]), later.dtype)
    return jnp.concatenate([state.reshape(rows, -1), decay, decay, spare], axis=0)


def received(packed, axis, by, heads):
    place = lax.axis_index(axis)
    extra = -(-2 * heads // 16) * 16
    rows = packed.shape[0] - extra
    row = lax.broadcasted_iota(jnp.int32, packed.shape, 0)
    high = packed.astype(jnp.bfloat16)
    low = (packed - high.astype(jnp.float32)).astype(jnp.bfloat16)
    wire = jnp.where((row >= rows + heads) & (row < rows + 2 * heads), low, high)
    got = shifted(wire, axis, by).astype(jnp.float32)
    missing = (place < by).astype(jnp.float32)
    decay = got[rows : rows + heads] + got[rows + heads : rows + 2 * heads] + missing
    spare = jnp.zeros((extra - 2 * heads, packed.shape[1]), packed.dtype)
    return jnp.concatenate([got[:rows], decay, decay, spare], axis=0)


def exclusive_scan(packed, axis, side, heads):
    count = lax.axis_size(axis)
    if count == 1:
        return received(packed, axis, 1, heads), side
    held = received(packed, axis, 1, heads)
    if count > 2:
        held = combine_packed(received(packed, axis, 2, heads), held, heads)
    cover = 2
    while cover < count - 1:
        if cover == 2:
            held, side = lax.optimization_barrier((held, side))
        held = combine_packed(received(held, axis, cover, heads), held, heads)
        cover *= 2
    return held, side


def exchange(block, axis, dim):
    count = lax.axis_size(axis)
    if count & (count - 1):
        return lax.all_gather(block, axis, axis=dim, tiled=True), None
    held, codes = block, [0]
    bit = count // 2
    while bit >= 1:
        other = lax.ppermute(held, axis, [(i, i ^ bit) for i in range(count)])
        held = jnp.concatenate([held, other], axis=dim)
        codes = codes + [c ^ bit for c in codes]
        bit //= 2
    return held, codes


def to_natural(held, codes, axis, dim):
    if codes is None:
        return held
    count = len(codes)
    width = held.shape[dim] // count
    where_code = [0] * count
    for position, code in enumerate(codes):
        where_code[code] = position
    table = jnp.asarray(where_code, jnp.int32)
    place = lax.axis_index(axis)
    parts = [
        lax.dynamic_slice_in_dim(held, table[jnp.bitwise_xor(index, place)] * width, width, axis=dim)
        for index in range(count)
    ]
    return jnp.concatenate(parts, axis=dim)


def summed_columns(partial, axis):
    count = lax.axis_size(axis)
    if count & (count - 1) or partial.shape[1] % 2:
        return lax.psum(partial, axis).astype(jnp.bfloat16)
    if count == 1:
        return partial.astype(jnp.bfloat16)
    place = lax.axis_index(axis)
    half = partial.shape[1] // 2
    side = place % 2
    kept = lax.dynamic_slice_in_dim(partial, side * half, half, axis=1)
    sent = lax.dynamic_slice_in_dim(partial, (1 - side) * half, half, axis=1)
    kept = kept + lax.ppermute(sent, axis, [(i, i ^ 1) for i in range(count)])
    bit = 2
    while bit < count:
        kept = kept + lax.ppermute(kept, axis, [(i, i ^ bit) for i in range(count)])
        bit *= 2
    kept = kept.astype(jnp.bfloat16)
    other = lax.ppermute(kept, axis, [(i, i ^ 1) for i in range(count)])
    both = jnp.concatenate([kept, other], axis=1)
    return jnp.where(side == 0, both, jnp.concatenate([other, kept], axis=1))


def segment_of(positions, lengths):
    prompt_ends = jnp.cumsum(lengths)
    counted = (positions[:, None] >= prompt_ends[None, :]).astype(jnp.int32)
    return jnp.sum(counted, axis=1)


def causal_conv(extended, segment_ids, weights, conv_width):
    out_rows = extended.shape[0] - conv_width + 1
    target = segment_ids[conv_width - 1 :]
    running = jnp.zeros((out_rows, extended.shape[1]), jnp.float32)
    for tap_index in range(conv_width):
        matched = (segment_ids[tap_index : tap_index + out_rows] == target).astype(jnp.float32)
        running = (
            running
            + weights[tap_index][None, :]
            * extended[tap_index : tap_index + out_rows]
            * matched[:, None]
        )
    return running


def local_terms(x_heads, b_rows, c_rows, step_size, decay_log, segment_ids, seg_before):
    log_decay = -jnp.exp(decay_log)[None, :] * step_size
    positions_in = jnp.arange(x_heads.shape[0], dtype=jnp.int32)
    lower = (positions_in[:, None] >= positions_in[None, :]).astype(jnp.float32)
    cum_decay = jnp.dot(lower, log_decay, precision=precise)
    same_prompt = (segment_ids[:, None] == segment_ids[None, :]) & (
        positions_in[:, None] >= positions_in[None, :]
    )
    decay_gap = cum_decay.T[:, :, None] - cum_decay.T[:, None, :]
    decay_matrix = jnp.exp(jnp.where(same_prompt[None], decay_gap, -jnp.inf))
    scores = jnp.dot(c_rows, b_rows.T, precision=precise)
    x_step = x_heads * step_size[:, :, None]
    intra = jnp.einsum("hts,shp->thp", scores[None] * decay_matrix, x_step, precision=precise)
    to_end = jnp.exp(
        jnp.where(
            (segment_ids == segment_ids[-1])[:, None], cum_decay[-1][None, :] - cum_decay, -jnp.inf
        )
    )
    state_out = jnp.einsum("shp,sn->hpn", x_step * to_end[:, :, None], b_rows)
    carried = segment_ids == seg_before
    carry_in = jnp.exp(jnp.where(carried[:, None], cum_decay, -jnp.inf))
    block_decay = jnp.where(carried[-1], jnp.exp(cum_decay[-1]), 0.0)
    return (intra, state_out, carry_in, block_decay)


def per_device(
    tokens,
    deal_order,
    lengths,
    x_weight,
    z_weight,
    shared_weight,
    step_weight,
    conv_heads,
    conv_shared,
    step_bias,
    decay_log,
    skip_gain,
):
    seq_count = lax.axis_size("seq")
    own_index = lax.axis_index("seq")
    tok_dev = tokens.shape[0]
    piece_rows = tok_dev // seq_count
    slot_rows = tokens.reshape(seq_count, piece_rows, tokens.shape[1])
    arrived = lax.all_to_all(slot_rows, "seq", split_axis=0, concat_axis=0, tiled=True)
    dealt_row = lax.dynamic_slice_in_dim(deal_order, own_index, 1, 0)[0]
    inverse = jnp.argsort(dealt_row)
    stream_block = jnp.take(arrived, inverse, axis=0).reshape(tok_dev, tokens.shape[1])
    inner_dev = x_weight.shape[1]
    heads_dev = step_weight.shape[1]
    head_dim = inner_dev // heads_dev
    state_dim = shared_weight.shape[1] // 2
    bc_partial = jnp.dot(stream_block, shared_weight, preferred_element_type=jnp.float32)
    bc_raw = summed_columns(bc_partial, "fsdp")
    feature_held, codes = exchange(stream_block, "fsdp", 1)
    feature_part = to_natural(feature_held, codes, "fsdp", 1)
    x_acc, z_acc, step_acc = tuple(
        (
            jnp.dot(feature_part, weight, preferred_element_type=jnp.float32)
            for weight in (x_weight, z_weight, step_weight)
        )
    )
    x_raw = x_acc.astype(jnp.bfloat16)
    z_raw = z_acc.astype(jnp.bfloat16)
    step_size = jax.nn.softplus(step_acc + step_bias[None, :])
    mixed_in = jnp.concatenate([x_raw, bc_raw], axis=1)
    conv_width = conv_heads.shape[0]
    prior_rows = shifted(mixed_in[tok_dev - conv_width + 1 :], "seq", 1)
    first_pos = own_index * tok_dev
    positions = first_pos - (conv_width - 1) + jnp.arange(tok_dev + conv_width - 1, dtype=jnp.int32)
    seg_ext = segment_of(positions, lengths)
    extended = jnp.concatenate([prior_rows, mixed_in], axis=0).astype(jnp.float32)
    activated = jax.nn.silu(
        causal_conv(
            extended, seg_ext, jnp.concatenate([conv_heads, conv_shared], axis=1), conv_width
        )
    )
    segment_ids = seg_ext[conv_width - 1 :]
    seg_before = jnp.where(own_index == 0, -1, seg_ext[conv_width - 2])
    x_heads = activated[:, :inner_dev].reshape(tok_dev, heads_dev, head_dim)
    b_rows = activated[:, inner_dev : inner_dev + state_dim]
    c_rows = activated[:, inner_dev + state_dim :]
    intra, state_out, carry_in, block_decay = local_terms(
        x_heads, b_rows, c_rows, step_size, decay_log, segment_ids, seg_before
    )
    decay_rows = jnp.broadcast_to(block_decay[:, None], (heads_dev, state_dim))
    spare = jnp.zeros((-(-2 * heads_dev // 16) * 16 - 2 * heads_dev, state_dim), jnp.float32)
    packed = jnp.concatenate(
        [state_out.reshape(heads_dev * head_dim, state_dim), decay_rows, decay_rows, spare], axis=0
    )
    local_y = intra + skip_gain[None, :, None] * x_heads
    gate = jax.nn.silu(z_raw.astype(jnp.float32)).reshape(tok_dev, heads_dev, head_dim)
    scanned, (local_y, gate, carry_in) = exclusive_scan(packed, "seq", (local_y, gate, carry_in), heads_dev)
    state_in = scanned[: heads_dev * head_dim].reshape(heads_dev, head_dim, state_dim)
    incoming = jnp.einsum("tn,hpn->thp", c_rows, state_in, precision=lax.Precision.HIGH)
    y_block = local_y + carry_in[:, :, None] * incoming
    gated = (y_block * gate).reshape(tok_dev, inner_dev).astype(jnp.bfloat16)
    ordered = gated.reshape(seq_count, piece_rows, inner_dev)
    outgoing = jnp.take(ordered, dealt_row, axis=0)
    returned = lax.all_to_all(outgoing, "seq", split_axis=0, concat_axis=0, tiled=True)
    return returned.reshape(tok_dev, inner_dev)


def solution(mesh):
    return jax.shard_map(
        per_device,
        mesh=mesh,
        in_specs=(
            P("seq", "fsdp"),
            P(),
            P(),
            P(None, "fsdp"),
            P(None, "fsdp"),
            P("fsdp", None),
            P(None, "fsdp"),
            P(None, "fsdp"),
            P(),
            P("fsdp"),
            P("fsdp"),
            P("fsdp"),
        ),
        out_specs=P("seq", "fsdp"),
        check_vma=False,
    )
```

```python
import jax
import jax.numpy as jnp
from jax import lax
from jax.sharding import PartitionSpec as P

precise = lax.Precision.HIGHEST


def shifted(array, axis, by):
    count = lax.axis_size(axis)
    pairs = [(i, i + by) for i in range(count) if 0 <= i + by < count]
    return lax.ppermute(array, axis, pairs)


def combine_packed(earlier, later, heads):
    extra = -(-2 * heads // 16) * 16
    rows = later.shape[0] - extra
    d_e = earlier[rows : rows + heads]
    d_l = later[rows : rows + heads]
    head_dim = rows // heads
    state = d_l[:, None, :] * earlier[:rows].reshape(heads, head_dim, -1) + later[:rows].reshape(heads, head_dim, -1)
    decay = d_e * d_l
    spare = jnp.zeros((extra - 2 * heads, later.shape[1]), later.dtype)
    return jnp.concatenate([state.reshape(rows, -1), decay, decay, spare], axis=0)


def received(packed, axis, by, heads):
    place = lax.axis_index(axis)
    extra = -(-2 * heads // 16) * 16
    rows = packed.shape[0] - extra
    row = lax.broadcasted_iota(jnp.int32, packed.shape, 0)
    high = packed.astype(jnp.bfloat16)
    low = (packed - high.astype(jnp.float32)).astype(jnp.bfloat16)
    wire = jnp.where((row >= rows + heads) & (row < rows + 2 * heads), low, high)
    got = shifted(wire, axis, by).astype(jnp.float32)
    missing = (place < by).astype(jnp.float32)
    decay = got[rows : rows + heads] + got[rows + heads : rows + 2 * heads] + missing
    spare = jnp.zeros((extra - 2 * heads, packed.shape[1]), packed.dtype)
    return jnp.concatenate([got[:rows], decay, decay, spare], axis=0)


def exclusive_scan(packed, axis, side, heads):
    count = lax.axis_size(axis)
    if count == 1:
        return received(packed, axis, 1, heads), side
    held = received(packed, axis, 1, heads)
    if count > 2:
        held = combine_packed(received(packed, axis, 2, heads), held, heads)
    cover = 2
    while cover < count - 1:
        if cover * 2 >= count - 1:
            held, side = lax.optimization_barrier((held, side))
        held = combine_packed(received(held, axis, cover, heads), held, heads)
        cover *= 2
    return held, side


def exchange(block, axis, dim):
    count = lax.axis_size(axis)
    if count & (count - 1):
        return lax.all_gather(block, axis, axis=dim, tiled=True), None
    held, codes = block, [0]
    bit = count // 2
    while bit >= 1:
        other = lax.ppermute(held, axis, [(i, i ^ bit) for i in range(count)])
        held = jnp.concatenate([held, other], axis=dim)
        codes = codes + [c ^ bit for c in codes]
        bit //= 2
    return held, codes


def to_natural(held, codes, axis, dim):
    if codes is None:
        return held
    count = len(codes)
    width = held.shape[dim] // count
    where_code = [0] * count
    for position, code in enumerate(codes):
        where_code[code] = position
    table = jnp.asarray(where_code, jnp.int32)
    place = lax.axis_index(axis)
    parts = [
        lax.dynamic_slice_in_dim(held, table[jnp.bitwise_xor(index, place)] * width, width, axis=dim)
        for index in range(count)
    ]
    return jnp.concatenate(parts, axis=dim)


def summed_columns(partial, axis):
    count = lax.axis_size(axis)
    if count & (count - 1) or partial.shape[1] % 2:
        return lax.psum(partial, axis).astype(jnp.bfloat16)
    if count == 1:
        return partial.astype(jnp.bfloat16)
    place = lax.axis_index(axis)
    half = partial.shape[1] // 2
    side = place % 2
    kept = lax.dynamic_slice_in_dim(partial, side * half, half, axis=1)
    sent = lax.dynamic_slice_in_dim(partial, (1 - side) * half, half, axis=1)
    kept = kept + lax.ppermute(sent, axis, [(i, i ^ 1) for i in range(count)])
    bit = 2
    while bit < count:
        kept = kept + lax.ppermute(kept, axis, [(i, i ^ bit) for i in range(count)])
        bit *= 2
    kept = kept.astype(jnp.bfloat16)
    other = lax.ppermute(kept, axis, [(i, i ^ 1) for i in range(count)])
    both = jnp.concatenate([kept, other], axis=1)
    return jnp.where(side == 0, both, jnp.concatenate([other, kept], axis=1))


def segment_of(positions, lengths):
    prompt_ends = jnp.cumsum(lengths)
    counted = (positions[:, None] >= prompt_ends[None, :]).astype(jnp.int32)
    return jnp.sum(counted, axis=1)


def causal_conv(extended, segment_ids, weights, conv_width):
    out_rows = extended.shape[0] - conv_width + 1
    target = segment_ids[conv_width - 1 :]
    running = jnp.zeros((out_rows, extended.shape[1]), jnp.float32)
    for tap_index in range(conv_width):
        matched = (segment_ids[tap_index : tap_index + out_rows] == target).astype(jnp.float32)
        running = (
            running
            + weights[tap_index][None, :]
            * extended[tap_index : tap_index + out_rows]
            * matched[:, None]
        )
    return running


def local_terms(x_heads, b_rows, c_rows, step_size, decay_log, segment_ids, seg_before):
    log_decay = -jnp.exp(decay_log)[None, :] * step_size
    positions_in = jnp.arange(x_heads.shape[0], dtype=jnp.int32)
    lower = (positions_in[:, None] >= positions_in[None, :]).astype(jnp.float32)
    cum_decay = jnp.dot(lower, log_decay, precision=precise)
    same_prompt = (segment_ids[:, None] == segment_ids[None, :]) & (
        positions_in[:, None] >= positions_in[None, :]
    )
    decay_gap = cum_decay.T[:, :, None] - cum_decay.T[:, None, :]
    decay_matrix = jnp.exp(jnp.where(same_prompt[None], decay_gap, -jnp.inf))
    scores = jnp.dot(c_rows, b_rows.T, precision=precise)
    x_step = x_heads * step_size[:, :, None]
    intra = jnp.einsum("hts,shp->thp", scores[None] * decay_matrix, x_step, precision=precise)
    to_end = jnp.exp(
        jnp.where(
            (segment_ids == segment_ids[-1])[:, None], cum_decay[-1][None, :] - cum_decay, -jnp.inf
        )
    )
    state_out = jnp.einsum("shp,sn->hpn", x_step * to_end[:, :, None], b_rows, precision=precise)
    carried = segment_ids == seg_before
    carry_in = jnp.exp(jnp.where(carried[:, None], cum_decay, -jnp.inf))
    block_decay = jnp.where(carried[-1], jnp.exp(cum_decay[-1]), 0.0)
    return (intra, state_out, carry_in, block_decay)


def per_device(
    tokens,
    deal_order,
    lengths,
    x_weight,
    z_weight,
    shared_weight,
    step_weight,
    conv_heads,
    conv_shared,
    step_bias,
    decay_log,
    skip_gain,
):
    seq_count = lax.axis_size("seq")
    own_index = lax.axis_index("seq")
    tok_dev = tokens.shape[0]
    piece_rows = tok_dev // seq_count
    slot_rows = tokens.reshape(seq_count, piece_rows, tokens.shape[1])
    arrived = lax.all_to_all(slot_rows, "seq", split_axis=0, concat_axis=0, tiled=True)
    dealt_row = lax.dynamic_slice_in_dim(deal_order, own_index, 1, 0)[0]
    inverse = jnp.argsort(dealt_row)
    stream_block = jnp.take(arrived, inverse, axis=0).reshape(tok_dev, tokens.shape[1])
    inner_dev = x_weight.shape[1]
    heads_dev = step_weight.shape[1]
    head_dim = inner_dev // heads_dev
    state_dim = shared_weight.shape[1] // 2
    bc_partial = jnp.dot(stream_block, shared_weight, preferred_element_type=jnp.float32)
    bc_raw = summed_columns(bc_partial, "fsdp")
    feature_held, codes = exchange(stream_block, "fsdp", 1)
    feature_part = to_natural(feature_held, codes, "fsdp", 1)
    x_acc, z_acc, step_acc = tuple(
        (
            jnp.dot(feature_part, weight, preferred_element_type=jnp.float32)
            for weight in (x_weight, z_weight, step_weight)
        )
    )
    x_raw = x_acc.astype(jnp.bfloat16)
    z_raw = z_acc.astype(jnp.bfloat16)
    step_size = jax.nn.softplus(step_acc + step_bias[None, :])
    mixed_in = jnp.concatenate([x_raw, bc_raw], axis=1)
    conv_width = conv_heads.shape[0]
    prior_rows = shifted(mixed_in[tok_dev - conv_width + 1 :], "seq", 1)
    first_pos = own_index * tok_dev
    positions = first_pos - (conv_width - 1) + jnp.arange(tok_dev + conv_width - 1, dtype=jnp.int32)
    seg_ext = segment_of(positions, lengths)
    extended = jnp.concatenate([prior_rows, mixed_in], axis=0).astype(jnp.float32)
    activated = jax.nn.silu(
        causal_conv(
            extended, seg_ext, jnp.concatenate([conv_heads, conv_shared], axis=1), conv_width
        )
    )
    segment_ids = seg_ext[conv_width - 1 :]
    seg_before = jnp.where(own_index == 0, -1, seg_ext[conv_width - 2])
    x_heads = activated[:, :inner_dev].reshape(tok_dev, heads_dev, head_dim)
    b_rows = activated[:, inner_dev : inner_dev + state_dim]
    c_rows = activated[:, inner_dev + state_dim :]
    intra, state_out, carry_in, block_decay = local_terms(
        x_heads, b_rows, c_rows, step_size, decay_log, segment_ids, seg_before
    )
    decay_rows = jnp.broadcast_to(block_decay[:, None], (heads_dev, state_dim))
    spare = jnp.zeros((-(-2 * heads_dev // 16) * 16 - 2 * heads_dev, state_dim), jnp.float32)
    packed = jnp.concatenate(
        [state_out.reshape(heads_dev * head_dim, state_dim), decay_rows, decay_rows, spare], axis=0
    )
    local_y = intra + skip_gain[None, :, None] * x_heads
    gate = jax.nn.silu(z_raw.astype(jnp.float32)).reshape(tok_dev, heads_dev, head_dim)
    scanned, (local_y, gate, carry_in) = exclusive_scan(packed, "seq", (local_y, gate, carry_in), heads_dev)
    state_in = scanned[: heads_dev * head_dim].reshape(heads_dev, head_dim, state_dim)
    incoming = jnp.einsum("tn,hpn->thp", c_rows, state_in, precision=precise)
    y_block = local_y + carry_in[:, :, None] * incoming
    gated = (y_block * gate).reshape(tok_dev, inner_dev).astype(jnp.bfloat16)
    ordered = gated.reshape(seq_count, piece_rows, inner_dev)
    chooser = (dealt_row[:, None] == jnp.arange(seq_count, dtype=dealt_row.dtype)[None, :]).astype(jnp.bfloat16)
    outgoing = jnp.einsum("mp,pri->mri", chooser, ordered, preferred_element_type=jnp.float32).astype(
        jnp.bfloat16
    )
    returned = lax.all_to_all(outgoing, "seq", split_axis=0, concat_axis=0, tiled=True)
    return returned.reshape(tok_dev, inner_dev)


def solution(mesh):
    return jax.shard_map(
        per_device,
        mesh=mesh,
        in_specs=(
            P("seq", "fsdp"),
            P(),
            P(),
            P(None, "fsdp"),
            P(None, "fsdp"),
            P("fsdp", None),
            P(None, "fsdp"),
            P(None, "fsdp"),
            P(),
            P("fsdp"),
            P("fsdp"),
            P("fsdp"),
        ),
        out_specs=P("seq", "fsdp"),
        check_vma=False,
    )
```

```python
import jax
import jax.numpy as jnp
from jax import lax
from jax.sharding import PartitionSpec as P

precise = lax.Precision.HIGHEST


def shifted(array, axis, by):
    count = lax.axis_size(axis)
    pairs = [(i, i + by) for i in range(count) if 0 <= i + by < count]
    return lax.ppermute(array, axis, pairs)


def combine_packed(earlier, later, heads):
    extra = -(-2 * heads // 16) * 16
    rows = later.shape[0] - extra
    d_e = earlier[rows : rows + heads]
    d_l = later[rows : rows + heads]
    head_dim = rows // heads
    state = d_l[:, None, :] * earlier[:rows].reshape(heads, head_dim, -1) + later[:rows].reshape(heads, head_dim, -1)
    decay = d_e * d_l
    spare = jnp.zeros((extra - 2 * heads, later.shape[1]), later.dtype)
    return jnp.concatenate([state.reshape(rows, -1), decay, decay, spare], axis=0)


def received(packed, axis, by, heads):
    place = lax.axis_index(axis)
    extra = -(-2 * heads // 16) * 16
    rows = packed.shape[0] - extra
    row = lax.broadcasted_iota(jnp.int32, packed.shape, 0)
    high = packed.astype(jnp.bfloat16)
    low = (packed - high.astype(jnp.float32)).astype(jnp.bfloat16)
    wire = jnp.where((row >= rows + heads) & (row < rows + 2 * heads), low, high)
    got = shifted(wire, axis, by).astype(jnp.float32)
    missing = (place < by).astype(jnp.float32)
    decay = got[rows : rows + heads] + got[rows + heads : rows + 2 * heads] + missing
    spare = jnp.zeros((extra - 2 * heads, packed.shape[1]), packed.dtype)
    return jnp.concatenate([got[:rows], decay, decay, spare], axis=0)


def exclusive_scan(packed, axis, side, heads):
    count = lax.axis_size(axis)
    if count == 1:
        return received(packed, axis, 1, heads), side
    held = received(packed, axis, 1, heads)
    if count > 2:
        held = combine_packed(received(packed, axis, 2, heads), held, heads)
    cover = 2
    while cover < count - 1:
        if cover * 2 >= count - 1:
            held, side = lax.optimization_barrier((held, side))
        held = combine_packed(received(held, axis, cover, heads), held, heads)
        cover *= 2
    return held, side


def exchange(block, axis, dim):
    count = lax.axis_size(axis)
    if count & (count - 1):
        return lax.all_gather(block, axis, axis=dim, tiled=True), None
    held, codes = block, [0]
    bit = count // 2
    while bit >= 1:
        other = lax.ppermute(held, axis, [(i, i ^ bit) for i in range(count)])
        held = jnp.concatenate([held, other], axis=dim)
        codes = codes + [c ^ bit for c in codes]
        bit //= 2
    return held, codes


def to_natural(held, codes, axis, dim):
    if codes is None:
        return held
    count = len(codes)
    width = held.shape[dim] // count
    where_code = [0] * count
    for position, code in enumerate(codes):
        where_code[code] = position
    table = jnp.asarray(where_code, jnp.int32)
    place = lax.axis_index(axis)
    parts = [
        lax.dynamic_slice_in_dim(held, table[jnp.bitwise_xor(index, place)] * width, width, axis=dim)
        for index in range(count)
    ]
    return jnp.concatenate(parts, axis=dim)


def summed_columns(partial, axis):
    count = lax.axis_size(axis)
    if count & (count - 1) or partial.shape[1] % 2:
        return lax.psum(partial, axis).astype(jnp.bfloat16)
    if count == 1:
        return partial.astype(jnp.bfloat16)
    place = lax.axis_index(axis)
    half = partial.shape[1] // 2
    side = place % 2
    kept = lax.dynamic_slice_in_dim(partial, side * half, half, axis=1)
    sent = lax.dynamic_slice_in_dim(partial, (1 - side) * half, half, axis=1)
    kept = kept + lax.ppermute(sent, axis, [(i, i ^ 1) for i in range(count)])
    bit = 2
    while bit < count:
        kept = kept + lax.ppermute(kept, axis, [(i, i ^ bit) for i in range(count)])
        bit *= 2
    kept = kept.astype(jnp.bfloat16)
    other = lax.ppermute(kept, axis, [(i, i ^ 1) for i in range(count)])
    triple = jnp.concatenate([other, kept, other], axis=1)
    return lax.dynamic_slice_in_dim(triple, (1 - side) * half, 2 * half, axis=1)


def segment_of(positions, lengths):
    prompt_ends = jnp.cumsum(lengths)
    counted = (positions[:, None] >= prompt_ends[None, :]).astype(jnp.int32)
    return jnp.sum(counted, axis=1)


def causal_conv(extended, segment_ids, weights, conv_width):
    out_rows = extended.shape[0] - conv_width + 1
    target = segment_ids[conv_width - 1 :]
    running = jnp.zeros((out_rows, extended.shape[1]), jnp.float32)
    for tap_index in range(conv_width):
        matched = (segment_ids[tap_index : tap_index + out_rows] == target).astype(jnp.float32)
        running = (
            running
            + weights[tap_index][None, :]
            * extended[tap_index : tap_index + out_rows]
            * matched[:, None]
        )
    return running


def local_terms(x_heads, b_rows, c_rows, step_size, decay_log, segment_ids, seg_before):
    log_decay = -jnp.exp(decay_log)[None, :] * step_size
    positions_in = jnp.arange(x_heads.shape[0], dtype=jnp.int32)
    lower = (positions_in[:, None] >= positions_in[None, :]).astype(jnp.float32)
    cum_decay = jnp.dot(lower, log_decay, precision=precise)
    same_prompt = (segment_ids[:, None] == segment_ids[None, :]) & (
        positions_in[:, None] >= positions_in[None, :]
    )
    decay_gap = cum_decay.T[:, :, None] - cum_decay.T[:, None, :]
    decay_matrix = jnp.exp(jnp.where(same_prompt[None], decay_gap, -jnp.inf))
    scores = jnp.dot(c_rows, b_rows.T, precision=precise)
    x_step = x_heads * step_size[:, :, None]
    intra = jnp.einsum("hts,shp->thp", scores[None] * decay_matrix, x_step, precision=precise)
    to_end = jnp.exp(
        jnp.where(
            (segment_ids == segment_ids[-1])[:, None], cum_decay[-1][None, :] - cum_decay, -jnp.inf
        )
    )
    state_out = jnp.einsum("shp,sn->hpn", x_step * to_end[:, :, None], b_rows, precision=precise)
    carried = segment_ids == seg_before
    carry_in = jnp.exp(jnp.where(carried[:, None], cum_decay, -jnp.inf))
    block_decay = jnp.where(carried[-1], jnp.exp(cum_decay[-1]), 0.0)
    return (intra, state_out, carry_in, block_decay)


def per_device(
    tokens,
    deal_order,
    lengths,
    x_weight,
    z_weight,
    shared_weight,
    step_weight,
    conv_heads,
    conv_shared,
    step_bias,
    decay_log,
    skip_gain,
):
    seq_count = lax.axis_size("seq")
    own_index = lax.axis_index("seq")
    tok_dev = tokens.shape[0]
    piece_rows = tok_dev // seq_count
    slot_rows = tokens.reshape(seq_count, piece_rows, tokens.shape[1])
    arrived = lax.all_to_all(slot_rows, "seq", split_axis=0, concat_axis=0, tiled=True)
    dealt_row = lax.dynamic_slice_in_dim(deal_order, own_index, 1, 0)[0]
    inverse = jnp.argsort(dealt_row)
    stream_block = jnp.take(arrived, inverse, axis=0).reshape(tok_dev, tokens.shape[1])
    inner_dev = x_weight.shape[1]
    heads_dev = step_weight.shape[1]
    head_dim = inner_dev // heads_dev
    state_dim = shared_weight.shape[1] // 2
    bc_partial = jnp.dot(stream_block, shared_weight, preferred_element_type=jnp.float32)
    bc_raw = summed_columns(bc_partial, "fsdp")
    feature_held, codes = exchange(stream_block, "fsdp", 1)
    feature_part = to_natural(feature_held, codes, "fsdp", 1)
    x_acc, z_acc, step_acc = tuple(
        (
            jnp.dot(feature_part, weight, preferred_element_type=jnp.float32)
            for weight in (x_weight, z_weight, step_weight)
        )
    )
    x_raw = x_acc.astype(jnp.bfloat16)
    z_raw = z_acc.astype(jnp.bfloat16)
    step_size = jax.nn.softplus(step_acc + step_bias[None, :])
    mixed_in = jnp.concatenate([x_raw, bc_raw], axis=1)
    conv_width = conv_heads.shape[0]
    prior_rows = shifted(mixed_in[tok_dev - conv_width + 1 :], "seq", 1)
    first_pos = own_index * tok_dev
    positions = first_pos - (conv_width - 1) + jnp.arange(tok_dev + conv_width - 1, dtype=jnp.int32)
    seg_ext = segment_of(positions, lengths)
    extended = jnp.concatenate([prior_rows, mixed_in], axis=0).astype(jnp.float32)
    activated = jax.nn.silu(
        causal_conv(
            extended, seg_ext, jnp.concatenate([conv_heads, conv_shared], axis=1), conv_width
        )
    )
    segment_ids = seg_ext[conv_width - 1 :]
    seg_before = jnp.where(own_index == 0, -1, seg_ext[conv_width - 2])
    x_heads = activated[:, :inner_dev].reshape(tok_dev, heads_dev, head_dim)
    b_rows = activated[:, inner_dev : inner_dev + state_dim]
    c_rows = activated[:, inner_dev + state_dim :]
    intra, state_out, carry_in, block_decay = local_terms(
        x_heads, b_rows, c_rows, step_size, decay_log, segment_ids, seg_before
    )
    decay_rows = jnp.broadcast_to(block_decay[:, None], (heads_dev, state_dim))
    spare = jnp.zeros((-(-2 * heads_dev // 16) * 16 - 2 * heads_dev, state_dim), jnp.float32)
    packed = jnp.concatenate(
        [state_out.reshape(heads_dev * head_dim, state_dim), decay_rows, decay_rows, spare], axis=0
    )
    local_y = intra + skip_gain[None, :, None] * x_heads
    gate = jax.nn.silu(z_raw.astype(jnp.float32)).reshape(tok_dev, heads_dev, head_dim)
    scanned, (local_y, gate, carry_in) = exclusive_scan(packed, "seq", (local_y, gate, carry_in), heads_dev)
    state_in = scanned[: heads_dev * head_dim].reshape(heads_dev, head_dim, state_dim)
    incoming = jnp.einsum("tn,hpn->thp", c_rows, state_in, precision=precise)
    y_block = local_y + carry_in[:, :, None] * incoming
    gated = (y_block * gate).reshape(tok_dev, inner_dev).astype(jnp.bfloat16)
    ordered = gated.reshape(seq_count, piece_rows, inner_dev)
    outgoing = jnp.take(ordered, dealt_row, axis=0)
    returned = lax.all_to_all(outgoing, "seq", split_axis=0, concat_axis=0, tiled=True)
    return returned.reshape(tok_dev, inner_dev)


def solution(mesh):
    return jax.shard_map(
        per_device,
        mesh=mesh,
        in_specs=(
            P("seq", "fsdp"),
            P(),
            P(),
            P(None, "fsdp"),
            P(None, "fsdp"),
            P("fsdp", None),
            P(None, "fsdp"),
            P(None, "fsdp"),
            P(),
            P("fsdp"),
            P("fsdp"),
            P("fsdp"),
        ),
        out_specs=P("seq", "fsdp"),
        check_vma=False,
    )
```

```python
import jax
import jax.numpy as jnp
from jax import lax
from jax.sharding import PartitionSpec as P

precise = lax.Precision.HIGHEST


def shifted(array, axis, by):
    count = lax.axis_size(axis)
    pairs = [(i, i + by) for i in range(count) if 0 <= i + by < count]
    return lax.ppermute(array, axis, pairs)


def combine_packed(earlier, later, heads):
    extra = -(-2 * heads // 16) * 16
    rows = later.shape[0] - extra
    d_e = earlier[rows : rows + heads]
    d_l = later[rows : rows + heads]
    head_dim = rows // heads
    state = d_l[:, None, :] * earlier[:rows].reshape(heads, head_dim, -1) + later[:rows].reshape(heads, head_dim, -1)
    decay = d_e * d_l
    spare = jnp.zeros((extra - 2 * heads, later.shape[1]), later.dtype)
    return jnp.concatenate([state.reshape(rows, -1), decay, decay, spare], axis=0)


def received(packed, axis, by, heads):
    place = lax.axis_index(axis)
    extra = -(-2 * heads // 16) * 16
    rows = packed.shape[0] - extra
    row = lax.broadcasted_iota(jnp.int32, packed.shape, 0)
    high = packed.astype(jnp.bfloat16)
    low = (packed - high.astype(jnp.float32)).astype(jnp.bfloat16)
    wire = jnp.where((row >= rows + heads) & (row < rows + 2 * heads), low, high)
    got = shifted(wire, axis, by).astype(jnp.float32)
    missing = (place < by).astype(jnp.float32)
    decay = got[rows : rows + heads] + got[rows + heads : rows + 2 * heads] + missing
    spare = jnp.zeros((extra - 2 * heads, packed.shape[1]), packed.dtype)
    return jnp.concatenate([got[:rows], decay, decay, spare], axis=0)


def exclusive_scan(packed, axis, side, heads):
    count = lax.axis_size(axis)
    if count == 1:
        return received(packed, axis, 1, heads), side
    held = received(packed, axis, 1, heads)
    if count > 2:
        held = combine_packed(received(packed, axis, 2, heads), held, heads)
    cover = 2
    while cover < count - 1:
        if cover * 2 >= count - 1:
            held, side = lax.optimization_barrier((held, side))
        held = combine_packed(received(held, axis, cover, heads), held, heads)
        cover *= 2
    return held, side


def exchange(block, axis, dim):
    count = lax.axis_size(axis)
    if count & (count - 1):
        return lax.all_gather(block, axis, axis=dim, tiled=True), None
    held, codes = block, [0]
    bit = count // 2
    while bit >= 1:
        other = lax.ppermute(held, axis, [(i, i ^ bit) for i in range(count)])
        held = jnp.concatenate([held, other], axis=dim)
        codes = codes + [c ^ bit for c in codes]
        bit //= 2
    return held, codes


def to_natural(held, codes, axis, dim):
    if codes is None:
        return held
    count = len(codes)
    width = held.shape[dim] // count
    where_code = [0] * count
    for position, code in enumerate(codes):
        where_code[code] = position
    table = jnp.asarray(where_code, jnp.int32)
    place = lax.axis_index(axis)
    parts = [
        lax.dynamic_slice_in_dim(held, table[jnp.bitwise_xor(index, place)] * width, width, axis=dim)
        for index in range(count)
    ]
    return jnp.concatenate(parts, axis=dim)


def summed_columns(partial, axis):
    count = lax.axis_size(axis)
    if count & (count - 1) or partial.shape[1] % 2:
        return lax.psum(partial, axis).astype(jnp.bfloat16)
    if count == 1:
        return partial.astype(jnp.bfloat16)
    place = lax.axis_index(axis)
    half = partial.shape[1] // 2
    side = place % 2
    kept = lax.dynamic_slice_in_dim(partial, side * half, half, axis=1)
    sent = lax.dynamic_slice_in_dim(partial, (1 - side) * half, half, axis=1)
    kept = kept + lax.ppermute(sent, axis, [(i, i ^ 1) for i in range(count)])
    bit = 2
    while bit < count:
        kept = kept + lax.ppermute(kept, axis, [(i, i ^ bit) for i in range(count)])
        bit *= 2
    kept = kept.astype(jnp.bfloat16)
    other = lax.ppermute(kept, axis, [(i, i ^ 1) for i in range(count)])
    both = jnp.concatenate([kept, other], axis=1)
    return jnp.where(side == 0, both, jnp.concatenate([other, kept], axis=1))


def segment_of(positions, lengths):
    prompt_ends = jnp.cumsum(lengths)
    counted = (positions[:, None] >= prompt_ends[None, :]).astype(jnp.int32)
    return jnp.sum(counted, axis=1)


def causal_conv(extended, segment_ids, weights, conv_width):
    out_rows = extended.shape[0] - conv_width + 1
    target = segment_ids[conv_width - 1 :]
    running = jnp.zeros((out_rows, extended.shape[1]), jnp.float32)
    for tap_index in range(conv_width):
        matched = (segment_ids[tap_index : tap_index + out_rows] == target).astype(jnp.float32)
        running = (
            running
            + weights[tap_index][None, :]
            * extended[tap_index : tap_index + out_rows]
            * matched[:, None]
        )
    return running


def local_terms(x_heads, b_rows, c_rows, step_size, decay_log, segment_ids, seg_before):
    log_decay = -jnp.exp(decay_log)[None, :] * step_size
    positions_in = jnp.arange(x_heads.shape[0], dtype=jnp.int32)
    lower = (positions_in[:, None] >= positions_in[None, :]).astype(jnp.float32)
    cum_decay = jnp.dot(lower, log_decay, precision=precise)
    same_prompt = (segment_ids[:, None] == segment_ids[None, :]) & (
        positions_in[:, None] >= positions_in[None, :]
    )
    decay_gap = cum_decay.T[:, :, None] - cum_decay.T[:, None, :]
    decay_matrix = jnp.exp(jnp.where(same_prompt[None], decay_gap, -jnp.inf))
    scores = jnp.dot(c_rows, b_rows.T, precision=precise)
    x_step = x_heads * step_size[:, :, None]
    intra = jnp.einsum("hts,shp->thp", scores[None] * decay_matrix, x_step, precision=precise)
    to_end = jnp.exp(
        jnp.where(
            (segment_ids == segment_ids[-1])[:, None], cum_decay[-1][None, :] - cum_decay, -jnp.inf
        )
    )
    state_out = jnp.einsum("shp,sn->hpn", x_step * to_end[:, :, None], b_rows, precision=precise)
    carried = segment_ids == seg_before
    carry_in = jnp.exp(jnp.where(carried[:, None], cum_decay, -jnp.inf))
    block_decay = jnp.where(carried[-1], jnp.exp(cum_decay[-1]), 0.0)
    return (intra, state_out, carry_in, block_decay)


def per_device(
    tokens,
    deal_order,
    lengths,
    x_weight,
    z_weight,
    shared_weight,
    step_weight,
    conv_heads,
    conv_shared,
    step_bias,
    decay_log,
    skip_gain,
):
    seq_count = lax.axis_size("seq")
    own_index = lax.axis_index("seq")
    tok_dev = tokens.shape[0]
    piece_rows = tok_dev // seq_count
    slot_rows = tokens.reshape(seq_count, piece_rows, tokens.shape[1])
    arrived = lax.all_to_all(slot_rows, "seq", split_axis=0, concat_axis=0, tiled=True)
    dealt_row = lax.dynamic_slice_in_dim(deal_order, own_index, 1, 0)[0]
    inverse = jnp.argsort(dealt_row)
    chooser = (dealt_row[None, :] == jnp.arange(seq_count, dtype=dealt_row.dtype)[:, None]).astype(arrived.dtype)
    stream_block = jnp.einsum(
        "pm,mri->pri", chooser, arrived, preferred_element_type=jnp.float32
    ).astype(arrived.dtype).reshape(tok_dev, tokens.shape[1])
    inner_dev = x_weight.shape[1]
    heads_dev = step_weight.shape[1]
    head_dim = inner_dev // heads_dev
    state_dim = shared_weight.shape[1] // 2
    bc_partial = jnp.dot(stream_block, shared_weight, preferred_element_type=jnp.float32)
    bc_raw = summed_columns(bc_partial, "fsdp")
    feature_held, codes = exchange(stream_block, "fsdp", 1)
    feature_part = to_natural(feature_held, codes, "fsdp", 1)
    x_acc, z_acc, step_acc = tuple(
        (
            jnp.dot(feature_part, weight, preferred_element_type=jnp.float32)
            for weight in (x_weight, z_weight, step_weight)
        )
    )
    x_raw = x_acc.astype(jnp.bfloat16)
    z_raw = z_acc.astype(jnp.bfloat16)
    step_size = jax.nn.softplus(step_acc + step_bias[None, :])
    mixed_in = jnp.concatenate([x_raw, bc_raw], axis=1)
    conv_width = conv_heads.shape[0]
    prior_rows = shifted(mixed_in[tok_dev - conv_width + 1 :], "seq", 1)
    first_pos = own_index * tok_dev
    positions = first_pos - (conv_width - 1) + jnp.arange(tok_dev + conv_width - 1, dtype=jnp.int32)
    seg_ext = segment_of(positions, lengths)
    extended = jnp.concatenate([prior_rows, mixed_in], axis=0).astype(jnp.float32)
    activated = jax.nn.silu(
        causal_conv(
            extended, seg_ext, jnp.concatenate([conv_heads, conv_shared], axis=1), conv_width
        )
    )
    segment_ids = seg_ext[conv_width - 1 :]
    seg_before = jnp.where(own_index == 0, -1, seg_ext[conv_width - 2])
    x_heads = activated[:, :inner_dev].reshape(tok_dev, heads_dev, head_dim)
    b_rows = activated[:, inner_dev : inner_dev + state_dim]
    c_rows = activated[:, inner_dev + state_dim :]
    intra, state_out, carry_in, block_decay = local_terms(
        x_heads, b_rows, c_rows, step_size, decay_log, segment_ids, seg_before
    )
    decay_rows = jnp.broadcast_to(block_decay[:, None], (heads_dev, state_dim))
    spare = jnp.zeros((-(-2 * heads_dev // 16) * 16 - 2 * heads_dev, state_dim), jnp.float32)
    packed = jnp.concatenate(
        [state_out.reshape(heads_dev * head_dim, state_dim), decay_rows, decay_rows, spare], axis=0
    )
    local_y = intra + skip_gain[None, :, None] * x_heads
    gate = jax.nn.silu(z_raw.astype(jnp.float32)).reshape(tok_dev, heads_dev, head_dim)
    scanned, (local_y, gate, carry_in) = exclusive_scan(packed, "seq", (local_y, gate, carry_in), heads_dev)
    state_in = scanned[: heads_dev * head_dim].reshape(heads_dev, head_dim, state_dim)
    incoming = jnp.einsum("tn,hpn->thp", c_rows, state_in, precision=precise)
    y_block = local_y + carry_in[:, :, None] * incoming
    gated = (y_block * gate).reshape(tok_dev, inner_dev).astype(jnp.bfloat16)
    ordered = gated.reshape(seq_count, piece_rows, inner_dev)
    outgoing = jnp.take(ordered, dealt_row, axis=0)
    returned = lax.all_to_all(outgoing, "seq", split_axis=0, concat_axis=0, tiled=True)
    return returned.reshape(tok_dev, inner_dev)


def solution(mesh):
    return jax.shard_map(
        per_device,
        mesh=mesh,
        in_specs=(
            P("seq", "fsdp"),
            P(),
            P(),
            P(None, "fsdp"),
            P(None, "fsdp"),
            P("fsdp", None),
            P(None, "fsdp"),
            P(None, "fsdp"),
            P(),
            P("fsdp"),
            P("fsdp"),
            P("fsdp"),
        ),
        out_specs=P("seq", "fsdp"),
        check_vma=False,
    )
```

```python
import jax
import jax.numpy as jnp
from jax import lax
from jax.sharding import PartitionSpec as P

precise = lax.Precision.HIGHEST


def shifted(array, axis, by):
    count = lax.axis_size(axis)
    pairs = [(i, i + by) for i in range(count) if 0 <= i + by < count]
    return lax.ppermute(array, axis, pairs)


def combine_packed(earlier, later, heads):
    extra = -(-2 * heads // 16) * 16
    rows = later.shape[0] - extra
    d_e = earlier[rows : rows + heads]
    d_l = later[rows : rows + heads]
    head_dim = rows // heads
    state = d_l[:, None, :] * earlier[:rows].reshape(heads, head_dim, -1) + later[:rows].reshape(heads, head_dim, -1)
    decay = d_e * d_l
    spare = jnp.zeros((extra - 2 * heads, later.shape[1]), later.dtype)
    return jnp.concatenate([state.reshape(rows, -1), decay, decay, spare], axis=0)


def received(packed, axis, by, heads):
    place = lax.axis_index(axis)
    extra = -(-2 * heads // 16) * 16
    rows = packed.shape[0] - extra
    row = lax.broadcasted_iota(jnp.int32, packed.shape, 0)
    high = packed.astype(jnp.bfloat16)
    low = (packed - high.astype(jnp.float32)).astype(jnp.bfloat16)
    wire = jnp.where((row >= rows + heads) & (row < rows + 2 * heads), low, high)
    got = shifted(wire, axis, by).astype(jnp.float32)
    missing = (place < by).astype(jnp.float32)
    decay = got[rows : rows + heads] + got[rows + heads : rows + 2 * heads] + missing
    spare = jnp.zeros((extra - 2 * heads, packed.shape[1]), packed.dtype)
    return jnp.concatenate([got[:rows], decay, decay, spare], axis=0)


def exclusive_scan(packed, axis, side, heads):
    count = lax.axis_size(axis)
    if count == 1:
        return received(packed, axis, 1, heads), side
    held = received(packed, axis, 1, heads)
    if count > 2:
        held = combine_packed(received(packed, axis, 2, heads), held, heads)
    cover = 2
    while cover < count - 1:
        if cover * 2 >= count - 1:
            held, side = lax.optimization_barrier((held, side))
        held = combine_packed(received(held, axis, cover, heads), held, heads)
        cover *= 2
    return held, side


def exchange(block, axis, dim):
    count = lax.axis_size(axis)
    if count & (count - 1):
        return lax.all_gather(block, axis, axis=dim, tiled=True), None
    held, codes = block, [0]
    bit = count // 2
    while bit >= 1:
        other = lax.ppermute(held, axis, [(i, i ^ bit) for i in range(count)])
        held = jnp.concatenate([held, other], axis=dim)
        codes = codes + [c ^ bit for c in codes]
        bit //= 2
    return held, codes


def to_natural(held, codes, axis, dim):
    if codes is None:
        return held
    count = len(codes)
    width = held.shape[dim] // count
    where_code = [0] * count
    for position, code in enumerate(codes):
        where_code[code] = position
    table = jnp.asarray(where_code, jnp.int32)
    place = lax.axis_index(axis)
    parts = [
        lax.dynamic_slice_in_dim(held, table[jnp.bitwise_xor(index, place)] * width, width, axis=dim)
        for index in range(count)
    ]
    return jnp.concatenate(parts, axis=dim)


def summed_columns(partial, axis):
    count = lax.axis_size(axis)
    if count & (count - 1) or partial.shape[1] % 2:
        return lax.psum(partial, axis).astype(jnp.bfloat16)
    if count == 1:
        return partial.astype(jnp.bfloat16)
    place = lax.axis_index(axis)
    half = partial.shape[1] // 2
    side = place % 2
    kept = lax.dynamic_slice_in_dim(partial, side * half, half, axis=1)
    sent = lax.dynamic_slice_in_dim(partial, (1 - side) * half, half, axis=1)
    kept = kept + lax.ppermute(sent, axis, [(i, i ^ 1) for i in range(count)])
    bit = 2
    while bit < count:
        kept = kept + lax.ppermute(kept, axis, [(i, i ^ bit) for i in range(count)])
        bit *= 2
    kept = kept.astype(jnp.bfloat16)
    other = lax.ppermute(kept, axis, [(i, i ^ 1) for i in range(count)])
    both = jnp.concatenate([kept, other], axis=1)
    return jnp.where(side == 0, both, jnp.concatenate([other, kept], axis=1))


def segment_of(positions, lengths):
    prompt_ends = jnp.cumsum(lengths)
    counted = (positions[:, None] >= prompt_ends[None, :]).astype(jnp.int32)
    return jnp.sum(counted, axis=1)


def causal_conv(extended, segment_ids, weights, conv_width):
    out_rows = extended.shape[0] - conv_width + 1
    target = segment_ids[conv_width - 1 :]
    running = jnp.zeros((out_rows, extended.shape[1]), jnp.float32)
    for tap_index in range(conv_width):
        matched = (segment_ids[tap_index : tap_index + out_rows] == target).astype(jnp.float32)
        running = (
            running
            + weights[tap_index][None, :]
            * extended[tap_index : tap_index + out_rows]
            * matched[:, None]
        )
    return running


def local_terms(x_heads, b_rows, c_rows, step_size, decay_log, segment_ids, seg_before):
    log_decay = -jnp.exp(decay_log)[None, :] * step_size
    positions_in = jnp.arange(x_heads.shape[0], dtype=jnp.int32)
    lower = (positions_in[:, None] >= positions_in[None, :]).astype(jnp.float32)
    cum_decay = jnp.dot(lower, log_decay, precision=precise)
    same_prompt = (segment_ids[:, None] == segment_ids[None, :]) & (
        positions_in[:, None] >= positions_in[None, :]
    )
    decay_gap = cum_decay.T[:, :, None] - cum_decay.T[:, None, :]
    decay_matrix = jnp.exp(jnp.where(same_prompt[None], decay_gap, -jnp.inf))
    scores = jnp.dot(c_rows, b_rows.T, precision=precise)
    x_step = x_heads * step_size[:, :, None]
    intra = jnp.einsum("hts,shp->thp", scores[None] * decay_matrix, x_step, precision=precise)
    to_end = jnp.exp(
        jnp.where(
            (segment_ids == segment_ids[-1])[:, None], cum_decay[-1][None, :] - cum_decay, -jnp.inf
        )
    )
    state_out = jnp.einsum("shp,sn->hpn", x_step * to_end[:, :, None], b_rows, precision=precise)
    carried = segment_ids == seg_before
    carry_in = jnp.exp(jnp.where(carried[:, None], cum_decay, -jnp.inf))
    block_decay = jnp.where(carried[-1], jnp.exp(cum_decay[-1]), 0.0)
    return (intra, state_out, carry_in, block_decay)


def per_device(
    tokens,
    deal_order,
    lengths,
    x_weight,
    z_weight,
    shared_weight,
    step_weight,
    conv_heads,
    conv_shared,
    step_bias,
    decay_log,
    skip_gain,
):
    seq_count = lax.axis_size("seq")
    own_index = lax.axis_index("seq")
    tok_dev = tokens.shape[0]
    piece_rows = tok_dev // seq_count
    slot_rows = tokens.reshape(seq_count, piece_rows, tokens.shape[1])
    arrived = lax.all_to_all(slot_rows, "seq", split_axis=0, concat_axis=0, tiled=True)
    dealt_row = lax.dynamic_slice_in_dim(deal_order, own_index, 1, 0)[0]
    inverse = jnp.argsort(dealt_row)
    chooser = (dealt_row[None, :] == jnp.arange(seq_count, dtype=dealt_row.dtype)[:, None]).astype(arrived.dtype)
    stream_block = jnp.einsum(
        "pm,mri->pri", chooser, arrived, preferred_element_type=jnp.float32
    ).astype(arrived.dtype).reshape(tok_dev, tokens.shape[1])
    inner_dev = x_weight.shape[1]
    heads_dev = step_weight.shape[1]
    head_dim = inner_dev // heads_dev
    state_dim = shared_weight.shape[1] // 2
    bc_partial = jnp.dot(stream_block, shared_weight, preferred_element_type=jnp.float32)
    bc_raw = summed_columns(bc_partial, "fsdp")
    feature_held, codes = exchange(stream_block, "fsdp", 1)
    feature_part = to_natural(feature_held, codes, "fsdp", 1)
    x_acc, z_acc, step_acc = tuple(
        (
            jnp.dot(feature_part, weight, preferred_element_type=jnp.float32)
            for weight in (x_weight, z_weight, step_weight)
        )
    )
    x_raw = x_acc.astype(jnp.bfloat16)
    z_raw = z_acc.astype(jnp.bfloat16)
    step_size = jax.nn.softplus(step_acc + step_bias[None, :])
    mixed_in = jnp.concatenate([x_raw, bc_raw], axis=1)
    conv_width = conv_heads.shape[0]
    prior_rows = shifted(mixed_in[tok_dev - conv_width + 1 :], "seq", 1)
    first_pos = own_index * tok_dev
    positions = first_pos - (conv_width - 1) + jnp.arange(tok_dev + conv_width - 1, dtype=jnp.int32)
    seg_ext = segment_of(positions, lengths)
    extended = jnp.concatenate([prior_rows, mixed_in], axis=0).astype(jnp.float32)
    activated = jax.nn.silu(
        causal_conv(
            extended, seg_ext, jnp.concatenate([conv_heads, conv_shared], axis=1), conv_width
        )
    )
    segment_ids = seg_ext[conv_width - 1 :]
    seg_before = jnp.where(own_index == 0, -1, seg_ext[conv_width - 2])
    x_heads = activated[:, :inner_dev].reshape(tok_dev, heads_dev, head_dim)
    b_rows = activated[:, inner_dev : inner_dev + state_dim]
    c_rows = activated[:, inner_dev + state_dim :]
    intra, state_out, carry_in, block_decay = local_terms(
        x_heads, b_rows, c_rows, step_size, decay_log, segment_ids, seg_before
    )
    decay_rows = jnp.broadcast_to(block_decay[:, None], (heads_dev, state_dim))
    spare = jnp.zeros((-(-2 * heads_dev // 16) * 16 - 2 * heads_dev, state_dim), jnp.float32)
    packed = jnp.concatenate(
        [state_out.reshape(heads_dev * head_dim, state_dim), decay_rows, decay_rows, spare], axis=0
    )
    local_y = intra + skip_gain[None, :, None] * x_heads
    gate = jax.nn.silu(z_raw.astype(jnp.float32)).reshape(tok_dev, heads_dev, head_dim)
    scanned, (local_y, gate, carry_in) = exclusive_scan(packed, "seq", (local_y, gate, carry_in), heads_dev)
    state_in = scanned[: heads_dev * head_dim].reshape(heads_dev, head_dim, state_dim)
    incoming = jnp.einsum("tn,hpn->thp", c_rows, state_in, precision=precise)
    y_block = local_y + carry_in[:, :, None] * incoming
    gated = (y_block * gate).reshape(tok_dev, inner_dev).astype(jnp.bfloat16)
    ordered = gated.reshape(seq_count, piece_rows, inner_dev)
    picker = (dealt_row[:, None] == jnp.arange(seq_count, dtype=dealt_row.dtype)[None, :]).astype(jnp.bfloat16)
    outgoing = jnp.einsum("mp,pri->mri", picker, ordered, preferred_element_type=jnp.float32).astype(
        jnp.bfloat16
    )
    returned = lax.all_to_all(outgoing, "seq", split_axis=0, concat_axis=0, tiled=True)
    return returned.reshape(tok_dev, inner_dev)


def solution(mesh):
    return jax.shard_map(
        per_device,
        mesh=mesh,
        in_specs=(
            P("seq", "fsdp"),
            P(),
            P(),
            P(None, "fsdp"),
            P(None, "fsdp"),
            P("fsdp", None),
            P(None, "fsdp"),
            P(None, "fsdp"),
            P(),
            P("fsdp"),
            P("fsdp"),
            P("fsdp"),
        ),
        out_specs=P("seq", "fsdp"),
        check_vma=False,
    )
```
